32 devices in a mesh: freq: 16 (over z, y, core), rows: 2 (over x).
Axes of the slice: x: 2, y: 2, z: 4, core: 2. Of those that a mesh axis runs over, the one named last changes fastest.
Arguments:
- image_cube: float32 [2048, 64, 128], P('freq', 'rows'), may hold values from 0.05 to 2
- data_grad: float32 [2048, 64, 128], P('freq', 'rows'), may hold values from -4 to 4
- space_duals: float32 [4, 2048, 64, 128], P(None, 'freq', 'rows'), may hold values from -0.5 to 0.5
- freq_duals: float32 [8192, 2048], P(('rows', 'freq')), may hold values from -1 to 1
Outputs:
- image_next: float32 [2048, 64, 128], P('freq', 'rows')
- space_next: float32 [4, 2048, 64, 128], P(None, 'freq', 'rows')
- freq_next: float32 [8192, 2048], P(('rows', 'freq'))
The draws below stay inside these ranges and needn't reach their ends.
All inputs are finite; a program needn't handle non-finite values.
Results may differ from the reference program's by a relative error of at most 0.00008.
Values sent between devices are 32-bit elements; how exact they have to be, the bound alone decides.
No kernel may reach another device: no remote copies, remote signals or barrier semaphores. Data moves between devices by JAX's collectives and lax.ppermute only.
A program may use at most 128 MiB of HBM per device.

```python
import math
import jax
import jax.numpy as jnp
from jax import lax

F = 2048
W = 128
SCALES = 4
H = 64
PIX = 8192


def level_of(rng, extent, split, low, largest):
    loudness, own = 1.0, jax.random.fold_in(rng, 6)
    for position, parts in split:
        heights = jnp.exp(jax.random.uniform(jax.random.fold_in(own, position), (parts,), jnp.float32, low / len(split), largest / len(split)))
        loudness = loudness * jnp.repeat(heights, extent[position] // parts).reshape([-1 if axis == position else 1 for axis in range(len(extent))])
    return loudness


def gaussian(stream_key, extent, deviation, reach, shards=(), kind=jnp.bfloat16):
    level = level_of(stream_key, extent, shards, -0.22, 0.18) if shards else 1.0
    values = jax.random.normal(stream_key, extent, jnp.float32) * deviation * level
    return jnp.minimum(jnp.maximum(values, -reach), reach).astype(kind)


def setup_inputs(seed: int = 0) -> dict:
    key_list = jax.random.split(jax.random.key(seed), 5)
    return {
        "image_cube": jnp.clip(jnp.exp(math.log(2.0) - 3.6888794 * jax.random.uniform(key_list[0], (F, H, W), jnp.float32) ** level_of(key_list[0], (F, H, W), ((0, 16), (1, 2)), -0.2, 0.2)), 0.05, 2.0),
        "data_grad": gaussian(key_list[1], (F, H, W), 0.5, 4.0, ((0, 16), (1, 2)), jnp.float32),
        "space_duals": jnp.clip(jax.random.uniform(key_list[2], (SCALES, F, H, W), jnp.float32, -0.5, 0.5) * level_of(key_list[2], (SCALES, F, H, W), ((1, 16), (2, 2)), -0.4, 0.0), -0.5, 0.5),
        "freq_duals": jnp.clip(jax.random.uniform(key_list[3], (PIX, F), jnp.float32, -1.0, 1.0) * level_of(key_list[3], (PIX, F), ((0, 32),), -0.4, 0.0), -1.0, 1.0),
    }


TAPS = (0.0625, 0.25, 0.375, 0.25, 0.0625)
SIGMA = 0.5
TAU_STEP = 0.5
SPACE_BOUND = 0.5
FREQ_BOUND = 1.0

def smooth(planar, dilation):
    row_count = planar.shape[1]
    columns = planar.shape[2]
    reach_rows = 2 * dilation
    padded = jnp.pad(planar, ((0, 0), (reach_rows, reach_rows), (0, 0)))
    running = TAPS[0] * padded[:, 0:row_count, :]
    for tap_idx in range(1, 5):
        offset = tap_idx * dilation
        running = running + TAPS[tap_idx] * padded[:, offset:offset + row_count, :]
    padded = jnp.pad(running, ((0, 0), (0, 0), (reach_rows, reach_rows)))
    result = TAPS[0] * padded[:, :, 0:columns]
    for tap_idx in range(1, 5):
        offset = tap_idx * dilation
        result = result + TAPS[tap_idx] * padded[:, :, offset:offset + columns]
    return result

def spatial_block(pair):
    cube_part, dual_part = pair
    current = cube_part
    fresh_planes = []
    for level_idx in range(SCALES):
        smoothed = smooth(current, 2 ** level_idx)
        fresh_planes.append(jnp.clip(dual_part[level_idx] + SIGMA * (current - smoothed), -SPACE_BOUND, SPACE_BOUND))
        current = smoothed
    running = jnp.zeros_like(cube_part)
    for level_idx in reversed(range(SCALES)):
        running = smooth(running - fresh_planes[level_idx], 2 ** level_idx) + fresh_planes[level_idx]
    return (running, jnp.stack(fresh_planes))

def spectral_block(pair):
    rows_in, duals_in = pair
    length = rows_in.shape[-1]
    coef_idx = jnp.arange(length, dtype=jnp.float32)
    weights = jnp.where(coef_idx == 0, math.sqrt(1.0 / length), math.sqrt(2.0 / length))
    spectrum = jnp.fft.fft(rows_in, n=2 * length, axis=-1)[:, :length]
    coeffs = weights * jnp.real(spectrum * jnp.exp(-1j * math.pi * coef_idx / (2 * length)))
    fresh = jnp.clip(duals_in + SIGMA * coeffs, -FREQ_BOUND, FREQ_BOUND)
    lifted = fresh * weights * jnp.exp(1j * math.pi * coef_idx / (2 * length))
    back = jnp.real(jnp.fft.ifft(lifted, n=2 * length, axis=-1)[:, :length]) * (2 * length)
    return (back.astype(jnp.float32), fresh.astype(jnp.float32))

def reference(image_cube, data_grad, space_duals, freq_duals):
    chans, height, columns = image_cube.shape
    block_size = math.gcd(chans, 64)
    block_count = chans // block_size
    cube_blocks = image_cube.reshape(block_count, block_size, height, columns)
    dual_blocks = jnp.moveaxis(space_duals.reshape(SCALES, block_count, block_size, height, columns), 1, 0)
    space_terms, space_blocks = lax.map(spatial_block, (cube_blocks, dual_blocks))
    space_term = space_terms.reshape(chans, height, columns)
    space_next = jnp.moveaxis(space_blocks, 0, 1).reshape(SCALES, chans, height, columns)
    pixel_count = height * columns
    pixel_block = math.gcd(pixel_count, 512)
    pixel_groups = pixel_count // pixel_block
    pixel_rows = image_cube.reshape(chans, pixel_count).T
    back, fresh = lax.map(spectral_block, (pixel_rows.reshape(pixel_groups, pixel_block, chans), freq_duals.reshape(pixel_groups, pixel_block, chans)))
    freq_next = fresh.reshape(pixel_count, chans)
    spectral_term = back.reshape(pixel_count, chans).T.reshape(chans, height, columns)
    image_next = jnp.maximum(image_cube - TAU_STEP * (data_grad + space_term + spectral_term), 0.0)
    return (image_next, space_next, freq_next)
```

```python
import math

import jax
import jax.numpy as jnp
from jax import lax
from jax.sharding import PartitionSpec as P

SCALES = 4


TAPS = (0.0625, 0.25, 0.375, 0.25, 0.0625)
SIGMA = 0.5
TAU_STEP = 0.5
SPACE_BOUND = 0.5
FREQ_BOUND = 1.0


def padded_2(cells, sides, width):
    for axis, dim in sides:
        count = lax.axis_size(axis)
        ends = count - 1
        head = lax.slice_in_dim(cells, 0, width, axis=dim)
        tail = lax.slice_in_dim(cells, cells.shape[dim] - width, cells.shape[dim], axis=dim)
        cells = jnp.concatenate(
            [
                lax.ppermute(tail, axis, [(i, (i + 1) % count) for i in range(ends)]),
                cells,
                lax.ppermute(head, axis, [((i + 1) % count, i) for i in range(ends)]),
            ],
            axis=dim,
        )
    return cells


def blur_rows(padded, dilation, out_rows):
    running = TAPS[0] * padded[:, 0:out_rows, :]
    for tap_idx in range(1, 5):
        offset = tap_idx * dilation
        running = running + TAPS[tap_idx] * padded[:, offset : offset + out_rows, :]
    return running


def blur_cols(planar, dilation):
    columns = planar.shape[2]
    reach_cols = 2 * dilation
    padded = jnp.pad(planar, ((0, 0), (0, 0), (reach_cols, reach_cols)))
    running = TAPS[0] * padded[:, :, 0:columns]
    for tap_idx in range(1, 5):
        offset = tap_idx * dilation
        running = running + TAPS[tap_idx] * padded[:, :, offset : offset + columns]
    return running


def inside_rows(margin, local_rows):
    first_row = lax.axis_index("rows") * local_rows - margin
    positions = first_row + jnp.arange(local_rows + 2 * margin, dtype=jnp.int32)
    limit = local_rows * lax.axis_size("rows")
    return ((positions >= 0) & (positions < limit)).astype(jnp.float32)[None, :, None]


def analyse(image_cube):
    local_rows = image_cube.shape[1]
    details = []
    depth = 2 ** (SCALES + 1) - 2
    current = padded_2(image_cube, (("rows", 1),), depth)
    inside = inside_rows(depth, local_rows)
    margin = depth
    for level_idx in range(SCALES):
        dilation = 2**level_idx
        reach_rows = 2 * dilation
        new_margin = margin - reach_rows
        out_rows = local_rows + 2 * new_margin
        start_row = depth - new_margin
        smoothed = blur_cols(blur_rows(current, dilation, out_rows), dilation)
        smoothed = smoothed * inside[:, start_row : start_row + out_rows, :]
        kept = current[:, reach_rows : reach_rows + out_rows, :] - smoothed
        details.append(kept[:, new_margin : new_margin + local_rows, :])
        current = smoothed
        margin = new_margin
    return details


def synthesise(space_next):
    local_rows = space_next.shape[2]
    running = jnp.zeros_like(space_next[0])
    for level_idx in reversed(range(SCALES)):
        dilation = 2**level_idx
        operand = running - space_next[level_idx]
        padded = padded_2(operand, (("rows", 1),), 2 * dilation)
        running = (
            blur_cols(blur_rows(padded, dilation, local_rows), dilation) + space_next[level_idx]
        )
    return running


def dct_table(length):
    split = 64 if length % 64 == 0 else 1
    groups = length // split
    period = 4 * length
    coef_idx = jnp.arange(length, dtype=jnp.int32)
    scale = math.pi / (2 * length)
    outer_phase = (coef_idx[:, None] * (2 * split * jnp.arange(groups, dtype=jnp.int32))[None, :]) % period
    inner_phase = (coef_idx[:, None] * (2 * jnp.arange(split, dtype=jnp.int32) + 1)[None, :]) % period
    outer_angle = outer_phase.astype(jnp.float32) * scale
    inner_angle = inner_phase.astype(jnp.float32) * scale
    weights = jnp.where(
        coef_idx == 0, math.sqrt(1.0 / length), math.sqrt(2.0 / length)
    ).astype(jnp.float32)[:, None, None]
    table = (
        jnp.cos(outer_angle)[:, :, None] * jnp.cos(inner_angle)[:, None, :]
        - jnp.sin(outer_angle)[:, :, None] * jnp.sin(inner_angle)[:, None, :]
    ) * weights
    return table.reshape(length, length)


def spectral(pixel_cube, freq_duals):
    chans_all, pixel_count = pixel_cube.shape
    precision = lax.Precision.HIGH
    table = dct_table(chans_all)
    coeffs = lax.dot_general(
        pixel_cube,
        table,
        (((0,), (1,)), ((), ())),
        precision=precision,
        preferred_element_type=jnp.float32,
    )
    freq_next = jnp.clip(freq_duals + SIGMA * coeffs, -FREQ_BOUND, FREQ_BOUND)
    running = lax.dot_general(
        table,
        freq_next,
        (((0,), (1,)), ((), ())),
        precision=precision,
        preferred_element_type=jnp.float32,
    )
    return (running, freq_next)


def local(image_cube, data_grad, space_duals, freq_duals):
    chans, local_rows, columns = image_cube.shape
    peers = lax.axis_size("freq")
    share = local_rows * columns // peers
    pieces = image_cube.reshape(chans, peers, share)
    pixel_cube = lax.all_to_all(pieces, "freq", split_axis=1, concat_axis=0, tiled=True).reshape(
        chans * peers, share
    )
    details = analyse(image_cube)
    space_next = jnp.stack(
        [
            jnp.clip(space_duals[level_idx] + SIGMA * details[level_idx], -SPACE_BOUND, SPACE_BOUND)
            for level_idx in range(SCALES)
        ]
    )
    space_term = synthesise(space_next)
    spectral_sum, freq_next = spectral(pixel_cube, freq_duals)
    returned = lax.all_to_all(
        spectral_sum.reshape(chans * peers, 1, share),
        "freq",
        split_axis=0,
        concat_axis=1,
        tiled=True,
    )
    spectral_term = returned.reshape(chans, local_rows, columns)
    image_next = jnp.maximum(image_cube - TAU_STEP * (data_grad + space_term + spectral_term), 0.0)
    return (image_next, space_next, freq_next)


def solution(mesh):
    in_specs = (
        P("freq", "rows", None),
        P("freq", "rows", None),
        P(None, "freq", "rows", None),
        P(("rows", "freq"), None),
    )
    out_specs = (P("freq", "rows", None), P(None, "freq", "rows", None), P(("rows", "freq"), None))
    return jax.shard_map(local, mesh=mesh, in_specs=in_specs, out_specs=out_specs, check_vma=False)
```

```python
import math

import jax
import jax.numpy as jnp
from jax import lax
from jax.sharding import PartitionSpec as P
from jax.experimental import pallas as pl
from jax.experimental.pallas import tpu as pltpu

SCALES = 4


TAPS = (0.0625, 0.25, 0.375, 0.25, 0.0625)
SIGMA = 0.5
TAU_STEP = 0.5
SPACE_BOUND = 0.5
FREQ_BOUND = 1.0


def padded_2(cells, sides, width):
    for axis, dim in sides:
        count = lax.axis_size(axis)
        ends = count - 1
        head = lax.slice_in_dim(cells, 0, width, axis=dim)
        tail = lax.slice_in_dim(cells, cells.shape[dim] - width, cells.shape[dim], axis=dim)
        cells = jnp.concatenate(
            [
                lax.ppermute(tail, axis, [(i, (i + 1) % count) for i in range(ends)]),
                cells,
                lax.ppermute(head, axis, [((i + 1) % count, i) for i in range(ends)]),
            ],
            axis=dim,
        )
    return cells


def blur_rows(padded, dilation, out_rows):
    running = TAPS[0] * padded[:, 0:out_rows, :]
    for tap_idx in range(1, 5):
        offset = tap_idx * dilation
        running = running + TAPS[tap_idx] * padded[:, offset : offset + out_rows, :]
    return running


def blur_cols(planar, dilation):
    columns = planar.shape[2]
    reach_cols = 2 * dilation
    padded = jnp.pad(planar, ((0, 0), (0, 0), (reach_cols, reach_cols)))
    running = TAPS[0] * padded[:, :, 0:columns]
    for tap_idx in range(1, 5):
        offset = tap_idx * dilation
        running = running + TAPS[tap_idx] * padded[:, :, offset : offset + columns]
    return running


def inside_rows(margin, local_rows):
    first_row = lax.axis_index("rows") * local_rows - margin
    positions = first_row + jnp.arange(local_rows + 2 * margin, dtype=jnp.int32)
    limit = local_rows * lax.axis_size("rows")
    return ((positions >= 0) & (positions < limit)).astype(jnp.float32)[None, :, None]


def analyse(image_cube):
    local_rows = image_cube.shape[1]
    details = []
    depth = 2 ** (SCALES + 1) - 2
    current = padded_2(image_cube, (("rows", 1),), depth)
    inside = inside_rows(depth, local_rows)
    margin = depth
    for level_idx in range(SCALES):
        dilation = 2**level_idx
        reach_rows = 2 * dilation
        new_margin = margin - reach_rows
        out_rows = local_rows + 2 * new_margin
        start_row = depth - new_margin
        smoothed = blur_cols(blur_rows(current, dilation, out_rows), dilation)
        smoothed = smoothed * inside[:, start_row : start_row + out_rows, :]
        kept = current[:, reach_rows : reach_rows + out_rows, :] - smoothed
        details.append(kept[:, new_margin : new_margin + local_rows, :])
        current = smoothed
        margin = new_margin
    return details


def synthesise(space_next):
    local_rows = space_next.shape[2]
    running = jnp.zeros_like(space_next[0])
    for level_idx in reversed(range(SCALES)):
        dilation = 2**level_idx
        operand = running - space_next[level_idx]
        padded = padded_2(operand, (("rows", 1),), 2 * dilation)
        running = (
            blur_cols(blur_rows(padded, dilation, local_rows), dilation) + space_next[level_idx]
        )
    return running


def dct_table(length):
    split = 64 if length % 64 == 0 else 1
    groups = length // split
    period = 4 * length
    coef_idx = jnp.arange(length, dtype=jnp.int32)
    scale = math.pi / (2 * length)
    outer_phase = (coef_idx[:, None] * (2 * split * jnp.arange(groups, dtype=jnp.int32))[None, :]) % period
    inner_phase = (coef_idx[:, None] * (2 * jnp.arange(split, dtype=jnp.int32) + 1)[None, :]) % period
    outer_angle = outer_phase.astype(jnp.float32) * scale
    inner_angle = inner_phase.astype(jnp.float32) * scale
    weights = jnp.where(
        coef_idx == 0, math.sqrt(1.0 / length), math.sqrt(2.0 / length)
    ).astype(jnp.float32)[:, None, None]
    table = (
        jnp.cos(outer_angle)[:, :, None] * jnp.cos(inner_angle)[:, None, :]
        - jnp.sin(outer_angle)[:, :, None] * jnp.sin(inner_angle)[:, None, :]
    ) * weights
    return table.reshape(length, length)


def spectral(pixel_cube, freq_duals):
    chans_all, pixel_count = pixel_cube.shape
    precision = lax.Precision.HIGH
    table = dct_table(chans_all)
    coeffs = lax.dot_general(
        pixel_cube,
        table,
        (((0,), (1,)), ((), ())),
        precision=precision,
        preferred_element_type=jnp.float32,
    )
    freq_next = jnp.clip(freq_duals + SIGMA * coeffs, -FREQ_BOUND, FREQ_BOUND)
    running = lax.dot_general(
        table,
        freq_next,
        (((0,), (1,)), ((), ())),
        precision=precision,
        preferred_element_type=jnp.float32,
    )
    return (running, freq_next)


def smooth_block(x, dilation, inside, lane):
    rows, columns = x.shape
    near = pltpu.roll(x, dilation, 0) + pltpu.roll(x, rows - dilation, 0)
    far = pltpu.roll(x, 2 * dilation, 0) + pltpu.roll(x, rows - 2 * dilation, 0)
    y = TAPS[0] * far + TAPS[1] * near + TAPS[2] * x
    zero = jnp.zeros_like(y)
    near = jnp.where(lane >= dilation, pltpu.roll(y, dilation, 1), zero) + jnp.where(
        lane < columns - dilation, pltpu.roll(y, columns - dilation, 1), zero
    )
    far = jnp.where(lane >= 2 * dilation, pltpu.roll(y, 2 * dilation, 1), zero) + jnp.where(
        lane < columns - 2 * dilation, pltpu.roll(y, columns - 2 * dilation, 1), zero
    )
    z = TAPS[0] * far + TAPS[1] * near + TAPS[2] * y
    return z * inside


def starlet_kernel(top_ref, mid_ref, bot_ref, duals_ref, inside_ref, sn_ref, ttop_ref, tmid_ref, tbot_ref):
    block, local_rows, columns = mid_ref.shape
    extent = 3 * local_rows
    inside = inside_ref[...]
    lane = lax.broadcasted_iota(jnp.int32, (extent, columns), 1)
    pad = jnp.zeros((local_rows, columns), jnp.float32)

    def body(ch, carry):
        current = jnp.concatenate([top_ref[ch], mid_ref[ch], bot_ref[ch]], axis=0)
        fresh = []
        for level_idx in range(SCALES):
            smoothed = smooth_block(current, 2**level_idx, inside, lane)
            detail = (current - smoothed)[local_rows : 2 * local_rows]
            plane = jnp.clip(duals_ref[level_idx, ch] + SIGMA * detail, -SPACE_BOUND, SPACE_BOUND)
            sn_ref[level_idx, ch] = plane
            fresh.append(plane)
            current = smoothed
        running = jnp.zeros((extent, columns), jnp.float32)
        for level_idx in reversed(range(SCALES)):
            plane = jnp.concatenate([pad, fresh[level_idx], pad], axis=0)
            running = smooth_block(running - plane, 2**level_idx, inside, lane) + plane
        ttop_ref[ch] = running[0:local_rows]
        tmid_ref[ch] = running[local_rows : 2 * local_rows]
        tbot_ref[ch] = running[2 * local_rows : extent]
        return carry

    lax.fori_loop(0, block, body, 0)


def starlet(above, image_cube, below, space_duals, inside, interpret=False):
    chans, local_rows, columns = image_cube.shape
    block = math.gcd(chans, 8)
    extent = 3 * local_rows
    plane_spec = pl.BlockSpec((block, local_rows, columns), lambda i: (i, 0, 0))
    dual_spec = pl.BlockSpec((SCALES, block, local_rows, columns), lambda i: (0, i, 0, 0))
    plane_shape = jax.ShapeDtypeStruct(image_cube.shape, jnp.float32)
    return pl.pallas_call(
        starlet_kernel,
        grid=(chans // block,),
        in_specs=[plane_spec, plane_spec, plane_spec, dual_spec, pl.BlockSpec((extent, columns), lambda i: (0, 0))],
        out_specs=[dual_spec, plane_spec, plane_spec, plane_spec],
        out_shape=[jax.ShapeDtypeStruct(space_duals.shape, jnp.float32), plane_shape, plane_shape, plane_shape],
        interpret=interpret,
    )(above, image_cube, below, space_duals, inside)


def spatial(image_cube, space_duals):
    chans, local_rows, columns = image_cube.shape
    assert local_rows >= 2 ** (SCALES + 1) - 2
    count = lax.axis_size("rows")
    down = [(i, i + 1) for i in range(count - 1)]
    up = [(i + 1, i) for i in range(count - 1)]
    above = lax.ppermute(image_cube, "rows", down)
    below = lax.ppermute(image_cube, "rows", up)
    first_row = (lax.axis_index("rows") - 1) * local_rows
    positions = first_row + jnp.arange(3 * local_rows, dtype=jnp.int32)
    inside = ((positions >= 0) & (positions < local_rows * count)).astype(jnp.float32)
    inside = jnp.broadcast_to(inside[:, None], (3 * local_rows, columns))
    space_next, spill_up, own, spill_down = starlet(above, image_cube, below, space_duals, inside)
    space_term = own + lax.ppermute(spill_down, "rows", down) + lax.ppermute(spill_up, "rows", up)
    return space_term, space_next


def local(image_cube, data_grad, space_duals, freq_duals):
    chans, local_rows, columns = image_cube.shape
    peers = lax.axis_size("freq")
    share = local_rows * columns // peers
    pieces = image_cube.reshape(chans, peers, share)
    pixel_cube = lax.all_to_all(pieces, "freq", split_axis=1, concat_axis=0, tiled=True).reshape(
        chans * peers, share
    )
    space_term, space_next = spatial(image_cube, space_duals)
    spectral_sum, freq_next = spectral(pixel_cube, freq_duals)
    returned = lax.all_to_all(
        spectral_sum.reshape(chans * peers, 1, share),
        "freq",
        split_axis=0,
        concat_axis=1,
        tiled=True,
    )
    spectral_term = returned.reshape(chans, local_rows, columns)
    image_next = jnp.maximum(image_cube - TAU_STEP * (data_grad + space_term + spectral_term), 0.0)
    return (image_next, space_next, freq_next)


def solution(mesh):
    in_specs = (
        P("freq", "rows", None),
        P("freq", "rows", None),
        P(None, "freq", "rows", None),
        P(("rows", "freq"), None),
    )
    out_specs = (P("freq", "rows", None), P(None, "freq", "rows", None), P(("rows", "freq"), None))
    return jax.shard_map(local, mesh=mesh, in_specs=in_specs, out_specs=out_specs, check_vma=False)
```

```python
import math

import jax
import jax.numpy as jnp
from jax import lax
from jax.sharding import PartitionSpec as P
from jax.experimental import pallas as pl
from jax.experimental.pallas import tpu as pltpu

SCALES = 4


TAPS = (0.0625, 0.25, 0.375, 0.25, 0.0625)
SIGMA = 0.5
TAU_STEP = 0.5
SPACE_BOUND = 0.5
FREQ_BOUND = 1.0


def padded_2(cells, sides, width):
    for axis, dim in sides:
        count = lax.axis_size(axis)
        ends = count - 1
        head = lax.slice_in_dim(cells, 0, width, axis=dim)
        tail = lax.slice_in_dim(cells, cells.shape[dim] - width, cells.shape[dim], axis=dim)
        cells = jnp.concatenate(
            [
                lax.ppermute(tail, axis, [(i, (i + 1) % count) for i in range(ends)]),
                cells,
                lax.ppermute(head, axis, [((i + 1) % count, i) for i in range(ends)]),
            ],
            axis=dim,
        )
    return cells


def blur_rows(padded, dilation, out_rows):
    running = TAPS[0] * padded[:, 0:out_rows, :]
    for tap_idx in range(1, 5):
        offset = tap_idx * dilation
        running = running + TAPS[tap_idx] * padded[:, offset : offset + out_rows, :]
    return running


def blur_cols(planar, dilation):
    columns = planar.shape[2]
    reach_cols = 2 * dilation
    padded = jnp.pad(planar, ((0, 0), (0, 0), (reach_cols, reach_cols)))
    running = TAPS[0] * padded[:, :, 0:columns]
    for tap_idx in range(1, 5):
        offset = tap_idx * dilation
        running = running + TAPS[tap_idx] * padded[:, :, offset : offset + columns]
    return running


def inside_rows(margin, local_rows):
    first_row = lax.axis_index("rows") * local_rows - margin
    positions = first_row + jnp.arange(local_rows + 2 * margin, dtype=jnp.int32)
    limit = local_rows * lax.axis_size("rows")
    return ((positions >= 0) & (positions < limit)).astype(jnp.float32)[None, :, None]


def analyse(image_cube):
    local_rows = image_cube.shape[1]
    details = []
    depth = 2 ** (SCALES + 1) - 2
    current = padded_2(image_cube, (("rows", 1),), depth)
    inside = inside_rows(depth, local_rows)
    margin = depth
    for level_idx in range(SCALES):
        dilation = 2**level_idx
        reach_rows = 2 * dilation
        new_margin = margin - reach_rows
        out_rows = local_rows + 2 * new_margin
        start_row = depth - new_margin
        smoothed = blur_cols(blur_rows(current, dilation, out_rows), dilation)
        smoothed = smoothed * inside[:, start_row : start_row + out_rows, :]
        kept = current[:, reach_rows : reach_rows + out_rows, :] - smoothed
        details.append(kept[:, new_margin : new_margin + local_rows, :])
        current = smoothed
        margin = new_margin
    return details


def synthesise(space_next):
    local_rows = space_next.shape[2]
    running = jnp.zeros_like(space_next[0])
    for level_idx in reversed(range(SCALES)):
        dilation = 2**level_idx
        operand = running - space_next[level_idx]
        padded = padded_2(operand, (("rows", 1),), 2 * dilation)
        running = (
            blur_cols(blur_rows(padded, dilation, local_rows), dilation) + space_next[level_idx]
        )
    return running


def dct_table(length):
    split = 64 if length % 64 == 0 else 1
    groups = length // split
    period = 4 * length
    coef_idx = jnp.arange(length, dtype=jnp.int32)
    scale = math.pi / (2 * length)
    outer_phase = (coef_idx[:, None] * (2 * split * jnp.arange(groups, dtype=jnp.int32))[None, :]) % period
    inner_phase = (coef_idx[:, None] * (2 * jnp.arange(split, dtype=jnp.int32) + 1)[None, :]) % period
    outer_angle = outer_phase.astype(jnp.float32) * scale
    inner_angle = inner_phase.astype(jnp.float32) * scale
    weights = jnp.where(
        coef_idx == 0, math.sqrt(1.0 / length), math.sqrt(2.0 / length)
    ).astype(jnp.float32)[:, None, None]
    table = (
        jnp.cos(outer_angle)[:, :, None] * jnp.cos(inner_angle)[:, None, :]
        - jnp.sin(outer_angle)[:, :, None] * jnp.sin(inner_angle)[:, None, :]
    ) * weights
    return table.reshape(length, length)


def spectral(pixel_cube, freq_duals):
    chans_all, pixel_count = pixel_cube.shape
    precision = lax.Precision.HIGH
    table = dct_table(chans_all)
    coeffs = lax.dot_general(
        pixel_cube,
        table,
        (((0,), (1,)), ((), ())),
        precision=precision,
        preferred_element_type=jnp.float32,
    )
    freq_next = jnp.clip(freq_duals + SIGMA * coeffs, -FREQ_BOUND, FREQ_BOUND)
    running = lax.dot_general(
        table,
        freq_next,
        (((0,), (1,)), ((), ())),
        precision=precision,
        preferred_element_type=jnp.float32,
    )
    return (running, freq_next)


def starlet_kernel(first_ref, above_ref, own_ref, below_ref, duals_ref, sn_ref, top_ref, mid_ref, bot_ref, buf_a, buf_b):
    halo, block, columns = above_ref.shape
    local_rows = own_ref.shape[0]
    extent = 2 * halo + local_rows
    pad = 2 ** SCALES
    total_rows = first_ref[1]
    row0 = first_ref[0] - halo
    lane = lax.broadcasted_iota(jnp.int32, (block, columns), 1)
    weights = {}
    for level_idx in range(SCALES):
        dilation = 2**level_idx
        weights[dilation] = tuple(
            jnp.where(keep, tap, 0.0).astype(jnp.float32)
            for step, tap in ((dilation, TAPS[1]), (2 * dilation, TAPS[0]))
            for keep in (lane >= step, lane < columns - step)
        )

    def smooth_rows(src, dst, dilation, lo, hi):
        near_w, far_w = weights[dilation][0:2], weights[dilation][2:4]

        def body(e, carry):
            at = e + pad
            y = TAPS[0] * (src[at - 2 * dilation] + src[at + 2 * dilation]) + TAPS[1] * (
                src[at - dilation] + src[at + dilation]
            ) + TAPS[2] * src[at]
            z = (
                pltpu.roll(y, dilation, 1) * near_w[0]
                + pltpu.roll(y, columns - dilation, 1) * near_w[1]
                + pltpu.roll(y, 2 * dilation, 1) * far_w[0]
                + pltpu.roll(y, columns - 2 * dilation, 1) * far_w[1]
                + TAPS[2] * y
            )
            row = row0 + e
            dst[at] = jnp.where((row >= 0) & (row < total_rows), z, 0.0)
            return carry

        lax.fori_loop(lo, hi, body, 0)

    buf_a[...] = jnp.zeros_like(buf_a)
    buf_a[pl.ds(pad, halo)] = above_ref[...]
    buf_a[pl.ds(pad + halo, local_rows)] = own_ref[...]
    buf_a[pl.ds(pad + halo + local_rows, halo)] = below_ref[...]
    bufs = (buf_a, buf_b)
    lo, hi = 0, extent
    for level_idx in range(SCALES):
        dilation = 2**level_idx
        src, dst = bufs[level_idx % 2], bufs[(level_idx + 1) % 2]
        lo, hi = lo + 2 * dilation, hi - 2 * dilation
        smooth_rows(src, dst, dilation, lo, hi)

        def detail_body(r, carry, src=src, dst=dst, level_idx=level_idx):
            at = pad + halo + r
            sn_ref[level_idx, r] = jnp.clip(
                duals_ref[level_idx, r] + SIGMA * (src[at] - dst[at]), -SPACE_BOUND, SPACE_BOUND
            )
            return carry

        lax.fori_loop(0, local_rows, detail_body, 0)

    buf_a[...] = jnp.zeros_like(buf_a)
    buf_b[...] = jnp.zeros_like(buf_b)
    lo, hi = halo, halo + local_rows
    for count, level_idx in enumerate(reversed(range(SCALES))):
        dilation = 2**level_idx
        src, dst = bufs[count % 2], bufs[(count + 1) % 2]
        own = pl.ds(pad + halo, local_rows)
        src[own] = src[own] - sn_ref[level_idx]
        lo, hi = lo - 2 * dilation, hi + 2 * dilation
        smooth_rows(src, dst, dilation, max(lo, 0), min(hi, extent))
        dst[own] = dst[own] + sn_ref[level_idx]
    top_ref[...] = dst[pl.ds(pad, halo)]
    mid_ref[...] = dst[pl.ds(pad + halo, local_rows)]
    bot_ref[...] = dst[pl.ds(pad + halo + local_rows, halo)]


def starlet(first, above, own, below, duals, interpret=False):
    halo, chans, columns = above.shape
    local_rows = own.shape[0]
    block = math.gcd(chans, 8)
    extent = 2 * halo + local_rows + 2 * 2**SCALES
    edge_spec = pl.BlockSpec((halo, block, columns), lambda i: (0, i, 0))
    own_spec = pl.BlockSpec((local_rows, block, columns), lambda i: (0, i, 0))
    dual_spec = pl.BlockSpec((SCALES, local_rows, block, columns), lambda i: (0, 0, i, 0))
    edge_shape = jax.ShapeDtypeStruct(above.shape, jnp.float32)
    return pl.pallas_call(
        starlet_kernel,
        grid=(chans // block,),
        in_specs=[pl.BlockSpec(memory_space=pltpu.SMEM), edge_spec, own_spec, edge_spec, dual_spec],
        out_specs=[dual_spec, edge_spec, own_spec, edge_spec],
        out_shape=[
            jax.ShapeDtypeStruct(duals.shape, jnp.float32),
            edge_shape,
            jax.ShapeDtypeStruct(own.shape, jnp.float32),
            edge_shape,
        ],
        scratch_shapes=[pltpu.VMEM((extent, block, columns), jnp.float32)] * 2,
        interpret=interpret,
    )(first, above, own, below, duals)


def spatial(image_cube, space_duals):
    chans, local_rows, columns = image_cube.shape
    halo = 2 ** (SCALES + 1) - 2
    assert local_rows >= halo
    count = lax.axis_size("rows")
    down = [(i, i + 1) for i in range(count - 1)]
    up = [(i + 1, i) for i in range(count - 1)]
    own = jnp.transpose(image_cube, (1, 0, 2))
    duals = jnp.transpose(space_duals, (0, 2, 1, 3))
    above = lax.ppermute(own[local_rows - halo :], "rows", down)
    below = lax.ppermute(own[:halo], "rows", up)
    first = jnp.stack([lax.axis_index("rows") * local_rows, count * local_rows]).astype(jnp.int32)
    space_next, spill_up, mid, spill_down = starlet(first, above, own, below, duals)
    from_above = lax.ppermute(spill_down, "rows", down)
    from_below = lax.ppermute(spill_up, "rows", up)
    gap = local_rows - halo
    space_term = (
        mid
        + jnp.pad(from_above, ((0, gap), (0, 0), (0, 0)))
        + jnp.pad(from_below, ((gap, 0), (0, 0), (0, 0)))
    )
    return jnp.transpose(space_term, (1, 0, 2)), jnp.transpose(space_next, (0, 2, 1, 3))


def local(image_cube, data_grad, space_duals, freq_duals):
    chans, local_rows, columns = image_cube.shape
    peers = lax.axis_size("freq")
    share = local_rows * columns // peers
    pieces = image_cube.reshape(chans, peers, share)
    pixel_cube = lax.all_to_all(pieces, "freq", split_axis=1, concat_axis=0, tiled=True).reshape(
        chans * peers, share
    )
    space_term, space_next = spatial(image_cube, space_duals)
    spectral_sum, freq_next = spectral(pixel_cube, freq_duals)
    returned = lax.all_to_all(
        spectral_sum.reshape(chans * peers, 1, share),
        "freq",
        split_axis=0,
        concat_axis=1,
        tiled=True,
    )
    spectral_term = returned.reshape(chans, local_rows, columns)
    image_next = jnp.maximum(image_cube - TAU_STEP * (data_grad + space_term + spectral_term), 0.0)
    return (image_next, space_next, freq_next)


def solution(mesh):
    in_specs = (
        P("freq", "rows", None),
        P("freq", "rows", None),
        P(None, "freq", "rows", None),
        P(("rows", "freq"), None),
    )
    out_specs = (P("freq", "rows", None), P(None, "freq", "rows", None), P(("rows", "freq"), None))
    return jax.shard_map(local, mesh=mesh, in_specs=in_specs, out_specs=out_specs, check_vma=False)
```

```python
import math

import jax
import jax.numpy as jnp
from jax import lax
from jax.sharding import PartitionSpec as P
from jax.experimental import pallas as pl
from jax.experimental.pallas import tpu as pltpu

SCALES = 4


TAPS = (0.0625, 0.25, 0.375, 0.25, 0.0625)
SIGMA = 0.5
TAU_STEP = 0.5
SPACE_BOUND = 0.5
FREQ_BOUND = 1.0
CHUNK = 8


def padded_2(cells, sides, width):
    for axis, dim in sides:
        count = lax.axis_size(axis)
        ends = count - 1
        head = lax.slice_in_dim(cells, 0, width, axis=dim)
        tail = lax.slice_in_dim(cells, cells.shape[dim] - width, cells.shape[dim], axis=dim)
        cells = jnp.concatenate(
            [
                lax.ppermute(tail, axis, [(i, (i + 1) % count) for i in range(ends)]),
                cells,
                lax.ppermute(head, axis, [((i + 1) % count, i) for i in range(ends)]),
            ],
            axis=dim,
        )
    return cells


def blur_rows(padded, dilation, out_rows):
    running = TAPS[0] * padded[:, 0:out_rows, :]
    for tap_idx in range(1, 5):
        offset = tap_idx * dilation
        running = running + TAPS[tap_idx] * padded[:, offset : offset + out_rows, :]
    return running


def blur_cols(planar, dilation):
    columns = planar.shape[2]
    reach_cols = 2 * dilation
    padded = jnp.pad(planar, ((0, 0), (0, 0), (reach_cols, reach_cols)))
    running = TAPS[0] * padded[:, :, 0:columns]
    for tap_idx in range(1, 5):
        offset = tap_idx * dilation
        running = running + TAPS[tap_idx] * padded[:, :, offset : offset + columns]
    return running


def inside_rows(margin, local_rows):
    first_row = lax.axis_index("rows") * local_rows - margin
    positions = first_row + jnp.arange(local_rows + 2 * margin, dtype=jnp.int32)
    limit = local_rows * lax.axis_size("rows")
    return ((positions >= 0) & (positions < limit)).astype(jnp.float32)[None, :, None]


def analyse(image_cube):
    local_rows = image_cube.shape[1]
    details = []
    depth = 2 ** (SCALES + 1) - 2
    current = padded_2(image_cube, (("rows", 1),), depth)
    inside = inside_rows(depth, local_rows)
    margin = depth
    for level_idx in range(SCALES):
        dilation = 2**level_idx
        reach_rows = 2 * dilation
        new_margin = margin - reach_rows
        out_rows = local_rows + 2 * new_margin
        start_row = depth - new_margin
        smoothed = blur_cols(blur_rows(current, dilation, out_rows), dilation)
        smoothed = smoothed * inside[:, start_row : start_row + out_rows, :]
        kept = current[:, reach_rows : reach_rows + out_rows, :] - smoothed
        details.append(kept[:, new_margin : new_margin + local_rows, :])
        current = smoothed
        margin = new_margin
    return details


def synthesise(space_next):
    local_rows = space_next.shape[2]
    running = jnp.zeros_like(space_next[0])
    for level_idx in reversed(range(SCALES)):
        dilation = 2**level_idx
        operand = running - space_next[level_idx]
        padded = padded_2(operand, (("rows", 1),), 2 * dilation)
        running = (
            blur_cols(blur_rows(padded, dilation, local_rows), dilation) + space_next[level_idx]
        )
    return running


def dct_table(length):
    split = 64 if length % 64 == 0 else 1
    groups = length // split
    period = 4 * length
    coef_idx = jnp.arange(length, dtype=jnp.int32)
    scale = math.pi / (2 * length)
    outer_phase = (coef_idx[:, None] * (2 * split * jnp.arange(groups, dtype=jnp.int32))[None, :]) % period
    inner_phase = (coef_idx[:, None] * (2 * jnp.arange(split, dtype=jnp.int32) + 1)[None, :]) % period
    outer_angle = outer_phase.astype(jnp.float32) * scale
    inner_angle = inner_phase.astype(jnp.float32) * scale
    weights = jnp.where(
        coef_idx == 0, math.sqrt(1.0 / length), math.sqrt(2.0 / length)
    ).astype(jnp.float32)[:, None, None]
    table = (
        jnp.cos(outer_angle)[:, :, None] * jnp.cos(inner_angle)[:, None, :]
        - jnp.sin(outer_angle)[:, :, None] * jnp.sin(inner_angle)[:, None, :]
    ) * weights
    return table.reshape(length, length)


def spectral(pixel_cube, freq_duals):
    chans_all, pixel_count = pixel_cube.shape
    precision = lax.Precision.HIGH
    table = dct_table(chans_all)
    coeffs = lax.dot_general(
        pixel_cube,
        table,
        (((0,), (1,)), ((), ())),
        precision=precision,
        preferred_element_type=jnp.float32,
    )
    freq_next = jnp.clip(freq_duals + SIGMA * coeffs, -FREQ_BOUND, FREQ_BOUND)
    running = lax.dot_general(
        table,
        freq_next,
        (((0,), (1,)), ((), ())),
        precision=precision,
        preferred_element_type=jnp.float32,
    )
    return (running, freq_next)


def starlet_kernel(first_ref, above_ref, own_ref, below_ref, duals_ref, sn_ref, top_ref, mid_ref, bot_ref, buf_a, buf_b):
    halo, block, columns = above_ref.shape
    local_rows = own_ref.shape[0]
    extent = 2 * halo + local_rows
    pad = 2 ** SCALES
    total_rows = first_ref[1]
    row0 = first_ref[0] - halo
    lane = lax.broadcasted_iota(jnp.int32, (1, block, columns), 2)
    weights = {}
    for level_idx in range(SCALES):
        dilation = 2**level_idx
        weights[dilation] = tuple(
            jnp.where(keep, tap, 0.0).astype(jnp.float32)
            for step, tap in ((dilation, TAPS[1]), (2 * dilation, TAPS[0]))
            for keep in (lane >= step, lane < columns - step)
        )

    def smooth_rows(src, dst, dilation, lo, hi):
        near_w, far_w = weights[dilation][0:2], weights[dilation][2:4]
        for start in range(lo, hi, CHUNK):
            size = min(CHUNK, hi - start)
            at = start + pad

            def window(offset):
                return src[pl.ds(at + offset, size)]

            y = TAPS[0] * (window(-2 * dilation) + window(2 * dilation)) + TAPS[1] * (
                window(-dilation) + window(dilation)
            ) + TAPS[2] * window(0)
            z = (
                pltpu.roll(y, dilation, 2) * near_w[0]
                + pltpu.roll(y, columns - dilation, 2) * near_w[1]
                + pltpu.roll(y, 2 * dilation, 2) * far_w[0]
                + pltpu.roll(y, columns - 2 * dilation, 2) * far_w[1]
                + TAPS[2] * y
            )
            row = row0 + start + lax.broadcasted_iota(jnp.int32, (size, 1, 1), 0)
            dst[pl.ds(at, size)] = jnp.where((row >= 0) & (row < total_rows), z, 0.0)

    buf_a[...] = jnp.zeros_like(buf_a)
    buf_a[pl.ds(pad, halo)] = above_ref[...]
    buf_a[pl.ds(pad + halo, local_rows)] = own_ref[...]
    buf_a[pl.ds(pad + halo + local_rows, halo)] = below_ref[...]
    bufs = (buf_a, buf_b)
    lo, hi = 0, extent
    for level_idx in range(SCALES):
        dilation = 2**level_idx
        src, dst = bufs[level_idx % 2], bufs[(level_idx + 1) % 2]
        lo, hi = lo + 2 * dilation, hi - 2 * dilation
        smooth_rows(src, dst, dilation, lo, hi)

        own = pl.ds(pad + halo, local_rows)
        sn_ref[level_idx] = jnp.clip(
            duals_ref[level_idx] + SIGMA * (src[own] - dst[own]), -SPACE_BOUND, SPACE_BOUND
        )

    buf_a[...] = jnp.zeros_like(buf_a)
    buf_b[...] = jnp.zeros_like(buf_b)
    lo, hi = halo, halo + local_rows
    for count, level_idx in enumerate(reversed(range(SCALES))):
        dilation = 2**level_idx
        src, dst = bufs[count % 2], bufs[(count + 1) % 2]
        own = pl.ds(pad + halo, local_rows)
        src[own] = src[own] - sn_ref[level_idx]
        lo, hi = lo - 2 * dilation, hi + 2 * dilation
        smooth_rows(src, dst, dilation, max(lo, 0), min(hi, extent))
        dst[own] = dst[own] + sn_ref[level_idx]
    top_ref[...] = dst[pl.ds(pad, halo)]
    mid_ref[...] = dst[pl.ds(pad + halo, local_rows)]
    bot_ref[...] = dst[pl.ds(pad + halo + local_rows, halo)]


def starlet(first, above, own, below, duals, interpret=False):
    halo, chans, columns = above.shape
    local_rows = own.shape[0]
    block = math.gcd(chans, 8)
    extent = 2 * halo + local_rows + 2 * 2**SCALES
    edge_spec = pl.BlockSpec((halo, block, columns), lambda i: (0, i, 0))
    own_spec = pl.BlockSpec((local_rows, block, columns), lambda i: (0, i, 0))
    dual_spec = pl.BlockSpec((SCALES, local_rows, block, columns), lambda i: (0, 0, i, 0))
    edge_shape = jax.ShapeDtypeStruct(above.shape, jnp.float32)
    return pl.pallas_call(
        starlet_kernel,
        grid=(chans // block,),
        in_specs=[pl.BlockSpec(memory_space=pltpu.SMEM), edge_spec, own_spec, edge_spec, dual_spec],
        out_specs=[dual_spec, edge_spec, own_spec, edge_spec],
        out_shape=[
            jax.ShapeDtypeStruct(duals.shape, jnp.float32),
            edge_shape,
            jax.ShapeDtypeStruct(own.shape, jnp.float32),
            edge_shape,
        ],
        scratch_shapes=[pltpu.VMEM((extent, block, columns), jnp.float32)] * 2,
        interpret=interpret,
    )(first, above, own, below, duals)


def spatial(image_cube, space_duals):
    chans, local_rows, columns = image_cube.shape
    halo = 2 ** (SCALES + 1) - 2
    assert local_rows >= halo
    count = lax.axis_size("rows")
    down = [(i, i + 1) for i in range(count - 1)]
    up = [(i + 1, i) for i in range(count - 1)]
    own = jnp.transpose(image_cube, (1, 0, 2))
    duals = jnp.transpose(space_duals, (0, 2, 1, 3))
    above = lax.ppermute(own[local_rows - halo :], "rows", down)
    below = lax.ppermute(own[:halo], "rows", up)
    first = jnp.stack([lax.axis_index("rows") * local_rows, count * local_rows]).astype(jnp.int32)
    space_next, spill_up, mid, spill_down = starlet(first, above, own, below, duals)
    from_above = lax.ppermute(spill_down, "rows", down)
    from_below = lax.ppermute(spill_up, "rows", up)
    gap = local_rows - halo
    space_term = (
        mid
        + jnp.pad(from_above, ((0, gap), (0, 0), (0, 0)))
        + jnp.pad(from_below, ((gap, 0), (0, 0), (0, 0)))
    )
    return jnp.transpose(space_term, (1, 0, 2)), jnp.transpose(space_next, (0, 2, 1, 3))


def local(image_cube, data_grad, space_duals, freq_duals):
    chans, local_rows, columns = image_cube.shape
    peers = lax.axis_size("freq")
    share = local_rows * columns // peers
    pieces = image_cube.reshape(chans, peers, share)
    pixel_cube = lax.all_to_all(pieces, "freq", split_axis=1, concat_axis=0, tiled=True).reshape(
        chans * peers, share
    )
    space_term, space_next = spatial(image_cube, space_duals)
    spectral_sum, freq_next = spectral(pixel_cube, freq_duals)
    returned = lax.all_to_all(
        spectral_sum.reshape(chans * peers, 1, share),
        "freq",
        split_axis=0,
        concat_axis=1,
        tiled=True,
    )
    spectral_term = returned.reshape(chans, local_rows, columns)
    image_next = jnp.maximum(image_cube - TAU_STEP * (data_grad + space_term + spectral_term), 0.0)
    return (image_next, space_next, freq_next)


def solution(mesh):
    in_specs = (
        P("freq", "rows", None),
        P("freq", "rows", None),
        P(None, "freq", "rows", None),
        P(("rows", "freq"), None),
    )
    out_specs = (P("freq", "rows", None), P(None, "freq", "rows", None), P(("rows", "freq"), None))
    return jax.shard_map(local, mesh=mesh, in_specs=in_specs, out_specs=out_specs, check_vma=False)
```

```python
import math

import jax
import jax.numpy as jnp
from jax import lax
from jax.sharding import PartitionSpec as P
from jax.experimental import pallas as pl
from jax.experimental.pallas import tpu as pltpu

SCALES = 4


TAPS = (0.0625, 0.25, 0.375, 0.25, 0.0625)
SIGMA = 0.5
TAU_STEP = 0.5
SPACE_BOUND = 0.5
FREQ_BOUND = 1.0
CHUNK = 8


def padded_2(cells, sides, width):
    for axis, dim in sides:
        count = lax.axis_size(axis)
        ends = count - 1
        head = lax.slice_in_dim(cells, 0, width, axis=dim)
        tail = lax.slice_in_dim(cells, cells.shape[dim] - width, cells.shape[dim], axis=dim)
        cells = jnp.concatenate(
            [
                lax.ppermute(tail, axis, [(i, (i + 1) % count) for i in range(ends)]),
                cells,
                lax.ppermute(head, axis, [((i + 1) % count, i) for i in range(ends)]),
            ],
            axis=dim,
        )
    return cells


def blur_rows(padded, dilation, out_rows):
    running = TAPS[0] * padded[:, 0:out_rows, :]
    for tap_idx in range(1, 5):
        offset = tap_idx * dilation
        running = running + TAPS[tap_idx] * padded[:, offset : offset + out_rows, :]
    return running


def blur_cols(planar, dilation):
    columns = planar.shape[2]
    reach_cols = 2 * dilation
    padded = jnp.pad(planar, ((0, 0), (0, 0), (reach_cols, reach_cols)))
    running = TAPS[0] * padded[:, :, 0:columns]
    for tap_idx in range(1, 5):
        offset = tap_idx * dilation
        running = running + TAPS[tap_idx] * padded[:, :, offset : offset + columns]
    return running


def inside_rows(margin, local_rows):
    first_row = lax.axis_index("rows") * local_rows - margin
    positions = first_row + jnp.arange(local_rows + 2 * margin, dtype=jnp.int32)
    limit = local_rows * lax.axis_size("rows")
    return ((positions >= 0) & (positions < limit)).astype(jnp.float32)[None, :, None]


def analyse(image_cube):
    local_rows = image_cube.shape[1]
    details = []
    depth = 2 ** (SCALES + 1) - 2
    current = padded_2(image_cube, (("rows", 1),), depth)
    inside = inside_rows(depth, local_rows)
    margin = depth
    for level_idx in range(SCALES):
        dilation = 2**level_idx
        reach_rows = 2 * dilation
        new_margin = margin - reach_rows
        out_rows = local_rows + 2 * new_margin
        start_row = depth - new_margin
        smoothed = blur_cols(blur_rows(current, dilation, out_rows), dilation)
        smoothed = smoothed * inside[:, start_row : start_row + out_rows, :]
        kept = current[:, reach_rows : reach_rows + out_rows, :] - smoothed
        details.append(kept[:, new_margin : new_margin + local_rows, :])
        current = smoothed
        margin = new_margin
    return details


def synthesise(space_next):
    local_rows = space_next.shape[2]
    running = jnp.zeros_like(space_next[0])
    for level_idx in reversed(range(SCALES)):
        dilation = 2**level_idx
        operand = running - space_next[level_idx]
        padded = padded_2(operand, (("rows", 1),), 2 * dilation)
        running = (
            blur_cols(blur_rows(padded, dilation, local_rows), dilation) + space_next[level_idx]
        )
    return running


def dct_table(length):
    split = 64 if length % 64 == 0 else 1
    groups = length // split
    period = 4 * length
    coef_idx = jnp.arange(length, dtype=jnp.int32)
    scale = math.pi / (2 * length)
    outer_phase = (coef_idx[:, None] * (2 * split * jnp.arange(groups, dtype=jnp.int32))[None, :]) % period
    inner_phase = (coef_idx[:, None] * (2 * jnp.arange(split, dtype=jnp.int32) + 1)[None, :]) % period
    outer_angle = outer_phase.astype(jnp.float32) * scale
    inner_angle = inner_phase.astype(jnp.float32) * scale
    weights = jnp.where(
        coef_idx == 0, math.sqrt(1.0 / length), math.sqrt(2.0 / length)
    ).astype(jnp.float32)[:, None, None]
    table = (
        jnp.cos(outer_angle)[:, :, None] * jnp.cos(inner_angle)[:, None, :]
        - jnp.sin(outer_angle)[:, :, None] * jnp.sin(inner_angle)[:, None, :]
    ) * weights
    return table.reshape(length, length)


def spectral(pixel_cube, freq_duals):
    chans_all, pixel_count = pixel_cube.shape
    precision = lax.Precision.HIGH
    table = dct_table(chans_all)
    coeffs = lax.dot_general(
        pixel_cube,
        table,
        (((0,), (1,)), ((), ())),
        precision=precision,
        preferred_element_type=jnp.float32,
    )
    freq_next = jnp.clip(freq_duals + SIGMA * coeffs, -FREQ_BOUND, FREQ_BOUND)
    running = lax.dot_general(
        table,
        freq_next,
        (((0,), (1,)), ((), ())),
        precision=precision,
        preferred_element_type=jnp.float32,
    )
    return (running, freq_next)


def starlet_kernel(first_ref, above_ref, own_ref, below_ref, duals_ref, sn_ref, top_ref, mid_ref, bot_ref, buf_a, buf_b):
    halo, block, columns = above_ref.shape
    local_rows = own_ref.shape[0]
    extent = 2 * halo + local_rows
    pad = 2 ** SCALES
    total_rows = first_ref[1]
    row0 = first_ref[0] - halo
    lane = lax.broadcasted_iota(jnp.int32, (1, block, columns), 2)
    weights = {}
    for level_idx in range(SCALES):
        dilation = 2**level_idx
        weights[dilation] = tuple(
            jnp.where(keep, tap, 0.0).astype(jnp.float32)
            for step, tap in ((dilation, TAPS[1]), (2 * dilation, TAPS[0]))
            for keep in (lane >= step, lane < columns - step)
        )

    def smooth_rows(src, dst, dilation, lo, hi):
        near_w, far_w = weights[dilation][0:2], weights[dilation][2:4]
        for start in range(lo, hi, CHUNK):
            size = min(CHUNK, hi - start)
            at = start + pad

            def window(offset):
                return src[pl.ds(at + offset, size)]

            y = TAPS[0] * (window(-2 * dilation) + window(2 * dilation)) + TAPS[1] * (
                window(-dilation) + window(dilation)
            ) + TAPS[2] * window(0)
            z = (
                pltpu.roll(y, dilation, 2) * near_w[0]
                + pltpu.roll(y, columns - dilation, 2) * near_w[1]
                + pltpu.roll(y, 2 * dilation, 2) * far_w[0]
                + pltpu.roll(y, columns - 2 * dilation, 2) * far_w[1]
                + TAPS[2] * y
            )
            row = row0 + start + lax.broadcasted_iota(jnp.int32, (size, 1, 1), 0)
            dst[pl.ds(at, size)] = jnp.where((row >= 0) & (row < total_rows), z, 0.0)

    buf_a[...] = jnp.zeros_like(buf_a)
    buf_a[pl.ds(pad, halo)] = above_ref[...]
    buf_a[pl.ds(pad + halo, local_rows)] = own_ref[...]
    buf_a[pl.ds(pad + halo + local_rows, halo)] = below_ref[...]
    bufs = (buf_a, buf_b)
    lo, hi = 0, extent
    for level_idx in range(SCALES):
        dilation = 2**level_idx
        src, dst = bufs[level_idx % 2], bufs[(level_idx + 1) % 2]
        lo, hi = lo + 2 * dilation, hi - 2 * dilation
        smooth_rows(src, dst, dilation, lo, hi)

        own = pl.ds(pad + halo, local_rows)
        sn_ref[level_idx] = jnp.clip(
            duals_ref[level_idx] + SIGMA * (src[own] - dst[own]), -SPACE_BOUND, SPACE_BOUND
        )

    buf_a[...] = jnp.zeros_like(buf_a)
    buf_b[...] = jnp.zeros_like(buf_b)
    lo, hi = halo, halo + local_rows
    for count, level_idx in enumerate(reversed(range(SCALES))):
        dilation = 2**level_idx
        src, dst = bufs[count % 2], bufs[(count + 1) % 2]
        own = pl.ds(pad + halo, local_rows)
        src[own] = src[own] - sn_ref[level_idx]
        lo, hi = lo - 2 * dilation, hi + 2 * dilation
        smooth_rows(src, dst, dilation, max(lo, 0), min(hi, extent))
        dst[own] = dst[own] + sn_ref[level_idx]
    top_ref[...] = dst[pl.ds(pad, halo)]
    mid_ref[...] = dst[pl.ds(pad + halo, local_rows)]
    bot_ref[...] = dst[pl.ds(pad + halo + local_rows, halo)]


def starlet(first, above, own, below, duals, interpret=False):
    halo, chans, columns = above.shape
    local_rows = own.shape[0]
    block = math.gcd(chans, 8)
    extent = 2 * halo + local_rows + 2 * 2**SCALES
    edge_spec = pl.BlockSpec((halo, block, columns), lambda i: (0, i, 0))
    own_spec = pl.BlockSpec((local_rows, block, columns), lambda i: (0, i, 0))
    dual_spec = pl.BlockSpec((SCALES, local_rows, block, columns), lambda i: (0, 0, i, 0))
    edge_shape = jax.ShapeDtypeStruct(above.shape, jnp.float32)
    return pl.pallas_call(
        starlet_kernel,
        grid=(chans // block,),
        in_specs=[pl.BlockSpec(memory_space=pltpu.SMEM), edge_spec, own_spec, edge_spec, dual_spec],
        out_specs=[dual_spec, edge_spec, own_spec, edge_spec],
        out_shape=[
            jax.ShapeDtypeStruct(duals.shape, jnp.float32),
            edge_shape,
            jax.ShapeDtypeStruct(own.shape, jnp.float32),
            edge_shape,
        ],
        scratch_shapes=[pltpu.VMEM((extent, block, columns), jnp.float32)] * 2,
        interpret=interpret,
    )(first, above, own, below, duals)


def swap_rows(lower, upper):
    count = lax.axis_size("rows")
    down = [(i, i + 1) for i in range(count - 1)]
    up = [(i + 1, i) for i in range(count - 1)]
    if count != 2:
        return lax.ppermute(lower, "rows", down), lax.ppermute(upper, "rows", up)
    first = lax.axis_index("rows") == 0
    got = lax.ppermute(jnp.where(first, lower, upper), "rows", down + up)
    zero = jnp.zeros_like(got)
    return jnp.where(first, zero, got), jnp.where(first, got, zero)


def spatial(image_cube, space_duals):
    chans, local_rows, columns = image_cube.shape
    halo = 2 ** (SCALES + 1) - 2
    assert local_rows >= halo
    count = lax.axis_size("rows")
    own = jnp.transpose(image_cube, (1, 0, 2))
    duals = jnp.transpose(space_duals, (0, 2, 1, 3))
    above, below = swap_rows(own[local_rows - halo :], own[:halo])
    first = jnp.stack([lax.axis_index("rows") * local_rows, count * local_rows]).astype(jnp.int32)
    space_next, spill_up, mid, spill_down = starlet(first, above, own, below, duals)
    from_above, from_below = swap_rows(spill_down, spill_up)
    gap = local_rows - halo
    space_term = (
        mid
        + jnp.pad(from_above, ((0, gap), (0, 0), (0, 0)))
        + jnp.pad(from_below, ((gap, 0), (0, 0), (0, 0)))
    )
    return jnp.transpose(space_term, (1, 0, 2)), jnp.transpose(space_next, (0, 2, 1, 3))


def local(image_cube, data_grad, space_duals, freq_duals):
    chans, local_rows, columns = image_cube.shape
    peers = lax.axis_size("freq")
    share = local_rows * columns // peers
    pieces = image_cube.reshape(chans, peers, share)
    pixel_cube = lax.all_to_all(pieces, "freq", split_axis=1, concat_axis=0, tiled=True).reshape(
        chans * peers, share
    )
    space_term, space_next = spatial(image_cube, space_duals)
    spectral_sum, freq_next = spectral(pixel_cube, freq_duals)
    returned = lax.all_to_all(
        spectral_sum.reshape(peers, chans, share),
        "freq",
        split_axis=0,
        concat_axis=2,
        tiled=True,
    )
    spectral_term = returned.reshape(chans, local_rows, columns)
    image_next = jnp.maximum(image_cube - TAU_STEP * (data_grad + space_term + spectral_term), 0.0)
    return (image_next, space_next, freq_next)


def solution(mesh):
    in_specs = (
        P("freq", "rows", None),
        P("freq", "rows", None),
        P(None, "freq", "rows", None),
        P(("rows", "freq"), None),
    )
    out_specs = (P("freq", "rows", None), P(None, "freq", "rows", None), P(("rows", "freq"), None))
    return jax.shard_map(local, mesh=mesh, in_specs=in_specs, out_specs=out_specs, check_vma=False)
```

```python
import math

import jax
import jax.numpy as jnp
from jax import lax
from jax.sharding import PartitionSpec as P
from jax.experimental import pallas as pl
from jax.experimental.pallas import tpu as pltpu

SCALES = 4


TAPS = (0.0625, 0.25, 0.375, 0.25, 0.0625)
SIGMA = 0.5
TAU_STEP = 0.5
SPACE_BOUND = 0.5
FREQ_BOUND = 1.0
CHUNK = 8


def padded_2(cells, sides, width):
    for axis, dim in sides:
        count = lax.axis_size(axis)
        ends = count - 1
        head = lax.slice_in_dim(cells, 0, width, axis=dim)
        tail = lax.slice_in_dim(cells, cells.shape[dim] - width, cells.shape[dim], axis=dim)
        cells = jnp.concatenate(
            [
                lax.ppermute(tail, axis, [(i, (i + 1) % count) for i in range(ends)]),
                cells,
                lax.ppermute(head, axis, [((i + 1) % count, i) for i in range(ends)]),
            ],
            axis=dim,
        )
    return cells


def blur_rows(padded, dilation, out_rows):
    running = TAPS[0] * padded[:, 0:out_rows, :]
    for tap_idx in range(1, 5):
        offset = tap_idx * dilation
        running = running + TAPS[tap_idx] * padded[:, offset : offset + out_rows, :]
    return running


def blur_cols(planar, dilation):
    columns = planar.shape[2]
    reach_cols = 2 * dilation
    padded = jnp.pad(planar, ((0, 0), (0, 0), (reach_cols, reach_cols)))
    running = TAPS[0] * padded[:, :, 0:columns]
    for tap_idx in range(1, 5):
        offset = tap_idx * dilation
        running = running + TAPS[tap_idx] * padded[:, :, offset : offset + columns]
    return running


def inside_rows(margin, local_rows):
    first_row = lax.axis_index("rows") * local_rows - margin
    positions = first_row + jnp.arange(local_rows + 2 * margin, dtype=jnp.int32)
    limit = local_rows * lax.axis_size("rows")
    return ((positions >= 0) & (positions < limit)).astype(jnp.float32)[None, :, None]


def analyse(image_cube):
    local_rows = image_cube.shape[1]
    details = []
    depth = 2 ** (SCALES + 1) - 2
    current = padded_2(image_cube, (("rows", 1),), depth)
    inside = inside_rows(depth, local_rows)
    margin = depth
    for level_idx in range(SCALES):
        dilation = 2**level_idx
        reach_rows = 2 * dilation
        new_margin = margin - reach_rows
        out_rows = local_rows + 2 * new_margin
        start_row = depth - new_margin
        smoothed = blur_cols(blur_rows(current, dilation, out_rows), dilation)
        smoothed = smoothed * inside[:, start_row : start_row + out_rows, :]
        kept = current[:, reach_rows : reach_rows + out_rows, :] - smoothed
        details.append(kept[:, new_margin : new_margin + local_rows, :])
        current = smoothed
        margin = new_margin
    return details


def synthesise(space_next):
    local_rows = space_next.shape[2]
    running = jnp.zeros_like(space_next[0])
    for level_idx in reversed(range(SCALES)):
        dilation = 2**level_idx
        operand = running - space_next[level_idx]
        padded = padded_2(operand, (("rows", 1),), 2 * dilation)
        running = (
            blur_cols(blur_rows(padded, dilation, local_rows), dilation) + space_next[level_idx]
        )
    return running


def dct_table(length):
    split = 64 if length % 64 == 0 else 1
    groups = length // split
    period = 4 * length
    coef_idx = jnp.arange(length, dtype=jnp.int32)
    scale = math.pi / (2 * length)
    outer_phase = (coef_idx[:, None] * (2 * split * jnp.arange(groups, dtype=jnp.int32))[None, :]) % period
    inner_phase = (coef_idx[:, None] * (2 * jnp.arange(split, dtype=jnp.int32) + 1)[None, :]) % period
    outer_angle = outer_phase.astype(jnp.float32) * scale
    inner_angle = inner_phase.astype(jnp.float32) * scale
    weights = jnp.where(
        coef_idx == 0, math.sqrt(1.0 / length), math.sqrt(2.0 / length)
    ).astype(jnp.float32)[:, None, None]
    table = (
        jnp.cos(outer_angle)[:, :, None] * jnp.cos(inner_angle)[:, None, :]
        - jnp.sin(outer_angle)[:, :, None] * jnp.sin(inner_angle)[:, None, :]
    ) * weights
    return table.reshape(length, length)


def spectral(pixel_cube, freq_duals):
    chans_all, pixel_count = pixel_cube.shape
    precision = lax.Precision.HIGH
    table = dct_table(chans_all)
    coeffs = lax.dot_general(
        pixel_cube,
        table,
        (((0,), (1,)), ((), ())),
        precision=precision,
        preferred_element_type=jnp.float32,
    )
    freq_next = jnp.clip(freq_duals + SIGMA * coeffs, -FREQ_BOUND, FREQ_BOUND)
    return table, freq_next


def spectral_back(table, freq_next):
    precision = lax.Precision.HIGH
    return lax.dot_general(
        table,
        freq_next,
        (((0,), (1,)), ((), ())),
        precision=precision,
        preferred_element_type=jnp.float32,
    )


def starlet_kernel(flags_ref, above_ref, own_ref, below_ref, duals_ref, sn_ref, send_ref, mid_ref, keep_ref, buf_a, buf_b):
    block, local_rows, columns = own_ref.shape
    halo = send_ref.shape[0]
    extent = 2 * halo + local_rows
    pad = 2 ** SCALES
    row0 = flags_ref[0] - halo
    total_rows = flags_ref[1]
    lane = lax.broadcasted_iota(jnp.int32, (1, block, columns), 2)
    weights = {}
    for level_idx in range(SCALES):
        dilation = 2**level_idx
        weights[dilation] = tuple(
            jnp.where(keep, tap, 0.0).astype(jnp.float32)
            for step, tap in ((dilation, TAPS[1]), (2 * dilation, TAPS[0]))
            for keep in (lane >= step, lane < columns - step)
        )

    def smooth_rows(src, dst, dilation, lo, hi):
        near_w, far_w = weights[dilation][0:2], weights[dilation][2:4]
        for start in range(lo, hi, CHUNK):
            size = min(CHUNK, hi - start)
            at = start + pad

            def window(offset):
                return src[pl.ds(at + offset, size)]

            y = TAPS[0] * (window(-2 * dilation) + window(2 * dilation)) + TAPS[1] * (
                window(-dilation) + window(dilation)
            ) + TAPS[2] * window(0)
            z = (
                pltpu.roll(y, dilation, 2) * near_w[0]
                + pltpu.roll(y, columns - dilation, 2) * near_w[1]
                + pltpu.roll(y, 2 * dilation, 2) * far_w[0]
                + pltpu.roll(y, columns - 2 * dilation, 2) * far_w[1]
                + TAPS[2] * y
            )
            if start >= halo and start + size <= halo + local_rows:
                dst[pl.ds(at, size)] = z
            else:
                row = row0 + start + lax.broadcasted_iota(jnp.int32, (size, 1, 1), 0)
                dst[pl.ds(at, size)] = jnp.where((row >= 0) & (row < total_rows), z, 0.0)

    def rows_major(value):
        return jnp.swapaxes(value, 0, 1)

    buf_a[...] = jnp.zeros_like(buf_a)
    above = rows_major(above_ref[...])[local_rows - halo :]
    below = rows_major(below_ref[...])[:halo]
    buf_a[pl.ds(pad, halo)] = jnp.where(flags_ref[2] > 0, above, 0.0)
    buf_a[pl.ds(pad + halo, local_rows)] = rows_major(own_ref[...])
    buf_a[pl.ds(pad + halo + local_rows, halo)] = jnp.where(flags_ref[3] > 0, below, 0.0)
    bufs = (buf_a, buf_b)
    own = pl.ds(pad + halo, local_rows)
    fresh = []
    lo, hi = 0, extent
    for level_idx in range(SCALES):
        dilation = 2**level_idx
        src, dst = bufs[level_idx % 2], bufs[(level_idx + 1) % 2]
        lo, hi = lo + 2 * dilation, hi - 2 * dilation
        smooth_rows(src, dst, dilation, lo, hi)
        plane = jnp.clip(
            duals_ref[level_idx] + SIGMA * rows_major(src[own] - dst[own]), -SPACE_BOUND, SPACE_BOUND
        )
        sn_ref[level_idx] = plane

    buf_a[...] = jnp.zeros_like(buf_a)
    buf_b[...] = jnp.zeros_like(buf_b)
    lo, hi = halo, halo + local_rows
    for count, level_idx in enumerate(reversed(range(SCALES))):
        dilation = 2**level_idx
        src, dst = bufs[count % 2], bufs[(count + 1) % 2]
        plane = rows_major(sn_ref[level_idx])
        src[own] = src[own] - plane
        lo, hi = lo - 2 * dilation, hi + 2 * dilation
        smooth_rows(src, dst, dilation, max(lo, 0), min(hi, extent))
        dst[own] = dst[own] + plane
    top = dst[pl.ds(pad, halo)]
    bot = dst[pl.ds(pad + halo + local_rows, halo)]
    swap = flags_ref[4] > 0
    send_ref[...] = jnp.where(swap, bot, top)
    keep_ref[...] = jnp.where(swap, top, bot)
    mid_ref[...] = rows_major(dst[own])


def starlet(flags, above, own, below, duals, halo, interpret=False):
    chans, local_rows, columns = own.shape
    block = math.gcd(chans, 8)
    extent = 2 * halo + local_rows + 2 * 2**SCALES
    edge_spec = pl.BlockSpec((halo, block, columns), lambda i: (0, i, 0))
    own_spec = pl.BlockSpec((block, local_rows, columns), lambda i: (i, 0, 0))
    dual_spec = pl.BlockSpec((SCALES, block, local_rows, columns), lambda i: (0, i, 0, 0))
    edge_shape = jax.ShapeDtypeStruct((halo, chans, columns), jnp.float32)
    return pl.pallas_call(
        starlet_kernel,
        grid=(chans // block,),
        in_specs=[pl.BlockSpec(memory_space=pltpu.SMEM), own_spec, own_spec, own_spec, dual_spec],
        out_specs=[dual_spec, edge_spec, own_spec, edge_spec],
        out_shape=[
            jax.ShapeDtypeStruct(duals.shape, jnp.float32),
            edge_shape,
            jax.ShapeDtypeStruct(own.shape, jnp.float32),
            edge_shape,
        ],
        scratch_shapes=[pltpu.VMEM((extent, block, columns), jnp.float32)] * 2,
        interpret=interpret,
    )(flags, above, own, below, duals)


def spatial(image_cube, space_duals):
    chans, local_rows, columns = image_cube.shape
    halo = 2 ** (SCALES + 1) - 2
    assert local_rows >= halo
    count = lax.axis_size("rows")
    index = lax.axis_index("rows")
    down = [(i, i + 1) for i in range(count - 1)]
    up = [(i + 1, i) for i in range(count - 1)]
    paired = count == 2
    flags = jnp.stack(
        [index * local_rows, count * local_rows, index > 0, index < count - 1, paired & (index == 0)]
    ).astype(jnp.int32)
    if paired:
        above = below = lax.ppermute(image_cube, "rows", down + up)
    else:
        above = lax.ppermute(image_cube, "rows", down)
        below = lax.ppermute(image_cube, "rows", up)
    space_next, send, mid, keep = starlet(flags, above, image_cube, below, space_duals, halo)
    return space_next, send, mid, keep


def settle(mid, send, keep):
    local_rows = mid.shape[1]
    halo = send.shape[0]
    gap = local_rows - halo
    count = lax.axis_size("rows")
    down = [(i, i + 1) for i in range(count - 1)]
    up = [(i + 1, i) for i in range(count - 1)]
    if count == 2:
        got = lax.ppermute(send, "rows", down + up)
        first = lax.axis_index("rows") == 0
        spill = jnp.where(
            first,
            jnp.pad(got, ((gap, 0), (0, 0), (0, 0))),
            jnp.pad(got, ((0, gap), (0, 0), (0, 0))),
        )
    else:
        spill = jnp.pad(lax.ppermute(keep, "rows", down), ((0, gap), (0, 0), (0, 0))) + jnp.pad(
            lax.ppermute(send, "rows", up), ((gap, 0), (0, 0), (0, 0))
        )
    return mid + jnp.transpose(spill, (1, 0, 2))


def local(image_cube, data_grad, space_duals, freq_duals):
    chans, local_rows, columns = image_cube.shape
    peers = lax.axis_size("freq")
    share = local_rows * columns // peers
    pieces = image_cube.reshape(chans, peers, share)
    pixel_cube = lax.all_to_all(pieces, "freq", split_axis=1, concat_axis=0, tiled=True).reshape(
        chans * peers, share
    )
    table, freq_next = spectral(pixel_cube, freq_duals)
    space_next, send, mid, keep = spatial(image_cube, space_duals)
    send, keep, freq_next = lax.optimization_barrier((send, keep, freq_next))
    spectral_sum = spectral_back(table, freq_next)
    space_term = settle(mid, send, keep)
    returned = lax.all_to_all(
        spectral_sum.reshape(peers, chans, share),
        "freq",
        split_axis=0,
        concat_axis=2,
        tiled=True,
    )
    spectral_term = returned.reshape(chans, local_rows, columns)
    image_next = jnp.maximum(image_cube - TAU_STEP * (data_grad + space_term + spectral_term), 0.0)
    return (image_next, space_next, freq_next)


def solution(mesh):
    in_specs = (
        P("freq", "rows", None),
        P("freq", "rows", None),
        P(None, "freq", "rows", None),
        P(("rows", "freq"), None),
    )
    out_specs = (P("freq", "rows", None), P(None, "freq", "rows", None), P(("rows", "freq"), None))
    return jax.shard_map(local, mesh=mesh, in_specs=in_specs, out_specs=out_specs, check_vma=False)
```

```python
import math

import jax
import jax.numpy as jnp
from jax import lax
from jax.sharding import PartitionSpec as P
from jax.experimental import pallas as pl
from jax.experimental.pallas import tpu as pltpu

SCALES = 4


TAPS = (0.0625, 0.25, 0.375, 0.25, 0.0625)
SIGMA = 0.5
TAU_STEP = 0.5
SPACE_BOUND = 0.5
FREQ_BOUND = 1.0
CHUNK = 8
GROUPS = 4


def padded_2(cells, sides, width):
    for axis, dim in sides:
        count = lax.axis_size(axis)
        ends = count - 1
        head = lax.slice_in_dim(cells, 0, width, axis=dim)
        tail = lax.slice_in_dim(cells, cells.shape[dim] - width, cells.shape[dim], axis=dim)
        cells = jnp.concatenate(
            [
                lax.ppermute(tail, axis, [(i, (i + 1) % count) for i in range(ends)]),
                cells,
                lax.ppermute(head, axis, [((i + 1) % count, i) for i in range(ends)]),
            ],
            axis=dim,
        )
    return cells


def blur_rows(padded, dilation, out_rows):
    running = TAPS[0] * padded[:, 0:out_rows, :]
    for tap_idx in range(1, 5):
        offset = tap_idx * dilation
        running = running + TAPS[tap_idx] * padded[:, offset : offset + out_rows, :]
    return running


def blur_cols(planar, dilation):
    columns = planar.shape[2]
    reach_cols = 2 * dilation
    padded = jnp.pad(planar, ((0, 0), (0, 0), (reach_cols, reach_cols)))
    running = TAPS[0] * padded[:, :, 0:columns]
    for tap_idx in range(1, 5):
        offset = tap_idx * dilation
        running = running + TAPS[tap_idx] * padded[:, :, offset : offset + columns]
    return running


def inside_rows(margin, local_rows):
    first_row = lax.axis_index("rows") * local_rows - margin
    positions = first_row + jnp.arange(local_rows + 2 * margin, dtype=jnp.int32)
    limit = local_rows * lax.axis_size("rows")
    return ((positions >= 0) & (positions < limit)).astype(jnp.float32)[None, :, None]


def analyse(image_cube):
    local_rows = image_cube.shape[1]
    details = []
    depth = 2 ** (SCALES + 1) - 2
    current = padded_2(image_cube, (("rows", 1),), depth)
    inside = inside_rows(depth, local_rows)
    margin = depth
    for level_idx in range(SCALES):
        dilation = 2**level_idx
        reach_rows = 2 * dilation
        new_margin = margin - reach_rows
        out_rows = local_rows + 2 * new_margin
        start_row = depth - new_margin
        smoothed = blur_cols(blur_rows(current, dilation, out_rows), dilation)
        smoothed = smoothed * inside[:, start_row : start_row + out_rows, :]
        kept = current[:, reach_rows : reach_rows + out_rows, :] - smoothed
        details.append(kept[:, new_margin : new_margin + local_rows, :])
        current = smoothed
        margin = new_margin
    return details


def synthesise(space_next):
    local_rows = space_next.shape[2]
    running = jnp.zeros_like(space_next[0])
    for level_idx in reversed(range(SCALES)):
        dilation = 2**level_idx
        operand = running - space_next[level_idx]
        padded = padded_2(operand, (("rows", 1),), 2 * dilation)
        running = (
            blur_cols(blur_rows(padded, dilation, local_rows), dilation) + space_next[level_idx]
        )
    return running


def dct_table(length):
    split = 64 if length % 64 == 0 else 1
    groups = length // split
    period = 4 * length
    coef_idx = jnp.arange(length, dtype=jnp.int32)
    scale = math.pi / (2 * length)
    outer_phase = (coef_idx[:, None] * (2 * split * jnp.arange(groups, dtype=jnp.int32))[None, :]) % period
    inner_phase = (coef_idx[:, None] * (2 * jnp.arange(split, dtype=jnp.int32) + 1)[None, :]) % period
    outer_angle = outer_phase.astype(jnp.float32) * scale
    inner_angle = inner_phase.astype(jnp.float32) * scale
    weights = jnp.where(
        coef_idx == 0, math.sqrt(1.0 / length), math.sqrt(2.0 / length)
    ).astype(jnp.float32)[:, None, None]
    table = (
        jnp.cos(outer_angle)[:, :, None] * jnp.cos(inner_angle)[:, None, :]
        - jnp.sin(outer_angle)[:, :, None] * jnp.sin(inner_angle)[:, None, :]
    ) * weights
    return table.reshape(length, length)


def spectral(pixel_cube, freq_duals):
    chans_all, pixel_count = pixel_cube.shape
    precision = lax.Precision.HIGH
    table = dct_table(chans_all)
    coeffs = lax.dot_general(
        pixel_cube,
        table,
        (((0,), (1,)), ((), ())),
        precision=precision,
        preferred_element_type=jnp.float32,
    )
    freq_next = jnp.clip(freq_duals + SIGMA * coeffs, -FREQ_BOUND, FREQ_BOUND)
    return table, freq_next


def spectral_back(table, freq_next):
    precision = lax.Precision.HIGH
    return lax.dot_general(
        table,
        freq_next,
        (((0,), (1,)), ((), ())),
        precision=precision,
        preferred_element_type=jnp.float32,
    )


def starlet_kernel(flags_ref, above_ref, own_ref, below_ref, duals_ref, *refs):
    sn_ref, send_ref, mid_ref, keep_ref, buf_a, buf_b = refs[-6:]
    block, local_rows, columns = own_ref.shape
    halo = send_ref.shape[0]
    extent = 2 * halo + local_rows
    pad = 2 ** SCALES
    row0 = flags_ref[0] - halo
    total_rows = flags_ref[1]
    lane = lax.broadcasted_iota(jnp.int32, (1, block, columns), 2)
    weights = {}
    for level_idx in range(SCALES):
        dilation = 2**level_idx
        weights[dilation] = tuple(
            jnp.where(keep, tap, 0.0).astype(jnp.float32)
            for step, tap in ((dilation, TAPS[1]), (2 * dilation, TAPS[0]))
            for keep in (lane >= step, lane < columns - step)
        )

    def smooth_rows(src, dst, dilation, lo, hi):
        near_w, far_w = weights[dilation][0:2], weights[dilation][2:4]
        for start in range(lo, hi, CHUNK):
            size = min(CHUNK, hi - start)
            at = start + pad

            def window(offset):
                return src[pl.ds(at + offset, size)]

            y = TAPS[0] * (window(-2 * dilation) + window(2 * dilation)) + TAPS[1] * (
                window(-dilation) + window(dilation)
            ) + TAPS[2] * window(0)
            z = (
                pltpu.roll(y, dilation, 2) * near_w[0]
                + pltpu.roll(y, columns - dilation, 2) * near_w[1]
                + pltpu.roll(y, 2 * dilation, 2) * far_w[0]
                + pltpu.roll(y, columns - 2 * dilation, 2) * far_w[1]
                + TAPS[2] * y
            )
            if start >= halo and start + size <= halo + local_rows:
                dst[pl.ds(at, size)] = z
            else:
                row = row0 + start + lax.broadcasted_iota(jnp.int32, (size, 1, 1), 0)
                dst[pl.ds(at, size)] = jnp.where((row >= 0) & (row < total_rows), z, 0.0)

    def rows_major(value):
        return jnp.swapaxes(value, 0, 1)

    buf_a[...] = jnp.zeros_like(buf_a)
    above = rows_major(above_ref[...])[local_rows - halo :]
    below = rows_major(below_ref[...])[:halo]
    buf_a[pl.ds(pad, halo)] = jnp.where(flags_ref[2] > 0, above, 0.0)
    buf_a[pl.ds(pad + halo, local_rows)] = rows_major(own_ref[...])
    buf_a[pl.ds(pad + halo + local_rows, halo)] = jnp.where(flags_ref[3] > 0, below, 0.0)
    bufs = (buf_a, buf_b)
    own = pl.ds(pad + halo, local_rows)
    fresh = []
    lo, hi = 0, extent
    for level_idx in range(SCALES):
        dilation = 2**level_idx
        src, dst = bufs[level_idx % 2], bufs[(level_idx + 1) % 2]
        lo, hi = lo + 2 * dilation, hi - 2 * dilation
        smooth_rows(src, dst, dilation, lo, hi)
        plane = jnp.clip(
            duals_ref[level_idx] + SIGMA * rows_major(src[own] - dst[own]), -SPACE_BOUND, SPACE_BOUND
        )
        sn_ref[level_idx] = plane

    buf_a[...] = jnp.zeros_like(buf_a)
    buf_b[...] = jnp.zeros_like(buf_b)
    lo, hi = halo, halo + local_rows
    for count, level_idx in enumerate(reversed(range(SCALES))):
        dilation = 2**level_idx
        src, dst = bufs[count % 2], bufs[(count + 1) % 2]
        plane = rows_major(sn_ref[level_idx])
        src[own] = src[own] - plane
        lo, hi = lo - 2 * dilation, hi + 2 * dilation
        smooth_rows(src, dst, dilation, max(lo, 0), min(hi, extent))
        dst[own] = dst[own] + plane
    top = dst[pl.ds(pad, halo)]
    bot = dst[pl.ds(pad + halo + local_rows, halo)]
    swap = flags_ref[4] > 0
    send_ref[...] = jnp.where(swap, bot, top)
    keep_ref[...] = jnp.where(swap, top, bot)
    mid_ref[...] = rows_major(dst[own])


def starlet(flags, above, own, below, duals, halo, group, groups, carry=(), interpret=False):
    chans, local_rows, columns = own.shape
    block = math.gcd(chans, 8)
    steps = chans // block // groups
    base = group * steps
    extent = 2 * halo + local_rows + 2 * 2**SCALES
    near_spec = pl.BlockSpec((block, local_rows, columns), lambda i: (i, 0, 0))
    own_spec = pl.BlockSpec((block, local_rows, columns), lambda i: (i + base, 0, 0))
    dual_spec = pl.BlockSpec((SCALES, block, local_rows, columns), lambda i: (0, i + base, 0, 0))
    edge_spec = pl.BlockSpec((halo, block, columns), lambda i: (0, i, 0))
    edge_shape = jax.ShapeDtypeStruct((halo, chans // groups, columns), jnp.float32)
    carry_specs = [pl.BlockSpec(memory_space=pl.ANY)] * len(carry)
    return pl.pallas_call(
        starlet_kernel,
        grid=(steps,),
        in_specs=[pl.BlockSpec(memory_space=pltpu.SMEM), near_spec, own_spec, near_spec, dual_spec] + carry_specs,
        out_specs=[dual_spec, edge_spec, own_spec, edge_spec],
        out_shape=[
            jax.ShapeDtypeStruct(duals.shape, jnp.float32),
            edge_shape,
            jax.ShapeDtypeStruct(own.shape, jnp.float32),
            edge_shape,
        ],
        scratch_shapes=[pltpu.VMEM((extent, block, columns), jnp.float32)] * 2,
        input_output_aliases={5: 0, 6: 2} if carry else {},
        interpret=interpret,
    )(flags, above, own, below, duals, *carry)


def spatial(image_cube, space_duals):
    chans, local_rows, columns = image_cube.shape
    halo = 2 ** (SCALES + 1) - 2
    assert local_rows >= halo
    count = lax.axis_size("rows")
    index = lax.axis_index("rows")
    down = [(i, i + 1) for i in range(count - 1)]
    up = [(i + 1, i) for i in range(count - 1)]
    paired = count == 2
    flags = jnp.stack(
        [index * local_rows, count * local_rows, index > 0, index < count - 1, paired & (index == 0)]
    ).astype(jnp.int32)
    block = math.gcd(chans, 8)
    groups = math.gcd(chans // block, GROUPS)
    width = chans // groups
    carry = ()
    sends, keeps = [], []
    for group in range(groups):
        part = image_cube[group * width : (group + 1) * width]
        if paired:
            above = below = lax.ppermute(part, "rows", down + up)
        else:
            above = lax.ppermute(part, "rows", down)
            below = lax.ppermute(part, "rows", up)
        space_next, send, mid, keep = starlet(flags, above, image_cube, below, space_duals, halo, group, groups, carry)
        carry = (space_next, mid)
        if paired:
            sends.append(lax.ppermute(send, "rows", down + up))
        else:
            sends.append(lax.ppermute(send, "rows", up))
            keeps.append(lax.ppermute(keep, "rows", down))
    got = jnp.concatenate(sends, axis=1)
    gap = local_rows - halo
    if paired:
        spill = jnp.where(
            index == 0,
            jnp.pad(got, ((gap, 0), (0, 0), (0, 0))),
            jnp.pad(got, ((0, gap), (0, 0), (0, 0))),
        )
    else:
        spill = jnp.pad(jnp.concatenate(keeps, axis=1), ((0, gap), (0, 0), (0, 0))) + jnp.pad(
            got, ((gap, 0), (0, 0), (0, 0))
        )
    return mid + jnp.transpose(spill, (1, 0, 2)), space_next


def local(image_cube, data_grad, space_duals, freq_duals):
    chans, local_rows, columns = image_cube.shape
    peers = lax.axis_size("freq")
    share = local_rows * columns // peers
    pieces = image_cube.reshape(chans, peers, share)
    pixel_cube = lax.all_to_all(pieces, "freq", split_axis=1, concat_axis=0, tiled=True).reshape(
        chans * peers, share
    )
    table, freq_next = spectral(pixel_cube, freq_duals)
    space_term, space_next = spatial(image_cube, space_duals)
    spectral_sum = spectral_back(table, freq_next)
    returned = lax.all_to_all(
        spectral_sum.reshape(peers, chans, share),
        "freq",
        split_axis=0,
        concat_axis=2,
        tiled=True,
    )
    spectral_term = returned.reshape(chans, local_rows, columns)
    image_next = jnp.maximum(image_cube - TAU_STEP * (data_grad + space_term + spectral_term), 0.0)
    return (image_next, space_next, freq_next)


def solution(mesh):
    in_specs = (
        P("freq", "rows", None),
        P("freq", "rows", None),
        P(None, "freq", "rows", None),
        P(("rows", "freq"), None),
    )
    out_specs = (P("freq", "rows", None), P(None, "freq", "rows", None), P(("rows", "freq"), None))
    return jax.shard_map(local, mesh=mesh, in_specs=in_specs, out_specs=out_specs, check_vma=False)
```

```python
import math

import jax
import jax.numpy as jnp
from jax import lax
from jax.sharding import PartitionSpec as P
from jax.experimental import pallas as pl
from jax.experimental.pallas import tpu as pltpu

SCALES = 4


TAPS = (0.0625, 0.25, 0.375, 0.25, 0.0625)
SIGMA = 0.5
TAU_STEP = 0.5
SPACE_BOUND = 0.5
FREQ_BOUND = 1.0
CHUNK = 8
GROUPS = 4


def padded_2(cells, sides, width):
    for axis, dim in sides:
        count = lax.axis_size(axis)
        ends = count - 1
        head = lax.slice_in_dim(cells, 0, width, axis=dim)
        tail = lax.slice_in_dim(cells, cells.shape[dim] - width, cells.shape[dim], axis=dim)
        cells = jnp.concatenate(
            [
                lax.ppermute(tail, axis, [(i, (i + 1) % count) for i in range(ends)]),
                cells,
                lax.ppermute(head, axis, [((i + 1) % count, i) for i in range(ends)]),
            ],
            axis=dim,
        )
    return cells


def blur_rows(padded, dilation, out_rows):
    running = TAPS[0] * padded[:, 0:out_rows, :]
    for tap_idx in range(1, 5):
        offset = tap_idx * dilation
        running = running + TAPS[tap_idx] * padded[:, offset : offset + out_rows, :]
    return running


def blur_cols(planar, dilation):
    columns = planar.shape[2]
    reach_cols = 2 * dilation
    padded = jnp.pad(planar, ((0, 0), (0, 0), (reach_cols, reach_cols)))
    running = TAPS[0] * padded[:, :, 0:columns]
    for tap_idx in range(1, 5):
        offset = tap_idx * dilation
        running = running + TAPS[tap_idx] * padded[:, :, offset : offset + columns]
    return running


def inside_rows(margin, local_rows):
    first_row = lax.axis_index("rows") * local_rows - margin
    positions = first_row + jnp.arange(local_rows + 2 * margin, dtype=jnp.int32)
    limit = local_rows * lax.axis_size("rows")
    return ((positions >= 0) & (positions < limit)).astype(jnp.float32)[None, :, None]


def analyse(image_cube):
    local_rows = image_cube.shape[1]
    details = []
    depth = 2 ** (SCALES + 1) - 2
    current = padded_2(image_cube, (("rows", 1),), depth)
    inside = inside_rows(depth, local_rows)
    margin = depth
    for level_idx in range(SCALES):
        dilation = 2**level_idx
        reach_rows = 2 * dilation
        new_margin = margin - reach_rows
        out_rows = local_rows + 2 * new_margin
        start_row = depth - new_margin
        smoothed = blur_cols(blur_rows(current, dilation, out_rows), dilation)
        smoothed = smoothed * inside[:, start_row : start_row + out_rows, :]
        kept = current[:, reach_rows : reach_rows + out_rows, :] - smoothed
        details.append(kept[:, new_margin : new_margin + local_rows, :])
        current = smoothed
        margin = new_margin
    return details


def synthesise(space_next):
    local_rows = space_next.shape[2]
    running = jnp.zeros_like(space_next[0])
    for level_idx in reversed(range(SCALES)):
        dilation = 2**level_idx
        operand = running - space_next[level_idx]
        padded = padded_2(operand, (("rows", 1),), 2 * dilation)
        running = (
            blur_cols(blur_rows(padded, dilation, local_rows), dilation) + space_next[level_idx]
        )
    return running


def dct_table(length):
    split = 64 if length % 64 == 0 else 1
    groups = length // split
    period = 4 * length
    coef_idx = jnp.arange(length, dtype=jnp.int32)
    scale = math.pi / (2 * length)
    outer_phase = (coef_idx[:, None] * (2 * split * jnp.arange(groups, dtype=jnp.int32))[None, :]) % period
    inner_phase = (coef_idx[:, None] * (2 * jnp.arange(split, dtype=jnp.int32) + 1)[None, :]) % period
    outer_angle = outer_phase.astype(jnp.float32) * scale
    inner_angle = inner_phase.astype(jnp.float32) * scale
    weights = jnp.where(
        coef_idx == 0, math.sqrt(1.0 / length), math.sqrt(2.0 / length)
    ).astype(jnp.float32)[:, None, None]
    table = (
        jnp.cos(outer_angle)[:, :, None] * jnp.cos(inner_angle)[:, None, :]
        - jnp.sin(outer_angle)[:, :, None] * jnp.sin(inner_angle)[:, None, :]
    ) * weights
    return table.reshape(length, length)


def spectral(pixel_cube, freq_duals):
    chans_all, pixel_count = pixel_cube.shape
    precision = lax.Precision.HIGH
    table = dct_table(chans_all)
    coeffs = lax.dot_general(
        pixel_cube,
        table,
        (((0,), (1,)), ((), ())),
        precision=precision,
        preferred_element_type=jnp.float32,
    )
    freq_next = jnp.clip(freq_duals + SIGMA * coeffs, -FREQ_BOUND, FREQ_BOUND)
    return table, freq_next


def spectral_back(table, freq_next):
    precision = lax.Precision.HIGH
    return lax.dot_general(
        table,
        freq_next,
        (((0,), (1,)), ((), ())),
        precision=precision,
        preferred_element_type=jnp.float32,
    )


def starlet_kernel(flags_ref, above_ref, own_ref, below_ref, duals_ref, *refs):
    sn_ref, send_ref, mid_ref, keep_ref, buf_a, buf_b = refs[-6:]
    block, local_rows, columns = own_ref.shape
    halo = send_ref.shape[0]
    extent = 2 * halo + local_rows
    pad = 2 ** SCALES
    row0 = flags_ref[0] - halo
    total_rows = flags_ref[1]
    lane = lax.broadcasted_iota(jnp.int32, (1, block, columns), 2)
    weights = {}
    for level_idx in range(SCALES):
        dilation = 2**level_idx
        weights[dilation] = tuple(
            jnp.where(keep, tap, 0.0).astype(jnp.float32)
            for step, tap in ((dilation, TAPS[1]), (2 * dilation, TAPS[0]))
            for keep in (lane >= step, lane < columns - step)
        )

    def smooth_rows(src, dst, dilation, lo, hi):
        near_w, far_w = weights[dilation][0:2], weights[dilation][2:4]
        for start in range(lo, hi, CHUNK):
            size = min(CHUNK, hi - start)
            at = start + pad

            def window(offset):
                return src[pl.ds(at + offset, size)]

            y = TAPS[0] * (window(-2 * dilation) + window(2 * dilation)) + TAPS[1] * (
                window(-dilation) + window(dilation)
            ) + TAPS[2] * window(0)
            z = (
                pltpu.roll(y, dilation, 2) * near_w[0]
                + pltpu.roll(y, columns - dilation, 2) * near_w[1]
                + pltpu.roll(y, 2 * dilation, 2) * far_w[0]
                + pltpu.roll(y, columns - 2 * dilation, 2) * far_w[1]
                + TAPS[2] * y
            )
            if start >= halo and start + size <= halo + local_rows:
                dst[pl.ds(at, size)] = z
            else:
                row = row0 + start + lax.broadcasted_iota(jnp.int32, (size, 1, 1), 0)
                dst[pl.ds(at, size)] = jnp.where((row >= 0) & (row < total_rows), z, 0.0)

    def rows_major(value):
        return jnp.swapaxes(value, 0, 1)

    buf_a[...] = jnp.zeros_like(buf_a)
    above = rows_major(above_ref[...])[local_rows - halo :]
    below = rows_major(below_ref[...])[:halo]
    buf_a[pl.ds(pad, halo)] = jnp.where(flags_ref[2] > 0, above, 0.0)
    buf_a[pl.ds(pad + halo, local_rows)] = rows_major(own_ref[...])
    buf_a[pl.ds(pad + halo + local_rows, halo)] = jnp.where(flags_ref[3] > 0, below, 0.0)
    bufs = (buf_a, buf_b)
    own = pl.ds(pad + halo, local_rows)
    fresh = []
    lo, hi = 0, extent
    for level_idx in range(SCALES):
        dilation = 2**level_idx
        src, dst = bufs[level_idx % 2], bufs[(level_idx + 1) % 2]
        lo, hi = lo + 2 * dilation, hi - 2 * dilation
        smooth_rows(src, dst, dilation, lo, hi)
        plane = jnp.clip(
            duals_ref[level_idx] + SIGMA * rows_major(src[own] - dst[own]), -SPACE_BOUND, SPACE_BOUND
        )
        sn_ref[level_idx] = plane

    buf_a[...] = jnp.zeros_like(buf_a)
    buf_b[...] = jnp.zeros_like(buf_b)
    lo, hi = halo, halo + local_rows
    for count, level_idx in enumerate(reversed(range(SCALES))):
        dilation = 2**level_idx
        src, dst = bufs[count % 2], bufs[(count + 1) % 2]
        plane = rows_major(sn_ref[level_idx])
        src[own] = src[own] - plane
        lo, hi = lo - 2 * dilation, hi + 2 * dilation
        smooth_rows(src, dst, dilation, max(lo, 0), min(hi, extent))
        dst[own] = dst[own] + plane
    top = dst[pl.ds(pad, halo)]
    bot = dst[pl.ds(pad + halo + local_rows, halo)]
    swap = flags_ref[4] > 0
    send_ref[...] = jnp.where(swap, bot, top)
    keep_ref[...] = jnp.where(swap, top, bot)
    mid_ref[...] = rows_major(dst[own])


def starlet(flags, above, own, below, duals, halo, group, groups, carry=(), interpret=False):
    chans, local_rows, columns = own.shape
    block = math.gcd(chans, 8)
    steps = chans // block // groups
    base = group * steps
    extent = 2 * halo + local_rows + 2 * 2**SCALES
    near_spec = pl.BlockSpec((block, local_rows, columns), lambda i: (i, 0, 0))
    own_spec = pl.BlockSpec((block, local_rows, columns), lambda i: (i + base, 0, 0))
    dual_spec = pl.BlockSpec((SCALES, block, local_rows, columns), lambda i: (0, i + base, 0, 0))
    edge_spec = pl.BlockSpec((halo, block, columns), lambda i: (0, i, 0))
    edge_shape = jax.ShapeDtypeStruct((halo, chans // groups, columns), jnp.float32)
    carry_specs = [pl.BlockSpec(memory_space=pl.ANY)] * len(carry)
    return pl.pallas_call(
        starlet_kernel,
        grid=(steps,),
        in_specs=[pl.BlockSpec(memory_space=pltpu.SMEM), near_spec, own_spec, near_spec, dual_spec] + carry_specs,
        out_specs=[dual_spec, edge_spec, own_spec, edge_spec],
        out_shape=[
            jax.ShapeDtypeStruct(duals.shape, jnp.float32),
            edge_shape,
            jax.ShapeDtypeStruct(own.shape, jnp.float32),
            edge_shape,
        ],
        scratch_shapes=[pltpu.VMEM((extent, block, columns), jnp.float32)] * 2,
        input_output_aliases={5: 0, 6: 2} if carry else {},
        interpret=interpret,
    )(flags, above, own, below, duals, *carry)


def spatial(image_cube, space_duals):
    chans, local_rows, columns = image_cube.shape
    halo = 2 ** (SCALES + 1) - 2
    assert local_rows >= halo
    count = lax.axis_size("rows")
    index = lax.axis_index("rows")
    down = [(i, i + 1) for i in range(count - 1)]
    up = [(i + 1, i) for i in range(count - 1)]
    paired = count == 2
    flags = jnp.stack(
        [index * local_rows, count * local_rows, index > 0, index < count - 1, paired & (index == 0)]
    ).astype(jnp.int32)
    block = math.gcd(chans, 8)
    groups = math.gcd(chans // block, GROUPS)
    width = chans // groups
    carry = ()
    sends, keeps = [], []
    for group in range(groups):
        part = image_cube[group * width : (group + 1) * width]
        if paired:
            above = below = lax.ppermute(part, "rows", down + up)
        else:
            above = lax.ppermute(part, "rows", down)
            below = lax.ppermute(part, "rows", up)
        space_next, send, mid, keep = starlet(flags, above, image_cube, below, space_duals, halo, group, groups, carry)
        carry = (space_next, mid)
        if paired:
            sends.append(lax.ppermute(send, "rows", down + up))
        else:
            sends.append(lax.ppermute(send, "rows", up))
            keeps.append(lax.ppermute(keep, "rows", down))
    got = jnp.concatenate(sends, axis=1)
    gap = local_rows - halo
    if paired:
        spill = jnp.where(
            index == 0,
            jnp.pad(got, ((gap, 0), (0, 0), (0, 0))),
            jnp.pad(got, ((0, gap), (0, 0), (0, 0))),
        )
    else:
        spill = jnp.pad(jnp.concatenate(keeps, axis=1), ((0, gap), (0, 0), (0, 0))) + jnp.pad(
            got, ((gap, 0), (0, 0), (0, 0))
        )
    return mid + jnp.transpose(spill, (1, 0, 2)), space_next


def local(image_cube, data_grad, space_duals, freq_duals):
    chans, local_rows, columns = image_cube.shape
    peers = lax.axis_size("freq")
    share = local_rows * columns // peers
    pieces = image_cube.reshape(chans, peers, share)
    pixel_cube = lax.all_to_all(pieces, "freq", split_axis=1, concat_axis=0, tiled=True).reshape(
        chans * peers, share
    )
    space_term, space_next = spatial(image_cube, space_duals)
    pixel_cube, space_term, space_next = lax.optimization_barrier((pixel_cube, space_term, space_next))
    table, freq_next = spectral(pixel_cube, freq_duals)
    spectral_sum = spectral_back(table, freq_next)
    returned = lax.all_to_all(
        spectral_sum.reshape(peers, chans, share),
        "freq",
        split_axis=0,
        concat_axis=2,
        tiled=True,
    )
    spectral_term = returned.reshape(chans, local_rows, columns)
    image_next = jnp.maximum(image_cube - TAU_STEP * (data_grad + space_term + spectral_term), 0.0)
    return (image_next, space_next, freq_next)


def solution(mesh):
    in_specs = (
        P("freq", "rows", None),
        P("freq", "rows", None),
        P(None, "freq", "rows", None),
        P(("rows", "freq"), None),
    )
    out_specs = (P("freq", "rows", None), P(None, "freq", "rows", None), P(("rows", "freq"), None))
    return jax.shard_map(local, mesh=mesh, in_specs=in_specs, out_specs=out_specs, check_vma=False)
```

```python
import math

import jax
import jax.numpy as jnp
from jax import lax
from jax.sharding import PartitionSpec as P
from jax.experimental import pallas as pl
from jax.experimental.pallas import tpu as pltpu

SCALES = 4


TAPS = (0.0625, 0.25, 0.375, 0.25, 0.0625)
SIGMA = 0.5
TAU_STEP = 0.5
SPACE_BOUND = 0.5
FREQ_BOUND = 1.0
CHUNK = 8
GROUPS = 4


def padded_2(cells, sides, width):
    for axis, dim in sides:
        count = lax.axis_size(axis)
        ends = count - 1
        head = lax.slice_in_dim(cells, 0, width, axis=dim)
        tail = lax.slice_in_dim(cells, cells.shape[dim] - width, cells.shape[dim], axis=dim)
        cells = jnp.concatenate(
            [
                lax.ppermute(tail, axis, [(i, (i + 1) % count) for i in range(ends)]),
                cells,
                lax.ppermute(head, axis, [((i + 1) % count, i) for i in range(ends)]),
            ],
            axis=dim,
        )
    return cells


def blur_rows(padded, dilation, out_rows):
    running = TAPS[0] * padded[:, 0:out_rows, :]
    for tap_idx in range(1, 5):
        offset = tap_idx * dilation
        running = running + TAPS[tap_idx] * padded[:, offset : offset + out_rows, :]
    return running


def blur_cols(planar, dilation):
    columns = planar.shape[2]
    reach_cols = 2 * dilation
    padded = jnp.pad(planar, ((0, 0), (0, 0), (reach_cols, reach_cols)))
    running = TAPS[0] * padded[:, :, 0:columns]
    for tap_idx in range(1, 5):
        offset = tap_idx * dilation
        running = running + TAPS[tap_idx] * padded[:, :, offset : offset + columns]
    return running


def inside_rows(margin, local_rows):
    first_row = lax.axis_index("rows") * local_rows - margin
    positions = first_row + jnp.arange(local_rows + 2 * margin, dtype=jnp.int32)
    limit = local_rows * lax.axis_size("rows")
    return ((positions >= 0) & (positions < limit)).astype(jnp.float32)[None, :, None]


def analyse(image_cube):
    local_rows = image_cube.shape[1]
    details = []
    depth = 2 ** (SCALES + 1) - 2
    current = padded_2(image_cube, (("rows", 1),), depth)
    inside = inside_rows(depth, local_rows)
    margin = depth
    for level_idx in range(SCALES):
        dilation = 2**level_idx
        reach_rows = 2 * dilation
        new_margin = margin - reach_rows
        out_rows = local_rows + 2 * new_margin
        start_row = depth - new_margin
        smoothed = blur_cols(blur_rows(current, dilation, out_rows), dilation)
        smoothed = smoothed * inside[:, start_row : start_row + out_rows, :]
        kept = current[:, reach_rows : reach_rows + out_rows, :] - smoothed
        details.append(kept[:, new_margin : new_margin + local_rows, :])
        current = smoothed
        margin = new_margin
    return details


def synthesise(space_next):
    local_rows = space_next.shape[2]
    running = jnp.zeros_like(space_next[0])
    for level_idx in reversed(range(SCALES)):
        dilation = 2**level_idx
        operand = running - space_next[level_idx]
        padded = padded_2(operand, (("rows", 1),), 2 * dilation)
        running = (
            blur_cols(blur_rows(padded, dilation, local_rows), dilation) + space_next[level_idx]
        )
    return running


def dct_table(length):
    split = 64 if length % 64 == 0 else 1
    groups = length // split
    period = 4 * length
    coef_idx = jnp.arange(length, dtype=jnp.int32)
    scale = math.pi / (2 * length)
    outer_phase = (coef_idx[:, None] * (2 * split * jnp.arange(groups, dtype=jnp.int32))[None, :]) % period
    inner_phase = (coef_idx[:, None] * (2 * jnp.arange(split, dtype=jnp.int32) + 1)[None, :]) % period
    outer_angle = outer_phase.astype(jnp.float32) * scale
    inner_angle = inner_phase.astype(jnp.float32) * scale
    weights = jnp.where(
        coef_idx == 0, math.sqrt(1.0 / length), math.sqrt(2.0 / length)
    ).astype(jnp.float32)[:, None, None]
    table = (
        jnp.cos(outer_angle)[:, :, None] * jnp.cos(inner_angle)[:, None, :]
        - jnp.sin(outer_angle)[:, :, None] * jnp.sin(inner_angle)[:, None, :]
    ) * weights
    return table.reshape(length, length)


def spectral(pixel_cube, freq_duals):
    chans_all, pixel_count = pixel_cube.shape
    precision = lax.Precision.HIGH
    table = dct_table(chans_all)
    coeffs = lax.dot_general(
        pixel_cube,
        table,
        (((0,), (1,)), ((), ())),
        precision=precision,
        preferred_element_type=jnp.float32,
    )
    freq_next = jnp.clip(freq_duals + SIGMA * coeffs, -FREQ_BOUND, FREQ_BOUND)
    return table, freq_next


def spectral_back(table, freq_next):
    precision = lax.Precision.HIGH
    return lax.dot_general(
        table,
        freq_next,
        (((0,), (1,)), ((), ())),
        precision=precision,
        preferred_element_type=jnp.float32,
    )


def starlet_kernel(flags_ref, above_ref, own_ref, below_ref, duals_ref, *refs):
    sn_ref, send_ref, mid_ref, keep_ref, buf_a, buf_b = refs[-6:]
    block, local_rows, columns = own_ref.shape
    halo = send_ref.shape[0]
    extent = 2 * halo + local_rows
    pad = 2 ** SCALES
    row0 = flags_ref[0] - halo
    total_rows = flags_ref[1]
    lane = lax.broadcasted_iota(jnp.int32, (1, block, columns), 2)
    weights = {}
    for level_idx in range(SCALES):
        dilation = 2**level_idx
        weights[dilation] = tuple(
            jnp.where(keep, tap, 0.0).astype(jnp.float32)
            for step, tap in ((dilation, TAPS[1]), (2 * dilation, TAPS[0]))
            for keep in (lane >= step, lane < columns - step)
        )

    def smooth_rows(src, dst, dilation, lo, hi):
        near_w, far_w = weights[dilation][0:2], weights[dilation][2:4]
        for start in range(lo, hi, CHUNK):
            size = min(CHUNK, hi - start)
            at = start + pad

            def window(offset):
                return src[pl.ds(at + offset, size)]

            y = TAPS[0] * (window(-2 * dilation) + window(2 * dilation)) + TAPS[1] * (
                window(-dilation) + window(dilation)
            ) + TAPS[2] * window(0)
            z = (
                pltpu.roll(y, dilation, 2) * near_w[0]
                + pltpu.roll(y, columns - dilation, 2) * near_w[1]
                + pltpu.roll(y, 2 * dilation, 2) * far_w[0]
                + pltpu.roll(y, columns - 2 * dilation, 2) * far_w[1]
                + TAPS[2] * y
            )
            if start >= halo and start + size <= halo + local_rows:
                dst[pl.ds(at, size)] = z
            else:
                row = row0 + start + lax.broadcasted_iota(jnp.int32, (size, 1, 1), 0)
                dst[pl.ds(at, size)] = jnp.where((row >= 0) & (row < total_rows), z, 0.0)

    def rows_major(value):
        return jnp.swapaxes(value, 0, 1)

    buf_a[...] = jnp.zeros_like(buf_a)
    above = rows_major(above_ref[...])[local_rows - halo :]
    below = rows_major(below_ref[...])[:halo]
    buf_a[pl.ds(pad, halo)] = jnp.where(flags_ref[2] > 0, above, 0.0)
    buf_a[pl.ds(pad + halo, local_rows)] = rows_major(own_ref[...])
    buf_a[pl.ds(pad + halo + local_rows, halo)] = jnp.where(flags_ref[3] > 0, below, 0.0)
    bufs = (buf_a, buf_b)
    own = pl.ds(pad + halo, local_rows)
    fresh = []
    lo, hi = 0, extent
    for level_idx in range(SCALES):
        dilation = 2**level_idx
        src, dst = bufs[level_idx % 2], bufs[(level_idx + 1) % 2]
        lo, hi = lo + 2 * dilation, hi - 2 * dilation
        smooth_rows(src, dst, dilation, lo, hi)
        plane = jnp.clip(
            duals_ref[level_idx] + SIGMA * rows_major(src[own] - dst[own]), -SPACE_BOUND, SPACE_BOUND
        )
        sn_ref[level_idx] = plane

    buf_a[...] = jnp.zeros_like(buf_a)
    buf_b[...] = jnp.zeros_like(buf_b)
    lo, hi = halo, halo + local_rows
    for count, level_idx in enumerate(reversed(range(SCALES))):
        dilation = 2**level_idx
        src, dst = bufs[count % 2], bufs[(count + 1) % 2]
        plane = rows_major(sn_ref[level_idx])
        src[own] = src[own] - plane
        lo, hi = lo - 2 * dilation, hi + 2 * dilation
        smooth_rows(src, dst, dilation, max(lo, 0), min(hi, extent))
        dst[own] = dst[own] + plane
    top = dst[pl.ds(pad, halo)]
    bot = dst[pl.ds(pad + halo + local_rows, halo)]
    swap = flags_ref[4] > 0
    send_ref[...] = jnp.where(swap, bot, top)
    keep_ref[...] = jnp.where(swap, top, bot)
    mid_ref[...] = rows_major(dst[own])


def starlet(flags, above, own, below, duals, halo, group, groups, carry=(), interpret=False):
    chans, local_rows, columns = own.shape
    block = math.gcd(chans, 8)
    steps = chans // block // groups
    base = group * steps
    extent = 2 * halo + local_rows + 2 * 2**SCALES
    near_spec = pl.BlockSpec((block, local_rows, columns), lambda i: (i, 0, 0))
    own_spec = pl.BlockSpec((block, local_rows, columns), lambda i: (i + base, 0, 0))
    dual_spec = pl.BlockSpec((SCALES, block, local_rows, columns), lambda i: (0, i + base, 0, 0))
    edge_spec = pl.BlockSpec((halo, block, columns), lambda i: (0, i, 0))
    edge_shape = jax.ShapeDtypeStruct((halo, chans // groups, columns), jnp.float32)
    carry_specs = [pl.BlockSpec(memory_space=pl.ANY)] * len(carry)
    return pl.pallas_call(
        starlet_kernel,
        grid=(steps,),
        in_specs=[pl.BlockSpec(memory_space=pltpu.SMEM), near_spec, own_spec, near_spec, dual_spec] + carry_specs,
        out_specs=[dual_spec, edge_spec, own_spec, edge_spec],
        out_shape=[
            jax.ShapeDtypeStruct(duals.shape, jnp.float32),
            edge_shape,
            jax.ShapeDtypeStruct(own.shape, jnp.float32),
            edge_shape,
        ],
        scratch_shapes=[pltpu.VMEM((extent, block, columns), jnp.float32)] * 2,
        input_output_aliases={5: 0, 6: 2} if carry else {},
        interpret=interpret,
    )(flags, above, own, below, duals, *carry)


def row_plan(chans, local_rows):
    halo = 2 ** (SCALES + 1) - 2
    assert local_rows >= halo
    block = math.gcd(chans, 8)
    groups = math.gcd(chans // block, GROUPS)
    return halo, groups, chans // groups


def exchange_halos(image_cube):
    chans, local_rows, columns = image_cube.shape
    halo, groups, width = row_plan(chans, local_rows)
    count = lax.axis_size("rows")
    down = [(i, i + 1) for i in range(count - 1)]
    up = [(i + 1, i) for i in range(count - 1)]
    halos = []
    for group in range(groups):
        part = image_cube[group * width : (group + 1) * width]
        if count == 2:
            got = lax.ppermute(part, "rows", down + up)
            halos.append((got, got))
        else:
            halos.append((lax.ppermute(part, "rows", down), lax.ppermute(part, "rows", up)))
    return halos


def spatial(halos, image_cube, space_duals):
    chans, local_rows, columns = image_cube.shape
    halo, groups, width = row_plan(chans, local_rows)
    count = lax.axis_size("rows")
    index = lax.axis_index("rows")
    down = [(i, i + 1) for i in range(count - 1)]
    up = [(i + 1, i) for i in range(count - 1)]
    paired = count == 2
    flags = jnp.stack(
        [index * local_rows, count * local_rows, index > 0, index < count - 1, paired & (index == 0)]
    ).astype(jnp.int32)
    carry = ()
    sends, keeps = [], []
    for group, (above, below) in enumerate(halos):
        space_next, send, mid, keep = starlet(flags, above, image_cube, below, space_duals, halo, group, groups, carry)
        carry = (space_next, mid)
        if paired:
            sends.append(lax.ppermute(send, "rows", down + up))
        else:
            sends.append(lax.ppermute(send, "rows", up))
            keeps.append(lax.ppermute(keep, "rows", down))
    got = jnp.concatenate(sends, axis=1)
    gap = local_rows - halo
    if paired:
        spill = jnp.where(
            index == 0,
            jnp.pad(got, ((gap, 0), (0, 0), (0, 0))),
            jnp.pad(got, ((0, gap), (0, 0), (0, 0))),
        )
    else:
        spill = jnp.pad(jnp.concatenate(keeps, axis=1), ((0, gap), (0, 0), (0, 0))) + jnp.pad(
            got, ((gap, 0), (0, 0), (0, 0))
        )
    return mid + jnp.transpose(spill, (1, 0, 2)), space_next


def local(image_cube, data_grad, space_duals, freq_duals):
    chans, local_rows, columns = image_cube.shape
    peers = lax.axis_size("freq")
    share = local_rows * columns // peers
    pieces = image_cube.reshape(chans, peers, share)
    halos = exchange_halos(image_cube)
    pixel_cube = lax.all_to_all(pieces, "freq", split_axis=1, concat_axis=0, tiled=True).reshape(
        chans * peers, share
    )
    pixel_cube, halos = lax.optimization_barrier((pixel_cube, halos))
    table, freq_next = spectral(pixel_cube, freq_duals)
    spectral_sum = spectral_back(table, freq_next)
    spectral_sum, halos = lax.optimization_barrier((spectral_sum, halos))
    returned = lax.all_to_all(
        spectral_sum.reshape(peers, chans, share),
        "freq",
        split_axis=0,
        concat_axis=2,
        tiled=True,
    )
    space_term, space_next = spatial(halos, image_cube, space_duals)
    spectral_term = returned.reshape(chans, local_rows, columns)
    image_next = jnp.maximum(image_cube - TAU_STEP * (data_grad + space_term + spectral_term), 0.0)
    return (image_next, space_next, freq_next)


def solution(mesh):
    in_specs = (
        P("freq", "rows", None),
        P("freq", "rows", None),
        P(None, "freq", "rows", None),
        P(("rows", "freq"), None),
    )
    out_specs = (P("freq", "rows", None), P(None, "freq", "rows", None), P(("rows", "freq"), None))
    return jax.shard_map(local, mesh=mesh, in_specs=in_specs, out_specs=out_specs, check_vma=False)
```

```python
import math

import jax
import jax.numpy as jnp
from jax import lax
from jax.sharding import PartitionSpec as P
from jax.experimental import pallas as pl
from jax.experimental.pallas import tpu as pltpu

SCALES = 4


TAPS = (0.0625, 0.25, 0.375, 0.25, 0.0625)
SIGMA = 0.5
TAU_STEP = 0.5
SPACE_BOUND = 0.5
FREQ_BOUND = 1.0
CHUNK = 8
GROUPS = 4


def padded_2(cells, sides, width):
    for axis, dim in sides:
        count = lax.axis_size(axis)
        ends = count - 1
        head = lax.slice_in_dim(cells, 0, width, axis=dim)
        tail = lax.slice_in_dim(cells, cells.shape[dim] - width, cells.shape[dim], axis=dim)
        cells = jnp.concatenate(
            [
                lax.ppermute(tail, axis, [(i, (i + 1) % count) for i in range(ends)]),
                cells,
                lax.ppermute(head, axis, [((i + 1) % count, i) for i in range(ends)]),
            ],
            axis=dim,
        )
    return cells


def blur_rows(padded, dilation, out_rows):
    running = TAPS[0] * padded[:, 0:out_rows, :]
    for tap_idx in range(1, 5):
        offset = tap_idx * dilation
        running = running + TAPS[tap_idx] * padded[:, offset : offset + out_rows, :]
    return running


def blur_cols(planar, dilation):
    columns = planar.shape[2]
    reach_cols = 2 * dilation
    padded = jnp.pad(planar, ((0, 0), (0, 0), (reach_cols, reach_cols)))
    running = TAPS[0] * padded[:, :, 0:columns]
    for tap_idx in range(1, 5):
        offset = tap_idx * dilation
        running = running + TAPS[tap_idx] * padded[:, :, offset : offset + columns]
    return running


def inside_rows(margin, local_rows):
    first_row = lax.axis_index("rows") * local_rows - margin
    positions = first_row + jnp.arange(local_rows + 2 * margin, dtype=jnp.int32)
    limit = local_rows * lax.axis_size("rows")
    return ((positions >= 0) & (positions < limit)).astype(jnp.float32)[None, :, None]


def analyse(image_cube):
    local_rows = image_cube.shape[1]
    details = []
    depth = 2 ** (SCALES + 1) - 2
    current = padded_2(image_cube, (("rows", 1),), depth)
    inside = inside_rows(depth, local_rows)
    margin = depth
    for level_idx in range(SCALES):
        dilation = 2**level_idx
        reach_rows = 2 * dilation
        new_margin = margin - reach_rows
        out_rows = local_rows + 2 * new_margin
        start_row = depth - new_margin
        smoothed = blur_cols(blur_rows(current, dilation, out_rows), dilation)
        smoothed = smoothed * inside[:, start_row : start_row + out_rows, :]
        kept = current[:, reach_rows : reach_rows + out_rows, :] - smoothed
        details.append(kept[:, new_margin : new_margin + local_rows, :])
        current = smoothed
        margin = new_margin
    return details


def synthesise(space_next):
    local_rows = space_next.shape[2]
    running = jnp.zeros_like(space_next[0])
    for level_idx in reversed(range(SCALES)):
        dilation = 2**level_idx
        operand = running - space_next[level_idx]
        padded = padded_2(operand, (("rows", 1),), 2 * dilation)
        running = (
            blur_cols(blur_rows(padded, dilation, local_rows), dilation) + space_next[level_idx]
        )
    return running


def dct_table(length, parity=None):
    half = length if parity is None else length // 2
    split = 64 if half % 64 == 0 else 1
    groups = half // split
    period = 4 * length
    if parity is None:
        coef_idx = jnp.arange(length, dtype=jnp.int32)
    else:
        coef_idx = 2 * jnp.arange(half, dtype=jnp.int32) + parity
    scale = math.pi / (2 * length)
    outer_phase = (coef_idx[:, None] * (2 * split * jnp.arange(groups, dtype=jnp.int32))[None, :]) % period
    inner_phase = (coef_idx[:, None] * (2 * jnp.arange(split, dtype=jnp.int32) + 1)[None, :]) % period
    outer_angle = outer_phase.astype(jnp.float32) * scale
    inner_angle = inner_phase.astype(jnp.float32) * scale
    weights = jnp.where(
        coef_idx == 0, math.sqrt(1.0 / length), math.sqrt(2.0 / length)
    ).astype(jnp.float32)[:, None, None]
    table = (
        jnp.cos(outer_angle)[:, :, None] * jnp.cos(inner_angle)[:, None, :]
        - jnp.sin(outer_angle)[:, :, None] * jnp.sin(inner_angle)[:, None, :]
    ) * weights
    return table.reshape(coef_idx.shape[0], half)


def forward_dot(samples, table):
    return lax.dot_general(
        samples,
        table,
        (((0,), (1,)), ((), ())),
        precision=lax.Precision.HIGH,
        preferred_element_type=jnp.float32,
    )


def spectral(pixel_cube, freq_duals):
    chans_all, pixel_count = pixel_cube.shape
    if chans_all % 2:
        table = dct_table(chans_all)
        coeffs = forward_dot(pixel_cube, table)
        freq_next = jnp.clip(freq_duals + SIGMA * coeffs, -FREQ_BOUND, FREQ_BOUND)
        return (table,), freq_next, (freq_next,)
    half = chans_all // 2
    head = pixel_cube[:half]
    tail = pixel_cube[half:][::-1]
    tables = (dct_table(chans_all, 0), dct_table(chans_all, 1))
    pairs = freq_duals.reshape(pixel_count, half, 2)
    fresh = tuple(
        jnp.clip(pairs[:, :, parity] + SIGMA * forward_dot(samples, tables[parity]), -FREQ_BOUND, FREQ_BOUND)
        for parity, samples in ((0, head + tail), (1, head - tail))
    )
    freq_next = jnp.stack(fresh, axis=2).reshape(pixel_count, chans_all)
    return tables, freq_next, fresh


def spectral_back(tables, fresh):
    parts = [
        lax.dot_general(
            table,
            values,
            (((0,), (1,)), ((), ())),
            precision=lax.Precision.HIGH,
            preferred_element_type=jnp.float32,
        )
        for table, values in zip(tables, fresh)
    ]
    if len(parts) == 1:
        return parts[0]
    return jnp.concatenate([parts[0] + parts[1], (parts[0] - parts[1])[::-1]], axis=0)


def starlet_kernel(flags_ref, above_ref, own_ref, below_ref, duals_ref, *refs):
    sn_ref, send_ref, mid_ref, keep_ref, buf_a, buf_b = refs[-6:]
    block, local_rows, columns = own_ref.shape
    halo = send_ref.shape[0]
    extent = 2 * halo + local_rows
    pad = 2 ** SCALES
    row0 = flags_ref[0] - halo
    total_rows = flags_ref[1]
    lane = lax.broadcasted_iota(jnp.int32, (1, block, columns), 2)
    weights = {}
    for level_idx in range(SCALES):
        dilation = 2**level_idx
        weights[dilation] = tuple(
            jnp.where(keep, tap, 0.0).astype(jnp.float32)
            for step, tap in ((dilation, TAPS[1]), (2 * dilation, TAPS[0]))
            for keep in (lane >= step, lane < columns - step)
        )

    def smooth_rows(src, dst, dilation, lo, hi):
        near_w, far_w = weights[dilation][0:2], weights[dilation][2:4]
        for start in range(lo, hi, CHUNK):
            size = min(CHUNK, hi - start)
            at = start + pad

            def window(offset):
                return src[pl.ds(at + offset, size)]

            y = TAPS[0] * (window(-2 * dilation) + window(2 * dilation)) + TAPS[1] * (
                window(-dilation) + window(dilation)
            ) + TAPS[2] * window(0)
            z = (
                pltpu.roll(y, dilation, 2) * near_w[0]
                + pltpu.roll(y, columns - dilation, 2) * near_w[1]
                + pltpu.roll(y, 2 * dilation, 2) * far_w[0]
                + pltpu.roll(y, columns - 2 * dilation, 2) * far_w[1]
                + TAPS[2] * y
            )
            if start >= halo and start + size <= halo + local_rows:
                dst[pl.ds(at, size)] = z
            else:
                row = row0 + start + lax.broadcasted_iota(jnp.int32, (size, 1, 1), 0)
                dst[pl.ds(at, size)] = jnp.where((row >= 0) & (row < total_rows), z, 0.0)

    def rows_major(value):
        return jnp.swapaxes(value, 0, 1)

    buf_a[...] = jnp.zeros_like(buf_a)
    above = rows_major(above_ref[...])[local_rows - halo :]
    below = rows_major(below_ref[...])[:halo]
    buf_a[pl.ds(pad, halo)] = jnp.where(flags_ref[2] > 0, above, 0.0)
    buf_a[pl.ds(pad + halo, local_rows)] = rows_major(own_ref[...])
    buf_a[pl.ds(pad + halo + local_rows, halo)] = jnp.where(flags_ref[3] > 0, below, 0.0)
    bufs = (buf_a, buf_b)
    own = pl.ds(pad + halo, local_rows)
    fresh = []
    lo, hi = 0, extent
    for level_idx in range(SCALES):
        dilation = 2**level_idx
        src, dst = bufs[level_idx % 2], bufs[(level_idx + 1) % 2]
        lo, hi = lo + 2 * dilation, hi - 2 * dilation
        smooth_rows(src, dst, dilation, lo, hi)
        plane = jnp.clip(
            duals_ref[level_idx] + SIGMA * rows_major(src[own] - dst[own]), -SPACE_BOUND, SPACE_BOUND
        )
        sn_ref[level_idx] = plane

    buf_a[...] = jnp.zeros_like(buf_a)
    buf_b[...] = jnp.zeros_like(buf_b)
    lo, hi = halo, halo + local_rows
    for count, level_idx in enumerate(reversed(range(SCALES))):
        dilation = 2**level_idx
        src, dst = bufs[count % 2], bufs[(count + 1) % 2]
        plane = rows_major(sn_ref[level_idx])
        src[own] = src[own] - plane
        lo, hi = lo - 2 * dilation, hi + 2 * dilation
        smooth_rows(src, dst, dilation, max(lo, 0), min(hi, extent))
        dst[own] = dst[own] + plane
    top = dst[pl.ds(pad, halo)]
    bot = dst[pl.ds(pad + halo + local_rows, halo)]
    swap = flags_ref[4] > 0
    send_ref[...] = jnp.where(swap, bot, top)
    keep_ref[...] = jnp.where(swap, top, bot)
    mid_ref[...] = rows_major(dst[own])


def starlet(flags, above, own, below, duals, halo, group, groups, carry=(), interpret=False):
    chans, local_rows, columns = own.shape
    block = math.gcd(chans, 8)
    steps = chans // block // groups
    base = group * steps
    extent = 2 * halo + local_rows + 2 * 2**SCALES
    near_spec = pl.BlockSpec((block, local_rows, columns), lambda i: (i, 0, 0))
    own_spec = pl.BlockSpec((block, local_rows, columns), lambda i: (i + base, 0, 0))
    dual_spec = pl.BlockSpec((SCALES, block, local_rows, columns), lambda i: (0, i + base, 0, 0))
    edge_spec = pl.BlockSpec((halo, block, columns), lambda i: (0, i, 0))
    edge_shape = jax.ShapeDtypeStruct((halo, chans // groups, columns), jnp.float32)
    carry_specs = [pl.BlockSpec(memory_space=pl.ANY)] * len(carry)
    return pl.pallas_call(
        starlet_kernel,
        grid=(steps,),
        in_specs=[pl.BlockSpec(memory_space=pltpu.SMEM), near_spec, own_spec, near_spec, dual_spec] + carry_specs,
        out_specs=[dual_spec, edge_spec, own_spec, edge_spec],
        out_shape=[
            jax.ShapeDtypeStruct(duals.shape, jnp.float32),
            edge_shape,
            jax.ShapeDtypeStruct(own.shape, jnp.float32),
            edge_shape,
        ],
        scratch_shapes=[pltpu.VMEM((extent, block, columns), jnp.float32)] * 2,
        input_output_aliases={5: 0, 6: 2} if carry else {},
        interpret=interpret,
    )(flags, above, own, below, duals, *carry)


def row_plan(chans, local_rows):
    halo = 2 ** (SCALES + 1) - 2
    assert local_rows >= halo
    block = math.gcd(chans, 8)
    groups = math.gcd(chans // block, GROUPS)
    return halo, groups, chans // groups


def exchange_halos(image_cube):
    chans, local_rows, columns = image_cube.shape
    halo, groups, width = row_plan(chans, local_rows)
    count = lax.axis_size("rows")
    down = [(i, i + 1) for i in range(count - 1)]
    up = [(i + 1, i) for i in range(count - 1)]
    halos = []
    for group in range(groups):
        part = image_cube[group * width : (group + 1) * width]
        if count == 2:
            got = lax.ppermute(part, "rows", down + up)
            halos.append((got, got))
        else:
            halos.append((lax.ppermute(part, "rows", down), lax.ppermute(part, "rows", up)))
    return halos


def spatial(halos, image_cube, space_duals):
    chans, local_rows, columns = image_cube.shape
    halo, groups, width = row_plan(chans, local_rows)
    count = lax.axis_size("rows")
    index = lax.axis_index("rows")
    down = [(i, i + 1) for i in range(count - 1)]
    up = [(i + 1, i) for i in range(count - 1)]
    paired = count == 2
    flags = jnp.stack(
        [index * local_rows, count * local_rows, index > 0, index < count - 1, paired & (index == 0)]
    ).astype(jnp.int32)
    carry = ()
    sends, keeps = [], []
    for group, (above, below) in enumerate(halos):
        space_next, send, mid, keep = starlet(flags, above, image_cube, below, space_duals, halo, group, groups, carry)
        carry = (space_next, mid)
        if paired:
            sends.append(lax.ppermute(send, "rows", down + up))
        else:
            sends.append(lax.ppermute(send, "rows", up))
            keeps.append(lax.ppermute(keep, "rows", down))
    got = jnp.concatenate(sends, axis=1)
    gap = local_rows - halo
    if paired:
        spill = jnp.where(
            index == 0,
            jnp.pad(got, ((gap, 0), (0, 0), (0, 0))),
            jnp.pad(got, ((0, gap), (0, 0), (0, 0))),
        )
    else:
        spill = jnp.pad(jnp.concatenate(keeps, axis=1), ((0, gap), (0, 0), (0, 0))) + jnp.pad(
            got, ((gap, 0), (0, 0), (0, 0))
        )
    return mid + jnp.transpose(spill, (1, 0, 2)), space_next


def local(image_cube, data_grad, space_duals, freq_duals):
    chans, local_rows, columns = image_cube.shape
    peers = lax.axis_size("freq")
    share = local_rows * columns // peers
    pieces = image_cube.reshape(chans, peers, share)
    halos = exchange_halos(image_cube)
    pixel_cube = lax.all_to_all(pieces, "freq", split_axis=1, concat_axis=0, tiled=True).reshape(
        chans * peers, share
    )
    pixel_cube, halos = lax.optimization_barrier((pixel_cube, halos))
    tables, freq_next, fresh = spectral(pixel_cube, freq_duals)
    spectral_sum = spectral_back(tables, fresh)
    spectral_sum, halos = lax.optimization_barrier((spectral_sum, halos))
    returned = lax.all_to_all(
        spectral_sum.reshape(peers, chans, share),
        "freq",
        split_axis=0,
        concat_axis=2,
        tiled=True,
    )
    space_term, space_next = spatial(halos, image_cube, space_duals)
    spectral_term = returned.reshape(chans, local_rows, columns)
    image_next = jnp.maximum(image_cube - TAU_STEP * (data_grad + space_term + spectral_term), 0.0)
    return (image_next, space_next, freq_next)


def solution(mesh):
    in_specs = (
        P("freq", "rows", None),
        P("freq", "rows", None),
        P(None, "freq", "rows", None),
        P(("rows", "freq"), None),
    )
    out_specs = (P("freq", "rows", None), P(None, "freq", "rows", None), P(("rows", "freq"), None))
    return jax.shard_map(local, mesh=mesh, in_specs=in_specs, out_specs=out_specs, check_vma=False)
```

```python
import math

import jax
import jax.numpy as jnp
from jax import lax
from jax.sharding import PartitionSpec as P
from jax.experimental import pallas as pl
from jax.experimental.pallas import tpu as pltpu

SCALES = 4


TAPS = (0.0625, 0.25, 0.375, 0.25, 0.0625)
SIGMA = 0.5
TAU_STEP = 0.5
SPACE_BOUND = 0.5
FREQ_BOUND = 1.0
CHUNK = 8
GROUPS = 4


def padded_2(cells, sides, width):
    for axis, dim in sides:
        count = lax.axis_size(axis)
        ends = count - 1
        head = lax.slice_in_dim(cells, 0, width, axis=dim)
        tail = lax.slice_in_dim(cells, cells.shape[dim] - width, cells.shape[dim], axis=dim)
        cells = jnp.concatenate(
            [
                lax.ppermute(tail, axis, [(i, (i + 1) % count) for i in range(ends)]),
                cells,
                lax.ppermute(head, axis, [((i + 1) % count, i) for i in range(ends)]),
            ],
            axis=dim,
        )
    return cells


def blur_rows(padded, dilation, out_rows):
    running = TAPS[0] * padded[:, 0:out_rows, :]
    for tap_idx in range(1, 5):
        offset = tap_idx * dilation
        running = running + TAPS[tap_idx] * padded[:, offset : offset + out_rows, :]
    return running


def blur_cols(planar, dilation):
    columns = planar.shape[2]
    reach_cols = 2 * dilation
    padded = jnp.pad(planar, ((0, 0), (0, 0), (reach_cols, reach_cols)))
    running = TAPS[0] * padded[:, :, 0:columns]
    for tap_idx in range(1, 5):
        offset = tap_idx * dilation
        running = running + TAPS[tap_idx] * padded[:, :, offset : offset + columns]
    return running


def inside_rows(margin, local_rows):
    first_row = lax.axis_index("rows") * local_rows - margin
    positions = first_row + jnp.arange(local_rows + 2 * margin, dtype=jnp.int32)
    limit = local_rows * lax.axis_size("rows")
    return ((positions >= 0) & (positions < limit)).astype(jnp.float32)[None, :, None]


def analyse(image_cube):
    local_rows = image_cube.shape[1]
    details = []
    depth = 2 ** (SCALES + 1) - 2
    current = padded_2(image_cube, (("rows", 1),), depth)
    inside = inside_rows(depth, local_rows)
    margin = depth
    for level_idx in range(SCALES):
        dilation = 2**level_idx
        reach_rows = 2 * dilation
        new_margin = margin - reach_rows
        out_rows = local_rows + 2 * new_margin
        start_row = depth - new_margin
        smoothed = blur_cols(blur_rows(current, dilation, out_rows), dilation)
        smoothed = smoothed * inside[:, start_row : start_row + out_rows, :]
        kept = current[:, reach_rows : reach_rows + out_rows, :] - smoothed
        details.append(kept[:, new_margin : new_margin + local_rows, :])
        current = smoothed
        margin = new_margin
    return details


def synthesise(space_next):
    local_rows = space_next.shape[2]
    running = jnp.zeros_like(space_next[0])
    for level_idx in reversed(range(SCALES)):
        dilation = 2**level_idx
        operand = running - space_next[level_idx]
        padded = padded_2(operand, (("rows", 1),), 2 * dilation)
        running = (
            blur_cols(blur_rows(padded, dilation, local_rows), dilation) + space_next[level_idx]
        )
    return running


def dct_table(length, parity=None):
    half = length if parity is None else length // 2
    split = 64 if half % 64 == 0 else 1
    groups = half // split
    period = 4 * length
    if parity is None:
        coef_idx = jnp.arange(length, dtype=jnp.int32)
    else:
        coef_idx = 2 * jnp.arange(half, dtype=jnp.int32) + parity
    scale = math.pi / (2 * length)
    outer_phase = (coef_idx[:, None] * (2 * split * jnp.arange(groups, dtype=jnp.int32))[None, :]) % period
    inner_phase = (coef_idx[:, None] * (2 * jnp.arange(split, dtype=jnp.int32) + 1)[None, :]) % period
    outer_angle = outer_phase.astype(jnp.float32) * scale
    inner_angle = inner_phase.astype(jnp.float32) * scale
    weights = jnp.where(
        coef_idx == 0, math.sqrt(1.0 / length), math.sqrt(2.0 / length)
    ).astype(jnp.float32)[:, None, None]
    table = (
        jnp.cos(outer_angle)[:, :, None] * jnp.cos(inner_angle)[:, None, :]
        - jnp.sin(outer_angle)[:, :, None] * jnp.sin(inner_angle)[:, None, :]
    ) * weights
    return table.reshape(coef_idx.shape[0], half)


def forward_dot(samples, table):
    return lax.dot_general(
        samples,
        table,
        (((0,), (1,)), ((), ())),
        precision=lax.Precision.HIGH,
        preferred_element_type=jnp.float32,
    )


def spectral(pixel_cube, freq_duals):
    chans_all, pixel_count = pixel_cube.shape
    if chans_all % 2:
        table = dct_table(chans_all)
        coeffs = forward_dot(pixel_cube, table)
        freq_next = jnp.clip(freq_duals + SIGMA * coeffs, -FREQ_BOUND, FREQ_BOUND)
        return (table,), freq_next, (freq_next,)
    half = chans_all // 2
    head = pixel_cube[:half]
    tail = pixel_cube[half:][::-1]
    tables = (dct_table(chans_all, 0), dct_table(chans_all, 1))
    pairs = freq_duals.reshape(pixel_count, half, 2)
    fresh = tuple(
        jnp.clip(pairs[:, :, parity] + SIGMA * forward_dot(samples, tables[parity]), -FREQ_BOUND, FREQ_BOUND)
        for parity, samples in ((0, head + tail), (1, head - tail))
    )
    freq_next = jnp.stack(fresh, axis=2).reshape(pixel_count, chans_all)
    return tables, freq_next, fresh


def spectral_back(tables, fresh):
    parts = [
        lax.dot_general(
            table,
            values,
            (((0,), (1,)), ((), ())),
            precision=lax.Precision.HIGH,
            preferred_element_type=jnp.float32,
        )
        for table, values in zip(tables, fresh)
    ]
    if len(parts) == 1:
        return parts[0]
    return jnp.concatenate([parts[0] + parts[1], (parts[0] - parts[1])[::-1]], axis=0)


def starlet_kernel(flags_ref, above_ref, own_ref, below_ref, duals_ref, *refs):
    sn_ref, send_ref, mid_ref, keep_ref, buf_a, buf_b = refs[-6:]
    block, local_rows, columns = own_ref.shape
    halo = send_ref.shape[0]
    extent = 2 * halo + local_rows
    pad = 2 ** SCALES
    row0 = flags_ref[0] - halo
    total_rows = flags_ref[1]
    lane = lax.broadcasted_iota(jnp.int32, (1, block, columns), 2)
    weights = {}
    for level_idx in range(SCALES):
        dilation = 2**level_idx
        weights[dilation] = tuple(
            jnp.where(keep, tap, 0.0).astype(jnp.float32)
            for step, tap in ((dilation, TAPS[1]), (2 * dilation, TAPS[0]))
            for keep in (lane >= step, lane < columns - step)
        )

    def smooth_rows(src, dst, dilation, lo, hi):
        near_w, far_w = weights[dilation][0:2], weights[dilation][2:4]
        for start in range(lo, hi, CHUNK):
            size = min(CHUNK, hi - start)
            at = start + pad

            def window(offset):
                return src[pl.ds(at + offset, size)]

            y = TAPS[0] * (window(-2 * dilation) + window(2 * dilation)) + TAPS[1] * (
                window(-dilation) + window(dilation)
            ) + TAPS[2] * window(0)
            z = (
                pltpu.roll(y, dilation, 2) * near_w[0]
                + pltpu.roll(y, columns - dilation, 2) * near_w[1]
                + pltpu.roll(y, 2 * dilation, 2) * far_w[0]
                + pltpu.roll(y, columns - 2 * dilation, 2) * far_w[1]
                + TAPS[2] * y
            )
            if start >= halo and start + size <= halo + local_rows:
                dst[pl.ds(at, size)] = z
            else:
                row = row0 + start + lax.broadcasted_iota(jnp.int32, (size, 1, 1), 0)
                dst[pl.ds(at, size)] = jnp.where((row >= 0) & (row < total_rows), z, 0.0)

    def rows_major(value):
        return jnp.swapaxes(value, 0, 1)

    buf_a[...] = jnp.zeros_like(buf_a)
    above = rows_major(above_ref[...])[local_rows - halo :]
    below = rows_major(below_ref[...])[:halo]
    buf_a[pl.ds(pad, halo)] = jnp.where(flags_ref[2] > 0, above, 0.0)
    buf_a[pl.ds(pad + halo, local_rows)] = rows_major(own_ref[...])
    buf_a[pl.ds(pad + halo + local_rows, halo)] = jnp.where(flags_ref[3] > 0, below, 0.0)
    bufs = (buf_a, buf_b)
    own = pl.ds(pad + halo, local_rows)
    fresh = []
    lo, hi = 0, extent
    for level_idx in range(SCALES):
        dilation = 2**level_idx
        src, dst = bufs[level_idx % 2], bufs[(level_idx + 1) % 2]
        lo, hi = lo + 2 * dilation, hi - 2 * dilation
        smooth_rows(src, dst, dilation, lo, hi)
        plane = jnp.clip(
            duals_ref[level_idx] + SIGMA * rows_major(src[own] - dst[own]), -SPACE_BOUND, SPACE_BOUND
        )
        sn_ref[level_idx] = plane

    buf_a[...] = jnp.zeros_like(buf_a)
    buf_b[...] = jnp.zeros_like(buf_b)
    lo, hi = halo, halo + local_rows
    for count, level_idx in enumerate(reversed(range(SCALES))):
        dilation = 2**level_idx
        src, dst = bufs[count % 2], bufs[(count + 1) % 2]
        plane = rows_major(sn_ref[level_idx])
        src[own] = src[own] - plane
        lo, hi = lo - 2 * dilation, hi + 2 * dilation
        smooth_rows(src, dst, dilation, max(lo, 0), min(hi, extent))
        dst[own] = dst[own] + plane
    top = dst[pl.ds(pad, halo)]
    bot = dst[pl.ds(pad + halo + local_rows, halo)]
    swap = flags_ref[4] > 0
    send_ref[...] = jnp.where(swap, bot, top)
    keep_ref[...] = jnp.where(swap, top, bot)
    mid_ref[...] = rows_major(dst[own])


def starlet(flags, above, own, below, duals, halo, group, groups, carry=(), interpret=False):
    chans, local_rows, columns = own.shape
    block = math.gcd(chans, 8)
    steps = chans // block // groups
    base = group * steps
    extent = 2 * halo + local_rows + 2 * 2**SCALES
    near_spec = pl.BlockSpec((block, local_rows, columns), lambda i: (i, 0, 0))
    own_spec = pl.BlockSpec((block, local_rows, columns), lambda i: (i + base, 0, 0))
    dual_spec = pl.BlockSpec((SCALES, block, local_rows, columns), lambda i: (0, i + base, 0, 0))
    edge_spec = pl.BlockSpec((halo, block, columns), lambda i: (0, i, 0))
    edge_shape = jax.ShapeDtypeStruct((halo, chans // groups, columns), jnp.float32)
    carry_specs = [pl.BlockSpec(memory_space=pl.ANY)] * len(carry)
    return pl.pallas_call(
        starlet_kernel,
        grid=(steps,),
        in_specs=[pl.BlockSpec(memory_space=pltpu.SMEM), near_spec, own_spec, near_spec, dual_spec] + carry_specs,
        out_specs=[dual_spec, edge_spec, own_spec, edge_spec],
        out_shape=[
            jax.ShapeDtypeStruct(duals.shape, jnp.float32),
            edge_shape,
            jax.ShapeDtypeStruct(own.shape, jnp.float32),
            edge_shape,
        ],
        scratch_shapes=[pltpu.VMEM((extent, block, columns), jnp.float32)] * 2,
        input_output_aliases={5: 0, 6: 2} if carry else {},
        interpret=interpret,
    )(flags, above, own, below, duals, *carry)


def row_plan(chans, local_rows):
    halo = 2 ** (SCALES + 1) - 2
    assert local_rows >= halo
    block = math.gcd(chans, 8)
    groups = math.gcd(chans // block, GROUPS)
    return halo, groups, chans // groups


def exchange_halos(image_cube):
    chans, local_rows, columns = image_cube.shape
    halo, groups, width = row_plan(chans, local_rows)
    count = lax.axis_size("rows")
    down = [(i, i + 1) for i in range(count - 1)]
    up = [(i + 1, i) for i in range(count - 1)]
    halos = []
    for group in range(groups):
        part = image_cube[group * width : (group + 1) * width]
        if halos:
            part, halos[-1] = lax.optimization_barrier((part, halos[-1]))
        if count == 2:
            got = lax.ppermute(part, "rows", down + up)
            halos.append((got, got))
        else:
            halos.append((lax.ppermute(part, "rows", down), lax.ppermute(part, "rows", up)))
    return halos


class Spatial:
    def __init__(self, image_cube, space_duals):
        self.image_cube = image_cube
        self.space_duals = space_duals
        chans, local_rows, columns = image_cube.shape
        self.halo, self.groups, self.width = row_plan(chans, local_rows)
        count = lax.axis_size("rows")
        self.index = lax.axis_index("rows")
        self.down = [(i, i + 1) for i in range(count - 1)]
        self.up = [(i + 1, i) for i in range(count - 1)]
        self.paired = count == 2
        index = self.index
        self.flags = jnp.stack(
            [index * local_rows, count * local_rows, index > 0, index < count - 1, self.paired & (index == 0)]
        ).astype(jnp.int32)
        self.sends, self.keeps = [], []

    def run(self, group, halos, carry):
        above, below = halos[group]
        space_next, send, mid, keep = starlet(
            self.flags, above, self.image_cube, below, self.space_duals, self.halo, group, self.groups, carry
        )
        if self.paired:
            self.sends.append(lax.ppermute(send, "rows", self.down + self.up))
        else:
            self.sends.append(lax.ppermute(send, "rows", self.up))
            self.keeps.append(lax.ppermute(keep, "rows", self.down))
        return (space_next, mid)

    def finish(self, carry):
        space_next, mid = carry
        local_rows = mid.shape[1]
        got = jnp.concatenate(self.sends, axis=1)
        gap = local_rows - self.halo
        if self.paired:
            spill = jnp.where(
                self.index == 0,
                jnp.pad(got, ((gap, 0), (0, 0), (0, 0))),
                jnp.pad(got, ((0, gap), (0, 0), (0, 0))),
            )
        else:
            spill = jnp.pad(jnp.concatenate(self.keeps, axis=1), ((0, gap), (0, 0), (0, 0))) + jnp.pad(
                got, ((gap, 0), (0, 0), (0, 0))
            )
        return mid + jnp.transpose(spill, (1, 0, 2)), space_next


def local(image_cube, data_grad, space_duals, freq_duals):
    chans, local_rows, columns = image_cube.shape
    peers = lax.axis_size("freq")
    share = local_rows * columns // peers
    pieces = image_cube.reshape(chans, peers, share)
    halos = exchange_halos(image_cube)
    pixel_cube = lax.all_to_all(pieces, "freq", split_axis=1, concat_axis=0, tiled=True).reshape(
        chans * peers, share
    )
    work = Spatial(image_cube, space_duals)
    early = work.groups // 2
    carry = ()
    for group in range(early):
        carry = work.run(group, halos, carry)
    pixel_cube, carry, later = lax.optimization_barrier((pixel_cube, carry, halos[early:]))
    halos = halos[:early] + list(later)
    tables, freq_next, fresh = spectral(pixel_cube, freq_duals)
    spectral_sum = spectral_back(tables, fresh)
    spectral_sum, carry, work.sends, work.keeps = lax.optimization_barrier(
        (spectral_sum, carry, work.sends, work.keeps)
    )
    returned = lax.all_to_all(
        spectral_sum.reshape(peers, chans, share),
        "freq",
        split_axis=0,
        concat_axis=2,
        tiled=True,
    )
    for group in range(early, work.groups):
        carry = work.run(group, halos, carry)
    space_term, space_next = work.finish(carry)
    spectral_term = returned.reshape(chans, local_rows, columns)
    image_next = jnp.maximum(image_cube - TAU_STEP * (data_grad + space_term + spectral_term), 0.0)
    return (image_next, space_next, freq_next)


def solution(mesh):
    in_specs = (
        P("freq", "rows", None),
        P("freq", "rows", None),
        P(None, "freq", "rows", None),
        P(("rows", "freq"), None),
    )
    out_specs = (P("freq", "rows", None), P(None, "freq", "rows", None), P(("rows", "freq"), None))
    return jax.shard_map(local, mesh=mesh, in_specs=in_specs, out_specs=out_specs, check_vma=False)
```

```python
import math

import jax
import jax.numpy as jnp
from jax import lax
from jax.sharding import PartitionSpec as P
from jax.experimental import pallas as pl
from jax.experimental.pallas import tpu as pltpu

SCALES = 4


TAPS = (0.0625, 0.25, 0.375, 0.25, 0.0625)
SIGMA = 0.5
TAU_STEP = 0.5
SPACE_BOUND = 0.5
FREQ_BOUND = 1.0
CHUNK = 8
GROUPS = 4


def padded_2(cells, sides, width):
    for axis, dim in sides:
        count = lax.axis_size(axis)
        ends = count - 1
        head = lax.slice_in_dim(cells, 0, width, axis=dim)
        tail = lax.slice_in_dim(cells, cells.shape[dim] - width, cells.shape[dim], axis=dim)
        cells = jnp.concatenate(
            [
                lax.ppermute(tail, axis, [(i, (i + 1) % count) for i in range(ends)]),
                cells,
                lax.ppermute(head, axis, [((i + 1) % count, i) for i in range(ends)]),
            ],
            axis=dim,
        )
    return cells


def blur_rows(padded, dilation, out_rows):
    running = TAPS[0] * padded[:, 0:out_rows, :]
    for tap_idx in range(1, 5):
        offset = tap_idx * dilation
        running = running + TAPS[tap_idx] * padded[:, offset : offset + out_rows, :]
    return running


def blur_cols(planar, dilation):
    columns = planar.shape[2]
    reach_cols = 2 * dilation
    padded = jnp.pad(planar, ((0, 0), (0, 0), (reach_cols, reach_cols)))
    running = TAPS[0] * padded[:, :, 0:columns]
    for tap_idx in range(1, 5):
        offset = tap_idx * dilation
        running = running + TAPS[tap_idx] * padded[:, :, offset : offset + columns]
    return running


def inside_rows(margin, local_rows):
    first_row = lax.axis_index("rows") * local_rows - margin
    positions = first_row + jnp.arange(local_rows + 2 * margin, dtype=jnp.int32)
    limit = local_rows * lax.axis_size("rows")
    return ((positions >= 0) & (positions < limit)).astype(jnp.float32)[None, :, None]


def analyse(image_cube):
    local_rows = image_cube.shape[1]
    details = []
    depth = 2 ** (SCALES + 1) - 2
    current = padded_2(image_cube, (("rows", 1),), depth)
    inside = inside_rows(depth, local_rows)
    margin = depth
    for level_idx in range(SCALES):
        dilation = 2**level_idx
        reach_rows = 2 * dilation
        new_margin = margin - reach_rows
        out_rows = local_rows + 2 * new_margin
        start_row = depth - new_margin
        smoothed = blur_cols(blur_rows(current, dilation, out_rows), dilation)
        smoothed = smoothed * inside[:, start_row : start_row + out_rows, :]
        kept = current[:, reach_rows : reach_rows + out_rows, :] - smoothed
        details.append(kept[:, new_margin : new_margin + local_rows, :])
        current = smoothed
        margin = new_margin
    return details


def synthesise(space_next):
    local_rows = space_next.shape[2]
    running = jnp.zeros_like(space_next[0])
    for level_idx in reversed(range(SCALES)):
        dilation = 2**level_idx
        operand = running - space_next[level_idx]
        padded = padded_2(operand, (("rows", 1),), 2 * dilation)
        running = (
            blur_cols(blur_rows(padded, dilation, local_rows), dilation) + space_next[level_idx]
        )
    return running


def dct_table(length, parity=None):
    half = length if parity is None else length // 2
    split = 64 if half % 64 == 0 else 1
    groups = half // split
    period = 4 * length
    if parity is None:
        coef_idx = jnp.arange(length, dtype=jnp.int32)
    else:
        coef_idx = 2 * jnp.arange(half, dtype=jnp.int32) + parity
    scale = math.pi / (2 * length)
    outer_phase = (coef_idx[:, None] * (2 * split * jnp.arange(groups, dtype=jnp.int32))[None, :]) % period
    inner_phase = (coef_idx[:, None] * (2 * jnp.arange(split, dtype=jnp.int32) + 1)[None, :]) % period
    outer_angle = outer_phase.astype(jnp.float32) * scale
    inner_angle = inner_phase.astype(jnp.float32) * scale
    weights = jnp.where(
        coef_idx == 0, math.sqrt(1.0 / length), math.sqrt(2.0 / length)
    ).astype(jnp.float32)[:, None, None]
    table = (
        jnp.cos(outer_angle)[:, :, None] * jnp.cos(inner_angle)[:, None, :]
        - jnp.sin(outer_angle)[:, :, None] * jnp.sin(inner_angle)[:, None, :]
    ) * weights
    return table.reshape(coef_idx.shape[0], half)


def forward_dot(samples, table):
    return lax.dot_general(
        samples,
        table,
        (((0,), (1,)), ((), ())),
        precision=lax.Precision.HIGH,
        preferred_element_type=jnp.float32,
    )


def spectral(pixel_cube, freq_duals):
    chans_all, pixel_count = pixel_cube.shape
    if chans_all % 2:
        table = dct_table(chans_all)
        coeffs = forward_dot(pixel_cube, table)
        freq_next = jnp.clip(freq_duals + SIGMA * coeffs, -FREQ_BOUND, FREQ_BOUND)
        return (table,), freq_next, (freq_next,)
    half = chans_all // 2
    head = pixel_cube[:half]
    tail = pixel_cube[half:][::-1]
    tables = (dct_table(chans_all, 0), dct_table(chans_all, 1))
    pairs = freq_duals.reshape(pixel_count, half, 2)
    fresh = tuple(
        jnp.clip(pairs[:, :, parity] + SIGMA * forward_dot(samples, tables[parity]), -FREQ_BOUND, FREQ_BOUND)
        for parity, samples in ((0, head + tail), (1, head - tail))
    )
    freq_next = jnp.stack(fresh, axis=2).reshape(pixel_count, chans_all)
    return tables, freq_next, fresh


def spectral_back(tables, fresh):
    parts = [
        lax.dot_general(
            table,
            values,
            (((0,), (1,)), ((), ())),
            precision=lax.Precision.HIGH,
            preferred_element_type=jnp.float32,
        )
        for table, values in zip(tables, fresh)
    ]
    if len(parts) == 1:
        return parts[0]
    return jnp.concatenate([parts[0] + parts[1], (parts[0] - parts[1])[::-1]], axis=0)


def starlet_kernel(flags_ref, above_ref, own_ref, below_ref, duals_ref, *refs):
    sn_ref, send_ref, mid_ref, keep_ref, buf_a, buf_b = refs[-6:]
    block, local_rows, columns = own_ref.shape
    halo = 2 ** (SCALES + 1) - 2
    extent = 2 * halo + local_rows
    pad = 2 ** SCALES
    row0 = flags_ref[0] - halo
    total_rows = flags_ref[1]
    lane = lax.broadcasted_iota(jnp.int32, (1, block, columns), 2)
    weights = {}
    for level_idx in range(SCALES):
        dilation = 2**level_idx
        weights[dilation] = tuple(
            jnp.where(keep, tap, 0.0).astype(jnp.float32)
            for step, tap in ((dilation, TAPS[1]), (2 * dilation, TAPS[0]))
            for keep in (lane >= step, lane < columns - step)
        )

    def smooth_rows(src, dst, dilation, lo, hi):
        near_w, far_w = weights[dilation][0:2], weights[dilation][2:4]
        for start in range(lo, hi, CHUNK):
            size = min(CHUNK, hi - start)
            at = start + pad

            def window(offset):
                return src[pl.ds(at + offset, size)]

            y = TAPS[0] * (window(-2 * dilation) + window(2 * dilation)) + TAPS[1] * (
                window(-dilation) + window(dilation)
            ) + TAPS[2] * window(0)
            z = (
                pltpu.roll(y, dilation, 2) * near_w[0]
                + pltpu.roll(y, columns - dilation, 2) * near_w[1]
                + pltpu.roll(y, 2 * dilation, 2) * far_w[0]
                + pltpu.roll(y, columns - 2 * dilation, 2) * far_w[1]
                + TAPS[2] * y
            )
            if start >= halo and start + size <= halo + local_rows:
                dst[pl.ds(at, size)] = z
            else:
                row = row0 + start + lax.broadcasted_iota(jnp.int32, (size, 1, 1), 0)
                dst[pl.ds(at, size)] = jnp.where((row >= 0) & (row < total_rows), z, 0.0)

    def rows_major(value):
        return jnp.swapaxes(value, 0, 1)

    buf_a[...] = jnp.zeros_like(buf_a)
    above = rows_major(above_ref[...])[local_rows - halo :]
    below = rows_major(below_ref[...])[:halo]
    buf_a[pl.ds(pad, halo)] = jnp.where(flags_ref[2] > 0, above, 0.0)
    buf_a[pl.ds(pad + halo, local_rows)] = rows_major(own_ref[...])
    buf_a[pl.ds(pad + halo + local_rows, halo)] = jnp.where(flags_ref[3] > 0, below, 0.0)
    bufs = (buf_a, buf_b)
    own = pl.ds(pad + halo, local_rows)
    fresh = []
    lo, hi = 0, extent
    for level_idx in range(SCALES):
        dilation = 2**level_idx
        src, dst = bufs[level_idx % 2], bufs[(level_idx + 1) % 2]
        lo, hi = lo + 2 * dilation, hi - 2 * dilation
        smooth_rows(src, dst, dilation, lo, hi)
        plane = jnp.clip(
            duals_ref[level_idx] + SIGMA * rows_major(src[own] - dst[own]), -SPACE_BOUND, SPACE_BOUND
        )
        sn_ref[level_idx] = plane

    buf_a[...] = jnp.zeros_like(buf_a)
    buf_b[...] = jnp.zeros_like(buf_b)
    lo, hi = halo, halo + local_rows
    for count, level_idx in enumerate(reversed(range(SCALES))):
        dilation = 2**level_idx
        src, dst = bufs[count % 2], bufs[(count + 1) % 2]
        plane = rows_major(sn_ref[level_idx])
        src[own] = src[own] - plane
        lo, hi = lo - 2 * dilation, hi + 2 * dilation
        smooth_rows(src, dst, dilation, max(lo, 0), min(hi, extent))
        dst[own] = dst[own] + plane
    top = dst[pl.ds(pad + halo - local_rows, local_rows)]
    bot = dst[pl.ds(pad + halo + local_rows, local_rows)]
    swap = flags_ref[4] > 0
    send_ref[...] = rows_major(jnp.where(swap, bot, top))
    keep_ref[...] = rows_major(jnp.where(swap, top, bot))
    mid_ref[...] = rows_major(dst[own])


def starlet(flags, above, own, below, duals, halo, group, groups, carry=(), interpret=False):
    chans, local_rows, columns = own.shape
    block = math.gcd(chans, 8)
    steps = chans // block // groups
    base = group * steps
    extent = 2 * halo + local_rows + 2 * 2**SCALES
    near_spec = pl.BlockSpec((block, local_rows, columns), lambda i: (i, 0, 0))
    own_spec = pl.BlockSpec((block, local_rows, columns), lambda i: (i + base, 0, 0))
    dual_spec = pl.BlockSpec((SCALES, block, local_rows, columns), lambda i: (0, i + base, 0, 0))
    assert local_rows - halo <= 2**SCALES <= halo
    edge_spec = near_spec
    edge_shape = jax.ShapeDtypeStruct((chans // groups, local_rows, columns), jnp.float32)
    carry_specs = [pl.BlockSpec(memory_space=pl.ANY)] * len(carry)
    return pl.pallas_call(
        starlet_kernel,
        grid=(steps,),
        in_specs=[pl.BlockSpec(memory_space=pltpu.SMEM), near_spec, own_spec, near_spec, dual_spec] + carry_specs,
        out_specs=[dual_spec, edge_spec, own_spec, edge_spec],
        out_shape=[
            jax.ShapeDtypeStruct(duals.shape, jnp.float32),
            edge_shape,
            jax.ShapeDtypeStruct(own.shape, jnp.float32),
            edge_shape,
        ],
        scratch_shapes=[pltpu.VMEM((extent, block, columns), jnp.float32)] * 2,
        input_output_aliases={5: 0, 6: 2} if carry else {},
        interpret=interpret,
    )(flags, above, own, below, duals, *carry)


def row_plan(chans, local_rows):
    halo = 2 ** (SCALES + 1) - 2
    assert local_rows >= halo
    block = math.gcd(chans, 8)
    groups = math.gcd(chans // block, GROUPS)
    return halo, groups, chans // groups


def exchange_halos(image_cube):
    chans, local_rows, columns = image_cube.shape
    halo, groups, width = row_plan(chans, local_rows)
    count = lax.axis_size("rows")
    down = [(i, i + 1) for i in range(count - 1)]
    up = [(i + 1, i) for i in range(count - 1)]
    halos = []
    for group in range(groups):
        part = image_cube[group * width : (group + 1) * width]
        if halos:
            part, halos[-1] = lax.optimization_barrier((part, halos[-1]))
        if count == 2:
            got = lax.ppermute(part, "rows", down + up)
            halos.append((got, got))
        else:
            halos.append((lax.ppermute(part, "rows", down), lax.ppermute(part, "rows", up)))
    return halos


class Spatial:
    def __init__(self, image_cube, space_duals):
        self.image_cube = image_cube
        self.space_duals = space_duals
        chans, local_rows, columns = image_cube.shape
        self.halo, self.groups, self.width = row_plan(chans, local_rows)
        count = lax.axis_size("rows")
        self.index = lax.axis_index("rows")
        self.down = [(i, i + 1) for i in range(count - 1)]
        self.up = [(i + 1, i) for i in range(count - 1)]
        self.paired = count == 2
        index = self.index
        self.flags = jnp.stack(
            [index * local_rows, count * local_rows, index > 0, index < count - 1, self.paired & (index == 0)]
        ).astype(jnp.int32)
        self.sends, self.keeps = [], []

    def run(self, group, halos, carry):
        above, below = halos[group]
        space_next, send, mid, keep = starlet(
            self.flags, above, self.image_cube, below, self.space_duals, self.halo, group, self.groups, carry
        )
        if self.paired:
            self.sends.append(lax.ppermute(send, "rows", self.down + self.up))
        else:
            self.sends.append(lax.ppermute(send, "rows", self.up))
            self.keeps.append(lax.ppermute(keep, "rows", self.down))
        return (space_next, mid)

    def finish(self, carry):
        space_next, mid = carry
        space_term = mid + jnp.concatenate(self.sends, axis=0)
        if not self.paired:
            space_term = space_term + jnp.concatenate(self.keeps, axis=0)
        return space_term, space_next


def local(image_cube, data_grad, space_duals, freq_duals):
    chans, local_rows, columns = image_cube.shape
    peers = lax.axis_size("freq")
    share = local_rows * columns // peers
    pieces = image_cube.reshape(chans, peers, share)
    halos = exchange_halos(image_cube)
    pixel_cube = lax.all_to_all(pieces, "freq", split_axis=1, concat_axis=0, tiled=True).reshape(
        chans * peers, share
    )
    work = Spatial(image_cube, space_duals)
    early = work.groups // 2
    carry = ()
    for group in range(early):
        carry = work.run(group, halos, carry)
    pixel_cube, carry, later = lax.optimization_barrier((pixel_cube, carry, halos[early:]))
    halos = halos[:early] + list(later)
    tables, freq_next, fresh = spectral(pixel_cube, freq_duals)
    spectral_sum = spectral_back(tables, fresh)
    spectral_sum, carry, work.sends, work.keeps = lax.optimization_barrier(
        (spectral_sum, carry, work.sends, work.keeps)
    )
    returned = lax.all_to_all(
        spectral_sum.reshape(peers, chans, share),
        "freq",
        split_axis=0,
        concat_axis=2,
        tiled=True,
    )
    for group in range(early, work.groups):
        carry = work.run(group, halos, carry)
    space_term, space_next = work.finish(carry)
    spectral_term = returned.reshape(chans, local_rows, columns)
    image_next = jnp.maximum(image_cube - TAU_STEP * (data_grad + space_term + spectral_term), 0.0)
    return (image_next, space_next, freq_next)


def solution(mesh):
    in_specs = (
        P("freq", "rows", None),
        P("freq", "rows", None),
        P(None, "freq", "rows", None),
        P(("rows", "freq"), None),
    )
    out_specs = (P("freq", "rows", None), P(None, "freq", "rows", None), P(("rows", "freq"), None))
    return jax.shard_map(local, mesh=mesh, in_specs=in_specs, out_specs=out_specs, check_vma=False)
```

```python
import math

import jax
import jax.numpy as jnp
from jax import lax
from jax.sharding import PartitionSpec as P
from jax.experimental import pallas as pl
from jax.experimental.pallas import tpu as pltpu

SCALES = 4


TAPS = (0.0625, 0.25, 0.375, 0.25, 0.0625)
SIGMA = 0.5
TAU_STEP = 0.5
SPACE_BOUND = 0.5
FREQ_BOUND = 1.0
CHUNK = 8
GROUPS = 4


def padded_2(cells, sides, width):
    for axis, dim in sides:
        count = lax.axis_size(axis)
        ends = count - 1
        head = lax.slice_in_dim(cells, 0, width, axis=dim)
        tail = lax.slice_in_dim(cells, cells.shape[dim] - width, cells.shape[dim], axis=dim)
        cells = jnp.concatenate(
            [
                lax.ppermute(tail, axis, [(i, (i + 1) % count) for i in range(ends)]),
                cells,
                lax.ppermute(head, axis, [((i + 1) % count, i) for i in range(ends)]),
            ],
            axis=dim,
        )
    return cells


def blur_rows(padded, dilation, out_rows):
    running = TAPS[0] * padded[:, 0:out_rows, :]
    for tap_idx in range(1, 5):
        offset = tap_idx * dilation
        running = running + TAPS[tap_idx] * padded[:, offset : offset + out_rows, :]
    return running


def blur_cols(planar, dilation):
    columns = planar.shape[2]
    reach_cols = 2 * dilation
    padded = jnp.pad(planar, ((0, 0), (0, 0), (reach_cols, reach_cols)))
    running = TAPS[0] * padded[:, :, 0:columns]
    for tap_idx in range(1, 5):
        offset = tap_idx * dilation
        running = running + TAPS[tap_idx] * padded[:, :, offset : offset + columns]
    return running


def inside_rows(margin, local_rows):
    first_row = lax.axis_index("rows") * local_rows - margin
    positions = first_row + jnp.arange(local_rows + 2 * margin, dtype=jnp.int32)
    limit = local_rows * lax.axis_size("rows")
    return ((positions >= 0) & (positions < limit)).astype(jnp.float32)[None, :, None]


def analyse(image_cube):
    local_rows = image_cube.shape[1]
    details = []
    depth = 2 ** (SCALES + 1) - 2
    current = padded_2(image_cube, (("rows", 1),), depth)
    inside = inside_rows(depth, local_rows)
    margin = depth
    for level_idx in range(SCALES):
        dilation = 2**level_idx
        reach_rows = 2 * dilation
        new_margin = margin - reach_rows
        out_rows = local_rows + 2 * new_margin
        start_row = depth - new_margin
        smoothed = blur_cols(blur_rows(current, dilation, out_rows), dilation)
        smoothed = smoothed * inside[:, start_row : start_row + out_rows, :]
        kept = current[:, reach_rows : reach_rows + out_rows, :] - smoothed
        details.append(kept[:, new_margin : new_margin + local_rows, :])
        current = smoothed
        margin = new_margin
    return details


def synthesise(space_next):
    local_rows = space_next.shape[2]
    running = jnp.zeros_like(space_next[0])
    for level_idx in reversed(range(SCALES)):
        dilation = 2**level_idx
        operand = running - space_next[level_idx]
        padded = padded_2(operand, (("rows", 1),), 2 * dilation)
        running = (
            blur_cols(blur_rows(padded, dilation, local_rows), dilation) + space_next[level_idx]
        )
    return running


def dct_table(length, parity=None):
    half = length if parity is None else length // 2
    split = 64 if half % 64 == 0 else 1
    groups = half // split
    period = 4 * length
    if parity is None:
        coef_idx = jnp.arange(length, dtype=jnp.int32)
    else:
        coef_idx = 2 * jnp.arange(half, dtype=jnp.int32) + parity
    scale = math.pi / (2 * length)
    outer_phase = (coef_idx[:, None] * (2 * split * jnp.arange(groups, dtype=jnp.int32))[None, :]) % period
    inner_phase = (coef_idx[:, None] * (2 * jnp.arange(split, dtype=jnp.int32) + 1)[None, :]) % period
    outer_angle = outer_phase.astype(jnp.float32) * scale
    inner_angle = inner_phase.astype(jnp.float32) * scale
    weights = jnp.where(
        coef_idx == 0, math.sqrt(1.0 / length), math.sqrt(2.0 / length)
    ).astype(jnp.float32)[:, None, None]
    table = (
        jnp.cos(outer_angle)[:, :, None] * jnp.cos(inner_angle)[:, None, :]
        - jnp.sin(outer_angle)[:, :, None] * jnp.sin(inner_angle)[:, None, :]
    ) * weights
    return table.reshape(coef_idx.shape[0], half)


def forward_dot(samples, table):
    return lax.dot_general(
        samples,
        table,
        (((0,), (1,)), ((), ())),
        precision=lax.Precision.HIGH,
        preferred_element_type=jnp.float32,
    )


def spectral(pixel_cube, freq_duals):
    chans_all, pixel_count = pixel_cube.shape
    if chans_all % 2:
        table = dct_table(chans_all)
        coeffs = forward_dot(pixel_cube, table)
        freq_next = jnp.clip(freq_duals + SIGMA * coeffs, -FREQ_BOUND, FREQ_BOUND)
        return (table,), freq_next, (freq_next,)
    half = chans_all // 2
    head = pixel_cube[:half]
    tail = pixel_cube[half:][::-1]
    tables = (dct_table(chans_all, 0), dct_table(chans_all, 1))
    pairs = freq_duals.reshape(pixel_count, half, 2)
    fresh = tuple(
        jnp.clip(pairs[:, :, parity] + SIGMA * forward_dot(samples, tables[parity]), -FREQ_BOUND, FREQ_BOUND)
        for parity, samples in ((0, head + tail), (1, head - tail))
    )
    freq_next = jnp.stack(fresh, axis=2).reshape(pixel_count, chans_all)
    return tables, freq_next, fresh


def spectral_back(tables, fresh):
    parts = [
        lax.dot_general(
            table,
            values,
            (((0,), (1,)), ((), ())),
            precision=lax.Precision.HIGH,
            preferred_element_type=jnp.float32,
        )
        for table, values in zip(tables, fresh)
    ]
    if len(parts) == 1:
        return parts[0]
    return jnp.concatenate([parts[0] + parts[1], (parts[0] - parts[1])[::-1]], axis=0)


def starlet_kernel(flags_ref, above_ref, own_ref, below_ref, duals_ref, *refs):
    sn_ref, send_ref, mid_ref, keep_ref, buf_a, buf_b = refs[-6:]
    block, local_rows, columns = own_ref.shape
    halo = 2 ** (SCALES + 1) - 2
    extent = 2 * halo + local_rows
    pad = 2 ** SCALES
    row0 = flags_ref[0] - halo
    total_rows = flags_ref[1]
    lane = lax.broadcasted_iota(jnp.int32, (1, block, columns), 2)
    weights = {}
    for level_idx in range(SCALES):
        dilation = 2**level_idx
        weights[dilation] = tuple(
            jnp.where(keep, tap, 0.0).astype(jnp.float32)
            for step, tap in ((dilation, TAPS[1]), (2 * dilation, TAPS[0]))
            for keep in (lane >= step, lane < columns - step)
        )

    def smooth_rows(src, dst, dilation, lo, hi):
        near_w, far_w = weights[dilation][0:2], weights[dilation][2:4]
        for start in range(lo, hi, CHUNK):
            size = min(CHUNK, hi - start)
            at = start + pad

            def window(offset):
                return src[pl.ds(at + offset, size)]

            y = TAPS[0] * (window(-2 * dilation) + window(2 * dilation)) + TAPS[1] * (
                window(-dilation) + window(dilation)
            ) + TAPS[2] * window(0)
            z = (
                pltpu.roll(y, dilation, 2) * near_w[0]
                + pltpu.roll(y, columns - dilation, 2) * near_w[1]
                + pltpu.roll(y, 2 * dilation, 2) * far_w[0]
                + pltpu.roll(y, columns - 2 * dilation, 2) * far_w[1]
                + TAPS[2] * y
            )
            if start >= halo and start + size <= halo + local_rows:
                dst[pl.ds(at, size)] = z
            else:
                row = row0 + start + lax.broadcasted_iota(jnp.int32, (size, 1, 1), 0)
                dst[pl.ds(at, size)] = jnp.where((row >= 0) & (row < total_rows), z, 0.0)

    def rows_major(value):
        return jnp.swapaxes(value, 0, 1)

    buf_a[...] = jnp.zeros_like(buf_a)
    above = rows_major(above_ref[...])[local_rows - halo :]
    below = rows_major(below_ref[...])[:halo]
    buf_a[pl.ds(pad, halo)] = jnp.where(flags_ref[2] > 0, above, 0.0)
    buf_a[pl.ds(pad + halo, local_rows)] = rows_major(own_ref[...])
    buf_a[pl.ds(pad + halo + local_rows, halo)] = jnp.where(flags_ref[3] > 0, below, 0.0)
    bufs = (buf_a, buf_b)
    own = pl.ds(pad + halo, local_rows)
    fresh = []
    lo, hi = 0, extent
    for level_idx in range(SCALES):
        dilation = 2**level_idx
        src, dst = bufs[level_idx % 2], bufs[(level_idx + 1) % 2]
        lo, hi = lo + 2 * dilation, hi - 2 * dilation
        smooth_rows(src, dst, dilation, lo, hi)
        plane = jnp.clip(
            duals_ref[level_idx] + SIGMA * rows_major(src[own] - dst[own]), -SPACE_BOUND, SPACE_BOUND
        )
        sn_ref[level_idx] = plane

    buf_a[...] = jnp.zeros_like(buf_a)
    buf_b[...] = jnp.zeros_like(buf_b)
    lo, hi = halo, halo + local_rows
    for count, level_idx in enumerate(reversed(range(SCALES))):
        dilation = 2**level_idx
        src, dst = bufs[count % 2], bufs[(count + 1) % 2]
        plane = rows_major(sn_ref[level_idx])
        src[own] = src[own] - plane
        lo, hi = lo - 2 * dilation, hi + 2 * dilation
        smooth_rows(src, dst, dilation, max(lo, 0), min(hi, extent))
        dst[own] = dst[own] + plane
    top = dst[pl.ds(pad + halo - local_rows, local_rows)]
    bot = dst[pl.ds(pad + halo + local_rows, local_rows)]
    swap = flags_ref[4] > 0
    send_ref[...] = rows_major(jnp.where(swap, bot, top))
    keep_ref[...] = rows_major(jnp.where(swap, top, bot))
    mid_ref[...] = rows_major(dst[own])


def starlet(flags, above, own, below, duals, halo, group, groups, carry=(), near_base=0, interpret=False):
    chans, local_rows, columns = own.shape
    block = math.gcd(chans, 8)
    steps = chans // block // groups
    base = group * steps
    extent = 2 * halo + local_rows + 2 * 2**SCALES
    near_spec = pl.BlockSpec((block, local_rows, columns), lambda i: (i + near_base, 0, 0))
    edge_spec = pl.BlockSpec((block, local_rows, columns), lambda i: (i, 0, 0))
    own_spec = pl.BlockSpec((block, local_rows, columns), lambda i: (i + base, 0, 0))
    dual_spec = pl.BlockSpec((SCALES, block, local_rows, columns), lambda i: (0, i + base, 0, 0))
    assert local_rows - halo <= 2**SCALES <= halo
    edge_shape = jax.ShapeDtypeStruct((chans // groups, local_rows, columns), jnp.float32)
    carry_specs = [pl.BlockSpec(memory_space=pl.ANY)] * len(carry)
    return pl.pallas_call(
        starlet_kernel,
        grid=(steps,),
        in_specs=[pl.BlockSpec(memory_space=pltpu.SMEM), near_spec, own_spec, near_spec, dual_spec] + carry_specs,
        out_specs=[dual_spec, edge_spec, own_spec, edge_spec],
        out_shape=[
            jax.ShapeDtypeStruct(duals.shape, jnp.float32),
            edge_shape,
            jax.ShapeDtypeStruct(own.shape, jnp.float32),
            edge_shape,
        ],
        scratch_shapes=[pltpu.VMEM((extent, block, columns), jnp.float32)] * 2,
        input_output_aliases={5: 0, 6: 2} if carry else {},
        interpret=interpret,
    )(flags, above, own, below, duals, *carry)


def row_plan(chans, local_rows):
    halo = 2 ** (SCALES + 1) - 2
    assert local_rows >= halo
    block = math.gcd(chans, 8)
    groups = math.gcd(chans // block, GROUPS)
    return halo, groups, chans // groups


def exchange_halos(image_cube, early):
    chans, local_rows, columns = image_cube.shape
    halo, groups, width = row_plan(chans, local_rows)
    count = lax.axis_size("rows")
    down = [(i, i + 1) for i in range(count - 1)]
    up = [(i + 1, i) for i in range(count - 1)]
    cuts = [(0, early), (early, groups)] if 0 < early < groups else [(0, groups)]
    halos = []
    previous = None
    for first, last in cuts:
        part = image_cube[first * width : last * width]
        if previous is not None:
            part, previous = lax.optimization_barrier((part, previous))
        if count == 2:
            got = lax.ppermute(part, "rows", down + up)
            pair = (got, got)
        else:
            pair = (lax.ppermute(part, "rows", down), lax.ppermute(part, "rows", up))
        previous = pair
        block = math.gcd(chans, 8)
        steps = width // block
        halos.extend((pair, (group - first) * steps) for group in range(first, last))
    return halos


class Spatial:
    def __init__(self, image_cube, space_duals):
        self.image_cube = image_cube
        self.space_duals = space_duals
        chans, local_rows, columns = image_cube.shape
        self.halo, self.groups, self.width = row_plan(chans, local_rows)
        count = lax.axis_size("rows")
        self.index = lax.axis_index("rows")
        self.down = [(i, i + 1) for i in range(count - 1)]
        self.up = [(i + 1, i) for i in range(count - 1)]
        self.paired = count == 2
        index = self.index
        self.flags = jnp.stack(
            [index * local_rows, count * local_rows, index > 0, index < count - 1, self.paired & (index == 0)]
        ).astype(jnp.int32)
        self.sends, self.keeps = [], []

    def run(self, group, halos, carry):
        (above, below), near_base = halos[group]
        space_next, send, mid, keep = starlet(
            self.flags, above, self.image_cube, below, self.space_duals, self.halo, group, self.groups, carry,
            near_base,
        )
        if self.paired:
            self.sends.append(lax.ppermute(send, "rows", self.down + self.up))
        else:
            self.sends.append(lax.ppermute(send, "rows", self.up))
            self.keeps.append(lax.ppermute(keep, "rows", self.down))
        return (space_next, mid)

    def finish(self, carry):
        space_next, mid = carry
        space_term = mid + jnp.concatenate(self.sends, axis=0)
        if not self.paired:
            space_term = space_term + jnp.concatenate(self.keeps, axis=0)
        return space_term, space_next


def local(image_cube, data_grad, space_duals, freq_duals):
    chans, local_rows, columns = image_cube.shape
    peers = lax.axis_size("freq")
    share = local_rows * columns // peers
    pieces = image_cube.reshape(chans, peers, share)
    work = Spatial(image_cube, space_duals)
    early = work.groups // 2
    halos = exchange_halos(image_cube, early)
    pixel_cube = lax.all_to_all(pieces, "freq", split_axis=1, concat_axis=0, tiled=True).reshape(
        chans * peers, share
    )
    carry = ()
    for group in range(early):
        carry = work.run(group, halos, carry)
    later = [pair for pair, _ in halos[early:]]
    pixel_cube, carry, later = lax.optimization_barrier((pixel_cube, carry, later))
    halos = halos[:early] + [(pair, base) for pair, (_, base) in zip(later, halos[early:])]
    tables, freq_next, fresh = spectral(pixel_cube, freq_duals)
    spectral_sum = spectral_back(tables, fresh)
    spectral_sum, carry, work.sends, work.keeps = lax.optimization_barrier(
        (spectral_sum, carry, work.sends, work.keeps)
    )
    returned = lax.all_to_all(
        spectral_sum.reshape(peers, chans, share),
        "freq",
        split_axis=0,
        concat_axis=2,
        tiled=True,
    )
    for group in range(early, work.groups):
        carry = work.run(group, halos, carry)
    space_term, space_next = work.finish(carry)
    spectral_term = returned.reshape(chans, local_rows, columns)
    image_next = jnp.maximum(image_cube - TAU_STEP * (data_grad + space_term + spectral_term), 0.0)
    return (image_next, space_next, freq_next)


def solution(mesh):
    in_specs = (
        P("freq", "rows", None),
        P("freq", "rows", None),
        P(None, "freq", "rows", None),
        P(("rows", "freq"), None),
    )
    out_specs = (P("freq", "rows", None), P(None, "freq", "rows", None), P(("rows", "freq"), None))
    return jax.shard_map(local, mesh=mesh, in_specs=in_specs, out_specs=out_specs, check_vma=False)
```

```python
import math

import jax
import jax.numpy as jnp
from jax import lax
from jax.sharding import PartitionSpec as P
from jax.experimental import pallas as pl
from jax.experimental.pallas import tpu as pltpu

SCALES = 4


TAPS = (0.0625, 0.25, 0.375, 0.25, 0.0625)
SIGMA = 0.5
TAU_STEP = 0.5
SPACE_BOUND = 0.5
FREQ_BOUND = 1.0
CHUNK = 8
GROUPS = 4


def padded_2(cells, sides, width):
    for axis, dim in sides:
        count = lax.axis_size(axis)
        ends = count - 1
        head = lax.slice_in_dim(cells, 0, width, axis=dim)
        tail = lax.slice_in_dim(cells, cells.shape[dim] - width, cells.shape[dim], axis=dim)
        cells = jnp.concatenate(
            [
                lax.ppermute(tail, axis, [(i, (i + 1) % count) for i in range(ends)]),
                cells,
                lax.ppermute(head, axis, [((i + 1) % count, i) for i in range(ends)]),
            ],
            axis=dim,
        )
    return cells


def blur_rows(padded, dilation, out_rows):
    running = TAPS[0] * padded[:, 0:out_rows, :]
    for tap_idx in range(1, 5):
        offset = tap_idx * dilation
        running = running + TAPS[tap_idx] * padded[:, offset : offset + out_rows, :]
    return running


def blur_cols(planar, dilation):
    columns = planar.shape[2]
    reach_cols = 2 * dilation
    padded = jnp.pad(planar, ((0, 0), (0, 0), (reach_cols, reach_cols)))
    running = TAPS[0] * padded[:, :, 0:columns]
    for tap_idx in range(1, 5):
        offset = tap_idx * dilation
        running = running + TAPS[tap_idx] * padded[:, :, offset : offset + columns]
    return running


def inside_rows(margin, local_rows):
    first_row = lax.axis_index("rows") * local_rows - margin
    positions = first_row + jnp.arange(local_rows + 2 * margin, dtype=jnp.int32)
    limit = local_rows * lax.axis_size("rows")
    return ((positions >= 0) & (positions < limit)).astype(jnp.float32)[None, :, None]


def analyse(image_cube):
    local_rows = image_cube.shape[1]
    details = []
    depth = 2 ** (SCALES + 1) - 2
    current = padded_2(image_cube, (("rows", 1),), depth)
    inside = inside_rows(depth, local_rows)
    margin = depth
    for level_idx in range(SCALES):
        dilation = 2**level_idx
        reach_rows = 2 * dilation
        new_margin = margin - reach_rows
        out_rows = local_rows + 2 * new_margin
        start_row = depth - new_margin
        smoothed = blur_cols(blur_rows(current, dilation, out_rows), dilation)
        smoothed = smoothed * inside[:, start_row : start_row + out_rows, :]
        kept = current[:, reach_rows : reach_rows + out_rows, :] - smoothed
        details.append(kept[:, new_margin : new_margin + local_rows, :])
        current = smoothed
        margin = new_margin
    return details


def synthesise(space_next):
    local_rows = space_next.shape[2]
    running = jnp.zeros_like(space_next[0])
    for level_idx in reversed(range(SCALES)):
        dilation = 2**level_idx
        operand = running - space_next[level_idx]
        padded = padded_2(operand, (("rows", 1),), 2 * dilation)
        running = (
            blur_cols(blur_rows(padded, dilation, local_rows), dilation) + space_next[level_idx]
        )
    return running


def dct_table(length, parity=None):
    half = length if parity is None else length // 2
    split = 64 if half % 64 == 0 else 1
    groups = half // split
    period = 4 * length
    if parity is None:
        coef_idx = jnp.arange(length, dtype=jnp.int32)
    else:
        coef_idx = 2 * jnp.arange(half, dtype=jnp.int32) + parity
    scale = math.pi / (2 * length)
    outer_phase = (coef_idx[:, None] * (2 * split * jnp.arange(groups, dtype=jnp.int32))[None, :]) % period
    inner_phase = (coef_idx[:, None] * (2 * jnp.arange(split, dtype=jnp.int32) + 1)[None, :]) % period
    outer_angle = outer_phase.astype(jnp.float32) * scale
    inner_angle = inner_phase.astype(jnp.float32) * scale
    weights = jnp.where(
        coef_idx == 0, math.sqrt(1.0 / length), math.sqrt(2.0 / length)
    ).astype(jnp.float32)[:, None, None]
    table = (
        jnp.cos(outer_angle)[:, :, None] * jnp.cos(inner_angle)[:, None, :]
        - jnp.sin(outer_angle)[:, :, None] * jnp.sin(inner_angle)[:, None, :]
    ) * weights
    return table.reshape(coef_idx.shape[0], half)


def forward_dot(samples, table):
    return lax.dot_general(
        samples,
        table,
        (((0,), (1,)), ((), ())),
        precision=lax.Precision.HIGH,
        preferred_element_type=jnp.float32,
    )


def spectral(pixel_cube, freq_duals):
    chans_all, pixel_count = pixel_cube.shape
    if chans_all % 2:
        table = dct_table(chans_all)
        coeffs = forward_dot(pixel_cube, table)
        freq_next = jnp.clip(freq_duals + SIGMA * coeffs, -FREQ_BOUND, FREQ_BOUND)
        return (table,), freq_next, (freq_next,)
    half = chans_all // 2
    head = pixel_cube[:half]
    tail = pixel_cube[half:][::-1]
    tables = (dct_table(chans_all, 0), dct_table(chans_all, 1))
    pairs = freq_duals.reshape(pixel_count, half, 2)
    fresh = tuple(
        jnp.clip(pairs[:, :, parity] + SIGMA * forward_dot(samples, tables[parity]), -FREQ_BOUND, FREQ_BOUND)
        for parity, samples in ((0, head + tail), (1, head - tail))
    )
    freq_next = jnp.stack(fresh, axis=2).reshape(pixel_count, chans_all)
    return tables, freq_next, fresh


def spectral_back(tables, fresh):
    parts = [
        lax.dot_general(
            table,
            values,
            (((0,), (1,)), ((), ())),
            precision=lax.Precision.HIGH,
            preferred_element_type=jnp.float32,
        )
        for table, values in zip(tables, fresh)
    ]
    if len(parts) == 1:
        return parts[0]
    return jnp.concatenate([parts[0] + parts[1], (parts[0] - parts[1])[::-1]], axis=0)


def starlet_kernel(flags_ref, above_ref, own_ref, below_ref, duals_ref, *refs):
    sn_ref, send_ref, mid_ref, keep_ref, buf_a, buf_b = refs[-6:]
    block, local_rows, columns = own_ref.shape
    halo = 2 ** (SCALES + 1) - 2
    extent = 2 * halo + local_rows
    pad = 2 ** SCALES
    row0 = flags_ref[0] - halo
    total_rows = flags_ref[1]
    lane = lax.broadcasted_iota(jnp.int32, (1, block, columns), 2)
    weights = {}
    for level_idx in range(SCALES):
        dilation = 2**level_idx
        weights[dilation] = tuple(
            jnp.where(keep, tap, 0.0).astype(jnp.float32)
            for step, tap in ((dilation, TAPS[1]), (2 * dilation, TAPS[0]))
            for keep in (lane >= step, lane < columns - step)
        )

    def smooth_rows(src, dst, dilation, lo, hi):
        near_w, far_w = weights[dilation][0:2], weights[dilation][2:4]
        for start in range(lo, hi, CHUNK):
            size = min(CHUNK, hi - start)
            at = start + pad

            def window(offset):
                return src[pl.ds(at + offset, size)]

            y = TAPS[0] * (window(-2 * dilation) + window(2 * dilation)) + TAPS[1] * (
                window(-dilation) + window(dilation)
            ) + TAPS[2] * window(0)
            z = (
                pltpu.roll(y, dilation, 2) * near_w[0]
                + pltpu.roll(y, columns - dilation, 2) * near_w[1]
                + pltpu.roll(y, 2 * dilation, 2) * far_w[0]
                + pltpu.roll(y, columns - 2 * dilation, 2) * far_w[1]
                + TAPS[2] * y
            )
            if start >= halo and start + size <= halo + local_rows:
                dst[pl.ds(at, size)] = z
            else:
                row = row0 + start + lax.broadcasted_iota(jnp.int32, (size, 1, 1), 0)
                dst[pl.ds(at, size)] = jnp.where((row >= 0) & (row < total_rows), z, 0.0)

    def rows_major(value):
        return jnp.swapaxes(value, 0, 1)

    buf_a[...] = jnp.zeros_like(buf_a)
    above = rows_major(above_ref[...])[local_rows - halo :]
    below = rows_major(below_ref[...])[:halo]
    buf_a[pl.ds(pad, halo)] = jnp.where(flags_ref[2] > 0, above, 0.0)
    buf_a[pl.ds(pad + halo, local_rows)] = rows_major(own_ref[...])
    buf_a[pl.ds(pad + halo + local_rows, halo)] = jnp.where(flags_ref[3] > 0, below, 0.0)
    bufs = (buf_a, buf_b)
    own = pl.ds(pad + halo, local_rows)
    fresh = []
    lo, hi = 0, extent
    for level_idx in range(SCALES):
        dilation = 2**level_idx
        src, dst = bufs[level_idx % 2], bufs[(level_idx + 1) % 2]
        lo, hi = lo + 2 * dilation, hi - 2 * dilation
        smooth_rows(src, dst, dilation, lo, hi)
        plane = jnp.clip(
            duals_ref[level_idx] + SIGMA * rows_major(src[own] - dst[own]), -SPACE_BOUND, SPACE_BOUND
        )
        sn_ref[level_idx] = plane

    buf_a[...] = jnp.zeros_like(buf_a)
    buf_b[...] = jnp.zeros_like(buf_b)
    lo, hi = halo, halo + local_rows
    for count, level_idx in enumerate(reversed(range(SCALES))):
        dilation = 2**level_idx
        src, dst = bufs[count % 2], bufs[(count + 1) % 2]
        plane = rows_major(sn_ref[level_idx])
        src[own] = src[own] - plane
        lo, hi = lo - 2 * dilation, hi + 2 * dilation
        smooth_rows(src, dst, dilation, max(lo, 0), min(hi, extent))
        dst[own] = dst[own] + plane
    top = dst[pl.ds(pad + halo - local_rows, local_rows)]
    bot = dst[pl.ds(pad + halo + local_rows, local_rows)]
    swap = flags_ref[4] > 0
    send_ref[...] = rows_major(jnp.where(swap, bot, top))
    keep_ref[...] = rows_major(jnp.where(swap, top, bot))
    mid_ref[...] = rows_major(dst[own])


def starlet(flags, above, own, below, duals, halo, group, groups, carry=(), near_base=0, interpret=False):
    chans, local_rows, columns = own.shape
    block = math.gcd(chans, 8)
    steps = chans // block // groups
    base = group * steps
    extent = 2 * halo + local_rows + 2 * 2**SCALES
    near_spec = pl.BlockSpec((block, local_rows, columns), lambda i: (i + near_base, 0, 0))
    edge_spec = pl.BlockSpec((block, local_rows, columns), lambda i: (i, 0, 0))
    own_spec = pl.BlockSpec((block, local_rows, columns), lambda i: (i + base, 0, 0))
    dual_spec = pl.BlockSpec((SCALES, block, local_rows, columns), lambda i: (0, i + base, 0, 0))
    assert local_rows - halo <= 2**SCALES <= halo
    edge_shape = jax.ShapeDtypeStruct((chans // groups, local_rows, columns), jnp.float32)
    carry_specs = [pl.BlockSpec(memory_space=pl.ANY)] * len(carry)
    return pl.pallas_call(
        starlet_kernel,
        grid=(steps,),
        in_specs=[pl.BlockSpec(memory_space=pltpu.SMEM), near_spec, own_spec, near_spec, dual_spec] + carry_specs,
        out_specs=[dual_spec, edge_spec, own_spec, edge_spec],
        out_shape=[
            jax.ShapeDtypeStruct(duals.shape, jnp.float32),
            edge_shape,
            jax.ShapeDtypeStruct(own.shape, jnp.float32),
            edge_shape,
        ],
        scratch_shapes=[pltpu.VMEM((extent, block, columns), jnp.float32)] * 2,
        input_output_aliases={5: 0, 6: 2} if carry else {},
        interpret=interpret,
    )(flags, above, own, below, duals, *carry)


def row_plan(chans, local_rows):
    halo = 2 ** (SCALES + 1) - 2
    assert local_rows >= halo
    block = math.gcd(chans, 8)
    groups = math.gcd(chans // block, GROUPS)
    return halo, groups, chans // groups


def exchange_halos(image_cube, early):
    chans, local_rows, columns = image_cube.shape
    halo, groups, width = row_plan(chans, local_rows)
    count = lax.axis_size("rows")
    down = [(i, i + 1) for i in range(count - 1)]
    up = [(i + 1, i) for i in range(count - 1)]
    cuts = [(0, early), (early, groups)] if 0 < early < groups else [(0, groups)]
    halos = []
    previous = None
    for first, last in cuts:
        part = image_cube[first * width : last * width]
        if previous is not None:
            part, previous = lax.optimization_barrier((part, previous))
        if count == 2:
            got = lax.ppermute(part, "rows", down + up)
            pair = (got, got)
        else:
            pair = (lax.ppermute(part, "rows", down), lax.ppermute(part, "rows", up))
        previous = pair
        block = math.gcd(chans, 8)
        steps = width // block
        halos.extend((pair, (group - first) * steps) for group in range(first, last))
    return halos


class Spatial:
    def __init__(self, image_cube, space_duals):
        self.image_cube = image_cube
        self.space_duals = space_duals
        chans, local_rows, columns = image_cube.shape
        self.halo, self.groups, self.width = row_plan(chans, local_rows)
        count = lax.axis_size("rows")
        self.index = lax.axis_index("rows")
        self.down = [(i, i + 1) for i in range(count - 1)]
        self.up = [(i + 1, i) for i in range(count - 1)]
        self.paired = count == 2
        index = self.index
        self.flags = jnp.stack(
            [index * local_rows, count * local_rows, index > 0, index < count - 1, self.paired & (index == 0)]
        ).astype(jnp.int32)
        self.sends, self.keeps = [], []

    def run(self, group, halos, carry):
        (above, below), near_base = halos[group]
        space_next, send, mid, keep = starlet(
            self.flags, above, self.image_cube, below, self.space_duals, self.halo, group, self.groups, carry,
            near_base,
        )
        if self.paired:
            self.sends.append(lax.ppermute(send, "rows", self.down + self.up))
        else:
            self.sends.append(lax.ppermute(send, "rows", self.up))
            self.keeps.append(lax.ppermute(keep, "rows", self.down))
        return (space_next, mid)

    def finish(self, carry):
        space_next, mid = carry
        got = jnp.concatenate(self.sends, axis=0)
        if not self.paired:
            got = got + jnp.concatenate(self.keeps, axis=0)
        return mid, got, space_next


def combine_kernel(image_ref, grad_ref, mid_ref, got_ref, returned_ref, out_ref):
    block, local_rows, columns = image_ref.shape
    slabs = [returned_ref[:, pl.ds(row * columns, columns)] for row in range(local_rows)]
    spectral_term = jnp.swapaxes(jnp.stack(slabs, axis=0), 0, 1)
    space_term = mid_ref[...] + got_ref[...]
    out_ref[...] = jnp.maximum(
        image_ref[...] - TAU_STEP * (grad_ref[...] + space_term + spectral_term), 0.0
    )


def combine(image_cube, data_grad, mid, got, returned):
    chans, local_rows, columns = image_cube.shape
    block = math.gcd(chans, 8)
    plane_spec = pl.BlockSpec((block, local_rows, columns), lambda i: (i, 0, 0))
    flat_spec = pl.BlockSpec((block, local_rows * columns), lambda i: (i, 0))
    return pl.pallas_call(
        combine_kernel,
        grid=(chans // block,),
        in_specs=[plane_spec, plane_spec, plane_spec, plane_spec, flat_spec],
        out_specs=plane_spec,
        out_shape=jax.ShapeDtypeStruct(image_cube.shape, jnp.float32),
    )(image_cube, data_grad, mid, got, returned)


def local(image_cube, data_grad, space_duals, freq_duals):
    chans, local_rows, columns = image_cube.shape
    peers = lax.axis_size("freq")
    share = local_rows * columns // peers
    pieces = image_cube.reshape(chans, peers, share)
    work = Spatial(image_cube, space_duals)
    early = work.groups // 2
    halos = exchange_halos(image_cube, early)
    pixel_cube = lax.all_to_all(pieces, "freq", split_axis=1, concat_axis=0, tiled=True).reshape(
        chans * peers, share
    )
    carry = ()
    for group in range(early):
        carry = work.run(group, halos, carry)
    later = [pair for pair, _ in halos[early:]]
    pixel_cube, carry, later = lax.optimization_barrier((pixel_cube, carry, later))
    halos = halos[:early] + [(pair, base) for pair, (_, base) in zip(later, halos[early:])]
    tables, freq_next, fresh = spectral(pixel_cube, freq_duals)
    spectral_sum = spectral_back(tables, fresh)
    spectral_sum, carry, work.sends, work.keeps = lax.optimization_barrier(
        (spectral_sum, carry, work.sends, work.keeps)
    )
    returned = lax.all_to_all(
        spectral_sum.reshape(peers, chans, share),
        "freq",
        split_axis=0,
        concat_axis=2,
        tiled=True,
    )
    for group in range(early, work.groups):
        carry = work.run(group, halos, carry)
    mid, got, space_next = work.finish(carry)
    image_next = combine(image_cube, data_grad, mid, got, returned.reshape(chans, local_rows * columns))
    return (image_next, space_next, freq_next)


def solution(mesh):
    in_specs = (
        P("freq", "rows", None),
        P("freq", "rows", None),
        P(None, "freq", "rows", None),
        P(("rows", "freq"), None),
    )
    out_specs = (P("freq", "rows", None), P(None, "freq", "rows", None), P(("rows", "freq"), None))
    return jax.shard_map(local, mesh=mesh, in_specs=in_specs, out_specs=out_specs, check_vma=False)
```

```python
import math

import jax
import jax.numpy as jnp
from jax import lax
from jax.sharding import PartitionSpec as P
from jax.experimental import pallas as pl
from jax.experimental.pallas import tpu as pltpu

SCALES = 4


TAPS = (0.0625, 0.25, 0.375, 0.25, 0.0625)
SIGMA = 0.5
TAU_STEP = 0.5
SPACE_BOUND = 0.5
FREQ_BOUND = 1.0
CHUNK = 8
GROUPS = 4


def padded_2(cells, sides, width):
    for axis, dim in sides:
        count = lax.axis_size(axis)
        ends = count - 1
        head = lax.slice_in_dim(cells, 0, width, axis=dim)
        tail = lax.slice_in_dim(cells, cells.shape[dim] - width, cells.shape[dim], axis=dim)
        cells = jnp.concatenate(
            [
                lax.ppermute(tail, axis, [(i, (i + 1) % count) for i in range(ends)]),
                cells,
                lax.ppermute(head, axis, [((i + 1) % count, i) for i in range(ends)]),
            ],
            axis=dim,
        )
    return cells


def blur_rows(padded, dilation, out_rows):
    running = TAPS[0] * padded[:, 0:out_rows, :]
    for tap_idx in range(1, 5):
        offset = tap_idx * dilation
        running = running + TAPS[tap_idx] * padded[:, offset : offset + out_rows, :]
    return running


def blur_cols(planar, dilation):
    columns = planar.shape[2]
    reach_cols = 2 * dilation
    padded = jnp.pad(planar, ((0, 0), (0, 0), (reach_cols, reach_cols)))
    running = TAPS[0] * padded[:, :, 0:columns]
    for tap_idx in range(1, 5):
        offset = tap_idx * dilation
        running = running + TAPS[tap_idx] * padded[:, :, offset : offset + columns]
    return running


def inside_rows(margin, local_rows):
    first_row = lax.axis_index("rows") * local_rows - margin
    positions = first_row + jnp.arange(local_rows + 2 * margin, dtype=jnp.int32)
    limit = local_rows * lax.axis_size("rows")
    return ((positions >= 0) & (positions < limit)).astype(jnp.float32)[None, :, None]


def analyse(image_cube):
    local_rows = image_cube.shape[1]
    details = []
    depth = 2 ** (SCALES + 1) - 2
    current = padded_2(image_cube, (("rows", 1),), depth)
    inside = inside_rows(depth, local_rows)
    margin = depth
    for level_idx in range(SCALES):
        dilation = 2**level_idx
        reach_rows = 2 * dilation
        new_margin = margin - reach_rows
        out_rows = local_rows + 2 * new_margin
        start_row = depth - new_margin
        smoothed = blur_cols(blur_rows(current, dilation, out_rows), dilation)
        smoothed = smoothed * inside[:, start_row : start_row + out_rows, :]
        kept = current[:, reach_rows : reach_rows + out_rows, :] - smoothed
        details.append(kept[:, new_margin : new_margin + local_rows, :])
        current = smoothed
        margin = new_margin
    return details


def synthesise(space_next):
    local_rows = space_next.shape[2]
    running = jnp.zeros_like(space_next[0])
    for level_idx in reversed(range(SCALES)):
        dilation = 2**level_idx
        operand = running - space_next[level_idx]
        padded = padded_2(operand, (("rows", 1),), 2 * dilation)
        running = (
            blur_cols(blur_rows(padded, dilation, local_rows), dilation) + space_next[level_idx]
        )
    return running


def dct_table(length, parity=None):
    half = length if parity is None else length // 2
    split = 64 if half % 64 == 0 else 1
    groups = half // split
    period = 4 * length
    if parity is None:
        coef_idx = jnp.arange(length, dtype=jnp.int32)
    else:
        coef_idx = 2 * jnp.arange(half, dtype=jnp.int32) + parity
    scale = math.pi / (2 * length)
    outer_phase = (coef_idx[:, None] * (2 * split * jnp.arange(groups, dtype=jnp.int32))[None, :]) % period
    inner_phase = (coef_idx[:, None] * (2 * jnp.arange(split, dtype=jnp.int32) + 1)[None, :]) % period
    outer_angle = outer_phase.astype(jnp.float32) * scale
    inner_angle = inner_phase.astype(jnp.float32) * scale
    weights = jnp.where(
        coef_idx == 0, math.sqrt(1.0 / length), math.sqrt(2.0 / length)
    ).astype(jnp.float32)[:, None, None]
    table = (
        jnp.cos(outer_angle)[:, :, None] * jnp.cos(inner_angle)[:, None, :]
        - jnp.sin(outer_angle)[:, :, None] * jnp.sin(inner_angle)[:, None, :]
    ) * weights
    return table.reshape(coef_idx.shape[0], half)


def forward_dot(samples, table):
    return lax.dot_general(
        samples,
        table,
        (((0,), (1,)), ((), ())),
        precision=lax.Precision.HIGH,
        preferred_element_type=jnp.float32,
    )


def spectral(pixel_cube, freq_duals):
    chans_all, pixel_count = pixel_cube.shape
    if chans_all % 2:
        table = dct_table(chans_all)
        coeffs = forward_dot(pixel_cube, table)
        freq_next = jnp.clip(freq_duals + SIGMA * coeffs, -FREQ_BOUND, FREQ_BOUND)
        return (table,), freq_next, (freq_next,)
    half = chans_all // 2
    head = pixel_cube[:half]
    tail = pixel_cube[half:][::-1]
    tables = (dct_table(chans_all, 0), dct_table(chans_all, 1))
    pairs = freq_duals.reshape(pixel_count, half, 2)
    fresh = tuple(
        jnp.clip(pairs[:, :, parity] + SIGMA * forward_dot(samples, tables[parity]), -FREQ_BOUND, FREQ_BOUND)
        for parity, samples in ((0, head + tail), (1, head - tail))
    )
    freq_next = jnp.stack(fresh, axis=2).reshape(pixel_count, chans_all)
    return tables, freq_next, fresh


def spectral_back(tables, fresh):
    parts = [
        lax.dot_general(
            table,
            values,
            (((0,), (1,)), ((), ())),
            precision=lax.Precision.HIGH,
            preferred_element_type=jnp.float32,
        )
        for table, values in zip(tables, fresh)
    ]
    if len(parts) == 1:
        return parts[0]
    return jnp.concatenate([parts[0] + parts[1], (parts[0] - parts[1])[::-1]], axis=0)


def starlet_kernel(flags_ref, above_ref, own_ref, below_ref, duals_ref, *refs):
    sn_ref, send_ref, mid_ref, keep_ref, buf_a, buf_b, planes = refs[-7:]
    block, local_rows, columns = own_ref.shape
    halo = 2 ** (SCALES + 1) - 2
    extent = 2 * halo + local_rows
    pad = 2 ** SCALES
    row0 = flags_ref[0] - halo
    total_rows = flags_ref[1]
    lane = lax.broadcasted_iota(jnp.int32, (1, block, columns), 2)
    weights = {}
    for level_idx in range(SCALES):
        dilation = 2**level_idx
        weights[dilation] = tuple(
            jnp.where(keep, tap, 0.0).astype(jnp.float32)
            for step, tap in ((dilation, TAPS[1]), (2 * dilation, TAPS[0]))
            for keep in (lane >= step, lane < columns - step)
        )

    def smooth_rows(src, dst, dilation, lo, hi):
        near_w, far_w = weights[dilation][0:2], weights[dilation][2:4]
        for start in range(lo, hi, CHUNK):
            size = min(CHUNK, hi - start)
            at = start + pad

            def window(offset):
                return src[pl.ds(at + offset, size)]

            y = TAPS[0] * (window(-2 * dilation) + window(2 * dilation)) + TAPS[1] * (
                window(-dilation) + window(dilation)
            ) + TAPS[2] * window(0)
            z = (
                pltpu.roll(y, dilation, 2) * near_w[0]
                + pltpu.roll(y, columns - dilation, 2) * near_w[1]
                + pltpu.roll(y, 2 * dilation, 2) * far_w[0]
                + pltpu.roll(y, columns - 2 * dilation, 2) * far_w[1]
                + TAPS[2] * y
            )
            if start >= halo and start + size <= halo + local_rows:
                dst[pl.ds(at, size)] = z
            else:
                row = row0 + start + lax.broadcasted_iota(jnp.int32, (size, 1, 1), 0)
                dst[pl.ds(at, size)] = jnp.where((row >= 0) & (row < total_rows), z, 0.0)

    def rows_major(value):
        return jnp.swapaxes(value, 0, 1)

    above = rows_major(above_ref[...])[local_rows - halo :]
    below = rows_major(below_ref[...])[:halo]
    buf_a[pl.ds(pad, halo)] = jnp.where(flags_ref[2] > 0, above, 0.0)
    buf_a[pl.ds(pad + halo, local_rows)] = rows_major(own_ref[...])
    buf_a[pl.ds(pad + halo + local_rows, halo)] = jnp.where(flags_ref[3] > 0, below, 0.0)
    bufs = (buf_a, buf_b)
    own = pl.ds(pad + halo, local_rows)
    fresh = []
    lo, hi = 0, extent
    for level_idx in range(SCALES):
        dilation = 2**level_idx
        src, dst = bufs[level_idx % 2], bufs[(level_idx + 1) % 2]
        lo, hi = lo + 2 * dilation, hi - 2 * dilation
        smooth_rows(src, dst, dilation, lo, hi)
        plane = jnp.clip(
            rows_major(duals_ref[level_idx]) + SIGMA * (src[own] - dst[own]), -SPACE_BOUND, SPACE_BOUND
        )
        planes[level_idx] = plane
        sn_ref[level_idx] = rows_major(plane)

    buf_a[...] = jnp.zeros_like(buf_a)
    buf_b[...] = jnp.zeros_like(buf_b)
    lo, hi = halo, halo + local_rows
    for count, level_idx in enumerate(reversed(range(SCALES))):
        dilation = 2**level_idx
        src, dst = bufs[count % 2], bufs[(count + 1) % 2]
        plane = planes[level_idx]
        src[own] = src[own] - plane
        lo, hi = lo - 2 * dilation, hi + 2 * dilation
        smooth_rows(src, dst, dilation, max(lo, 0), min(hi, extent))
        dst[own] = dst[own] + plane
    top = dst[pl.ds(pad + halo - local_rows, local_rows)]
    bot = dst[pl.ds(pad + halo + local_rows, local_rows)]
    swap = flags_ref[4] > 0
    send_ref[...] = rows_major(jnp.where(swap, bot, top))
    keep_ref[...] = rows_major(jnp.where(swap, top, bot))
    mid_ref[...] = rows_major(dst[own])


def starlet(flags, above, own, below, duals, halo, group, groups, carry=(), near_base=0, interpret=False):
    chans, local_rows, columns = own.shape
    block = math.gcd(chans, 8)
    steps = chans // block // groups
    base = group * steps
    extent = 2 * halo + local_rows + 2 * 2**SCALES
    near_spec = pl.BlockSpec((block, local_rows, columns), lambda i: (i + near_base, 0, 0))
    edge_spec = pl.BlockSpec((block, local_rows, columns), lambda i: (i, 0, 0))
    own_spec = pl.BlockSpec((block, local_rows, columns), lambda i: (i + base, 0, 0))
    dual_spec = pl.BlockSpec((SCALES, block, local_rows, columns), lambda i: (0, i + base, 0, 0))
    assert local_rows - halo <= 2**SCALES <= halo
    edge_shape = jax.ShapeDtypeStruct((chans // groups, local_rows, columns), jnp.float32)
    carry_specs = [pl.BlockSpec(memory_space=pl.ANY)] * len(carry)
    return pl.pallas_call(
        starlet_kernel,
        grid=(steps,),
        in_specs=[pl.BlockSpec(memory_space=pltpu.SMEM), near_spec, own_spec, near_spec, dual_spec] + carry_specs,
        out_specs=[dual_spec, edge_spec, own_spec, edge_spec],
        out_shape=[
            jax.ShapeDtypeStruct(duals.shape, jnp.float32),
            edge_shape,
            jax.ShapeDtypeStruct(own.shape, jnp.float32),
            edge_shape,
        ],
        scratch_shapes=[pltpu.VMEM((extent, block, columns), jnp.float32)] * 2
        + [pltpu.VMEM((SCALES, local_rows, block, columns), jnp.float32)],
        input_output_aliases={5: 0, 6: 2} if carry else {},
        interpret=interpret,
    )(flags, above, own, below, duals, *carry)


def row_plan(chans, local_rows):
    halo = 2 ** (SCALES + 1) - 2
    assert local_rows >= halo
    block = math.gcd(chans, 8)
    groups = math.gcd(chans // block, GROUPS)
    return halo, groups, chans // groups


def exchange_halos(image_cube, early):
    chans, local_rows, columns = image_cube.shape
    halo, groups, width = row_plan(chans, local_rows)
    count = lax.axis_size("rows")
    down = [(i, i + 1) for i in range(count - 1)]
    up = [(i + 1, i) for i in range(count - 1)]
    cuts = [(0, early), (early, groups)] if 0 < early < groups else [(0, groups)]
    halos = []
    previous = None
    for first, last in cuts:
        part = image_cube[first * width : last * width]
        if previous is not None:
            part, previous = lax.optimization_barrier((part, previous))
        if count == 2:
            got = lax.ppermute(part, "rows", down + up)
            pair = (got, got)
        else:
            pair = (lax.ppermute(part, "rows", down), lax.ppermute(part, "rows", up))
        previous = pair
        block = math.gcd(chans, 8)
        steps = width // block
        halos.extend((pair, (group - first) * steps) for group in range(first, last))
    return halos


class Spatial:
    def __init__(self, image_cube, space_duals):
        self.image_cube = image_cube
        self.space_duals = space_duals
        chans, local_rows, columns = image_cube.shape
        self.halo, self.groups, self.width = row_plan(chans, local_rows)
        count = lax.axis_size("rows")
        self.index = lax.axis_index("rows")
        self.down = [(i, i + 1) for i in range(count - 1)]
        self.up = [(i + 1, i) for i in range(count - 1)]
        self.paired = count == 2
        index = self.index
        self.flags = jnp.stack(
            [index * local_rows, count * local_rows, index > 0, index < count - 1, self.paired & (index == 0)]
        ).astype(jnp.int32)
        self.sends, self.keeps = [], []

    def run(self, group, halos, carry):
        (above, below), near_base = halos[group]
        space_next, send, mid, keep = starlet(
            self.flags, above, self.image_cube, below, self.space_duals, self.halo, group, self.groups, carry,
            near_base,
        )
        if self.paired:
            self.sends.append(lax.ppermute(send, "rows", self.down + self.up))
        else:
            self.sends.append(lax.ppermute(send, "rows", self.up))
            self.keeps.append(lax.ppermute(keep, "rows", self.down))
        return (space_next, mid)

    def finish(self, carry):
        space_next, mid = carry
        space_term = mid + jnp.concatenate(self.sends, axis=0)
        if not self.paired:
            space_term = space_term + jnp.concatenate(self.keeps, axis=0)
        return space_term, space_next


def local(image_cube, data_grad, space_duals, freq_duals):
    chans, local_rows, columns = image_cube.shape
    peers = lax.axis_size("freq")
    share = local_rows * columns // peers
    pieces = image_cube.reshape(chans, peers, share)
    work = Spatial(image_cube, space_duals)
    early = work.groups // 2
    halos = exchange_halos(image_cube, early)
    pixel_cube = lax.all_to_all(pieces, "freq", split_axis=1, concat_axis=0, tiled=True).reshape(
        chans * peers, share
    )
    carry = ()
    for group in range(early):
        carry = work.run(group, halos, carry)
    later = [pair for pair, _ in halos[early:]]
    pixel_cube, carry, later = lax.optimization_barrier((pixel_cube, carry, later))
    halos = halos[:early] + [(pair, base) for pair, (_, base) in zip(later, halos[early:])]
    tables, freq_next, fresh = spectral(pixel_cube, freq_duals)
    spectral_sum = spectral_back(tables, fresh)
    spectral_sum, carry, work.sends, work.keeps = lax.optimization_barrier(
        (spectral_sum, carry, work.sends, work.keeps)
    )
    returned = lax.all_to_all(
        spectral_sum.reshape(peers, chans, share),
        "freq",
        split_axis=0,
        concat_axis=2,
        tiled=True,
    )
    for group in range(early, work.groups):
        carry = work.run(group, halos, carry)
    space_term, space_next = work.finish(carry)
    spectral_term = returned.reshape(chans, local_rows, columns)
    image_next = jnp.maximum(image_cube - TAU_STEP * (data_grad + space_term + spectral_term), 0.0)
    return (image_next, space_next, freq_next)


def solution(mesh):
    in_specs = (
        P("freq", "rows", None),
        P("freq", "rows", None),
        P(None, "freq", "rows", None),
        P(("rows", "freq"), None),
    )
    out_specs = (P("freq", "rows", None), P(None, "freq", "rows", None), P(("rows", "freq"), None))
    return jax.shard_map(local, mesh=mesh, in_specs=in_specs, out_specs=out_specs, check_vma=False)
```

```python
import math

import jax
import jax.numpy as jnp
from jax import lax
from jax.sharding import PartitionSpec as P
from jax.experimental import pallas as pl
from jax.experimental.pallas import tpu as pltpu

SCALES = 4


TAPS = (0.0625, 0.25, 0.375, 0.25, 0.0625)
SIGMA = 0.5
TAU_STEP = 0.5
SPACE_BOUND = 0.5
FREQ_BOUND = 1.0
CHUNK = 16
GROUPS = 4


def padded_2(cells, sides, width):
    for axis, dim in sides:
        count = lax.axis_size(axis)
        ends = count - 1
        head = lax.slice_in_dim(cells, 0, width, axis=dim)
        tail = lax.slice_in_dim(cells, cells.shape[dim] - width, cells.shape[dim], axis=dim)
        cells = jnp.concatenate(
            [
                lax.ppermute(tail, axis, [(i, (i + 1) % count) for i in range(ends)]),
                cells,
                lax.ppermute(head, axis, [((i + 1) % count, i) for i in range(ends)]),
            ],
            axis=dim,
        )
    return cells


def blur_rows(padded, dilation, out_rows):
    running = TAPS[0] * padded[:, 0:out_rows, :]
    for tap_idx in range(1, 5):
        offset = tap_idx * dilation
        running = running + TAPS[tap_idx] * padded[:, offset : offset + out_rows, :]
    return running


def blur_cols(planar, dilation):
    columns = planar.shape[2]
    reach_cols = 2 * dilation
    padded = jnp.pad(planar, ((0, 0), (0, 0), (reach_cols, reach_cols)))
    running = TAPS[0] * padded[:, :, 0:columns]
    for tap_idx in range(1, 5):
        offset = tap_idx * dilation
        running = running + TAPS[tap_idx] * padded[:, :, offset : offset + columns]
    return running


def inside_rows(margin, local_rows):
    first_row = lax.axis_index("rows") * local_rows - margin
    positions = first_row + jnp.arange(local_rows + 2 * margin, dtype=jnp.int32)
    limit = local_rows * lax.axis_size("rows")
    return ((positions >= 0) & (positions < limit)).astype(jnp.float32)[None, :, None]


def analyse(image_cube):
    local_rows = image_cube.shape[1]
    details = []
    depth = 2 ** (SCALES + 1) - 2
    current = padded_2(image_cube, (("rows", 1),), depth)
    inside = inside_rows(depth, local_rows)
    margin = depth
    for level_idx in range(SCALES):
        dilation = 2**level_idx
        reach_rows = 2 * dilation
        new_margin = margin - reach_rows
        out_rows = local_rows + 2 * new_margin
        start_row = depth - new_margin
        smoothed = blur_cols(blur_rows(current, dilation, out_rows), dilation)
        smoothed = smoothed * inside[:, start_row : start_row + out_rows, :]
        kept = current[:, reach_rows : reach_rows + out_rows, :] - smoothed
        details.append(kept[:, new_margin : new_margin + local_rows, :])
        current = smoothed
        margin = new_margin
    return details


def synthesise(space_next):
    local_rows = space_next.shape[2]
    running = jnp.zeros_like(space_next[0])
    for level_idx in reversed(range(SCALES)):
        dilation = 2**level_idx
        operand = running - space_next[level_idx]
        padded = padded_2(operand, (("rows", 1),), 2 * dilation)
        running = (
            blur_cols(blur_rows(padded, dilation, local_rows), dilation) + space_next[level_idx]
        )
    return running


def dct_table(length, parity=None):
    half = length if parity is None else length // 2
    split = 64 if half % 64 == 0 else 1
    groups = half // split
    period = 4 * length
    if parity is None:
        coef_idx = jnp.arange(length, dtype=jnp.int32)
    else:
        coef_idx = 2 * jnp.arange(half, dtype=jnp.int32) + parity
    scale = math.pi / (2 * length)
    outer_phase = (coef_idx[:, None] * (2 * split * jnp.arange(groups, dtype=jnp.int32))[None, :]) % period
    inner_phase = (coef_idx[:, None] * (2 * jnp.arange(split, dtype=jnp.int32) + 1)[None, :]) % period
    outer_angle = outer_phase.astype(jnp.float32) * scale
    inner_angle = inner_phase.astype(jnp.float32) * scale
    weights = jnp.where(
        coef_idx == 0, math.sqrt(1.0 / length), math.sqrt(2.0 / length)
    ).astype(jnp.float32)[:, None, None]
    table = (
        jnp.cos(outer_angle)[:, :, None] * jnp.cos(inner_angle)[:, None, :]
        - jnp.sin(outer_angle)[:, :, None] * jnp.sin(inner_angle)[:, None, :]
    ) * weights
    return table.reshape(coef_idx.shape[0], half)


def forward_dot(samples, table):
    return lax.dot_general(
        samples,
        table,
        (((0,), (1,)), ((), ())),
        precision=lax.Precision.HIGH,
        preferred_element_type=jnp.float32,
    )


def spectral(pixel_cube, freq_duals):
    chans_all, pixel_count = pixel_cube.shape
    if chans_all % 2:
        table = dct_table(chans_all)
        coeffs = forward_dot(pixel_cube, table)
        freq_next = jnp.clip(freq_duals + SIGMA * coeffs, -FREQ_BOUND, FREQ_BOUND)
        return (table,), freq_next, (freq_next,)
    half = chans_all // 2
    head = pixel_cube[:half]
    tail = pixel_cube[half:][::-1]
    tables = (dct_table(chans_all, 0), dct_table(chans_all, 1))
    pairs = freq_duals.reshape(pixel_count, half, 2)
    fresh = tuple(
        jnp.clip(pairs[:, :, parity] + SIGMA * forward_dot(samples, tables[parity]), -FREQ_BOUND, FREQ_BOUND)
        for parity, samples in ((0, head + tail), (1, head - tail))
    )
    freq_next = jnp.stack(fresh, axis=2).reshape(pixel_count, chans_all)
    return tables, freq_next, fresh


def spectral_back(tables, fresh):
    parts = [
        lax.dot_general(
            table,
            values,
            (((0,), (1,)), ((), ())),
            precision=lax.Precision.HIGH,
            preferred_element_type=jnp.float32,
        )
        for table, values in zip(tables, fresh)
    ]
    if len(parts) == 1:
        return parts[0]
    return jnp.concatenate([parts[0] + parts[1], (parts[0] - parts[1])[::-1]], axis=0)


def starlet_kernel(flags_ref, above_ref, own_ref, below_ref, duals_ref, *refs):
    sn_ref, send_ref, mid_ref, keep_ref, buf_a, buf_b = refs[-6:]
    block, local_rows, columns = own_ref.shape
    halo = 2 ** (SCALES + 1) - 2
    extent = 2 * halo + local_rows
    pad = 2 ** SCALES
    row0 = flags_ref[0] - halo
    total_rows = flags_ref[1]
    lane = lax.broadcasted_iota(jnp.int32, (1, block, columns), 2)
    weights = {}
    for level_idx in range(SCALES):
        dilation = 2**level_idx
        weights[dilation] = tuple(
            jnp.where(keep, tap, 0.0).astype(jnp.float32)
            for step, tap in ((dilation, TAPS[1]), (2 * dilation, TAPS[0]))
            for keep in (lane >= step, lane < columns - step)
        )

    def smooth_rows(src, dst, dilation, lo, hi):
        near_w, far_w = weights[dilation][0:2], weights[dilation][2:4]
        for start in range(lo, hi, CHUNK):
            size = min(CHUNK, hi - start)
            at = start + pad

            def window(offset):
                return src[pl.ds(at + offset, size)]

            y = TAPS[0] * (window(-2 * dilation) + window(2 * dilation)) + TAPS[1] * (
                window(-dilation) + window(dilation)
            ) + TAPS[2] * window(0)
            z = (
                pltpu.roll(y, dilation, 2) * near_w[0]
                + pltpu.roll(y, columns - dilation, 2) * near_w[1]
                + pltpu.roll(y, 2 * dilation, 2) * far_w[0]
                + pltpu.roll(y, columns - 2 * dilation, 2) * far_w[1]
                + TAPS[2] * y
            )
            if start >= halo and start + size <= halo + local_rows:
                dst[pl.ds(at, size)] = z
            else:
                row = row0 + start + lax.broadcasted_iota(jnp.int32, (size, 1, 1), 0)
                dst[pl.ds(at, size)] = jnp.where((row >= 0) & (row < total_rows), z, 0.0)

    def rows_major(value):
        return jnp.swapaxes(value, 0, 1)

    buf_a[...] = jnp.zeros_like(buf_a)
    above = rows_major(above_ref[...])[local_rows - halo :]
    below = rows_major(below_ref[...])[:halo]
    buf_a[pl.ds(pad, halo)] = jnp.where(flags_ref[2] > 0, above, 0.0)
    buf_a[pl.ds(pad + halo, local_rows)] = rows_major(own_ref[...])
    buf_a[pl.ds(pad + halo + local_rows, halo)] = jnp.where(flags_ref[3] > 0, below, 0.0)
    bufs = (buf_a, buf_b)
    own = pl.ds(pad + halo, local_rows)
    fresh = []
    lo, hi = 0, extent
    for level_idx in range(SCALES):
        dilation = 2**level_idx
        src, dst = bufs[level_idx % 2], bufs[(level_idx + 1) % 2]
        lo, hi = lo + 2 * dilation, hi - 2 * dilation
        smooth_rows(src, dst, dilation, lo, hi)
        plane = jnp.clip(
            duals_ref[level_idx] + SIGMA * rows_major(src[own] - dst[own]), -SPACE_BOUND, SPACE_BOUND
        )
        sn_ref[level_idx] = plane

    buf_a[...] = jnp.zeros_like(buf_a)
    buf_b[...] = jnp.zeros_like(buf_b)
    lo, hi = halo, halo + local_rows
    for count, level_idx in enumerate(reversed(range(SCALES))):
        dilation = 2**level_idx
        src, dst = bufs[count % 2], bufs[(count + 1) % 2]
        plane = rows_major(sn_ref[level_idx])
        src[own] = src[own] - plane
        lo, hi = lo - 2 * dilation, hi + 2 * dilation
        smooth_rows(src, dst, dilation, max(lo, 0), min(hi, extent))
        dst[own] = dst[own] + plane
    top = dst[pl.ds(pad + halo - local_rows, local_rows)]
    bot = dst[pl.ds(pad + halo + local_rows, local_rows)]
    swap = flags_ref[4] > 0
    send_ref[...] = rows_major(jnp.where(swap, bot, top))
    keep_ref[...] = rows_major(jnp.where(swap, top, bot))
    mid_ref[...] = rows_major(dst[own])


def starlet(flags, above, own, below, duals, halo, group, groups, carry=(), near_base=0, interpret=False):
    chans, local_rows, columns = own.shape
    block = math.gcd(chans, 8)
    steps = chans // block // groups
    base = group * steps
    extent = 2 * halo + local_rows + 2 * 2**SCALES
    near_spec = pl.BlockSpec((block, local_rows, columns), lambda i: (i + near_base, 0, 0))
    edge_spec = pl.BlockSpec((block, local_rows, columns), lambda i: (i, 0, 0))
    own_spec = pl.BlockSpec((block, local_rows, columns), lambda i: (i + base, 0, 0))
    dual_spec = pl.BlockSpec((SCALES, block, local_rows, columns), lambda i: (0, i + base, 0, 0))
    assert local_rows - halo <= 2**SCALES <= halo
    edge_shape = jax.ShapeDtypeStruct((chans // groups, local_rows, columns), jnp.float32)
    carry_specs = [pl.BlockSpec(memory_space=pl.ANY)] * len(carry)
    return pl.pallas_call(
        starlet_kernel,
        grid=(steps,),
        in_specs=[pl.BlockSpec(memory_space=pltpu.SMEM), near_spec, own_spec, near_spec, dual_spec] + carry_specs,
        out_specs=[dual_spec, edge_spec, own_spec, edge_spec],
        out_shape=[
            jax.ShapeDtypeStruct(duals.shape, jnp.float32),
            edge_shape,
            jax.ShapeDtypeStruct(own.shape, jnp.float32),
            edge_shape,
        ],
        scratch_shapes=[pltpu.VMEM((extent, block, columns), jnp.float32)] * 2,
        input_output_aliases={5: 0, 6: 2} if carry else {},
        interpret=interpret,
    )(flags, above, own, below, duals, *carry)


def row_plan(chans, local_rows):
    halo = 2 ** (SCALES + 1) - 2
    assert local_rows >= halo
    block = math.gcd(chans, 8)
    groups = math.gcd(chans // block, GROUPS)
    return halo, groups, chans // groups


def exchange_halos(image_cube, early):
    chans, local_rows, columns = image_cube.shape
    halo, groups, width = row_plan(chans, local_rows)
    count = lax.axis_size("rows")
    down = [(i, i + 1) for i in range(count - 1)]
    up = [(i + 1, i) for i in range(count - 1)]
    cuts = [(0, early), (early, groups)] if 0 < early < groups else [(0, groups)]
    halos = []
    previous = None
    for first, last in cuts:
        part = image_cube[first * width : last * width]
        if previous is not None:
            part, previous = lax.optimization_barrier((part, previous))
        if count == 2:
            got = lax.ppermute(part, "rows", down + up)
            pair = (got, got)
        else:
            pair = (lax.ppermute(part, "rows", down), lax.ppermute(part, "rows", up))
        previous = pair
        block = math.gcd(chans, 8)
        steps = width // block
        halos.extend((pair, (group - first) * steps) for group in range(first, last))
    return halos


class Spatial:
    def __init__(self, image_cube, space_duals):
        self.image_cube = image_cube
        self.space_duals = space_duals
        chans, local_rows, columns = image_cube.shape
        self.halo, self.groups, self.width = row_plan(chans, local_rows)
        count = lax.axis_size("rows")
        self.index = lax.axis_index("rows")
        self.down = [(i, i + 1) for i in range(count - 1)]
        self.up = [(i + 1, i) for i in range(count - 1)]
        self.paired = count == 2
        index = self.index
        self.flags = jnp.stack(
            [index * local_rows, count * local_rows, index > 0, index < count - 1, self.paired & (index == 0)]
        ).astype(jnp.int32)
        self.sends, self.keeps = [], []

    def run(self, group, halos, carry):
        (above, below), near_base = halos[group]
        space_next, send, mid, keep = starlet(
            self.flags, above, self.image_cube, below, self.space_duals, self.halo, group, self.groups, carry,
            near_base,
        )
        if self.paired:
            self.sends.append(lax.ppermute(send, "rows", self.down + self.up))
        else:
            self.sends.append(lax.ppermute(send, "rows", self.up))
            self.keeps.append(lax.ppermute(keep, "rows", self.down))
        return (space_next, mid)

    def finish(self, carry):
        space_next, mid = carry
        space_term = mid + jnp.concatenate(self.sends, axis=0)
        if not self.paired:
            space_term = space_term + jnp.concatenate(self.keeps, axis=0)
        return space_term, space_next


def local(image_cube, data_grad, space_duals, freq_duals):
    chans, local_rows, columns = image_cube.shape
    peers = lax.axis_size("freq")
    share = local_rows * columns // peers
    pieces = image_cube.reshape(chans, peers, share)
    work = Spatial(image_cube, space_duals)
    early = work.groups // 2
    halos = exchange_halos(image_cube, early)
    pixel_cube = lax.all_to_all(pieces, "freq", split_axis=1, concat_axis=0, tiled=True).reshape(
        chans * peers, share
    )
    carry = ()
    for group in range(early):
        carry = work.run(group, halos, carry)
    later = [pair for pair, _ in halos[early:]]
    pixel_cube, carry, later = lax.optimization_barrier((pixel_cube, carry, later))
    halos = halos[:early] + [(pair, base) for pair, (_, base) in zip(later, halos[early:])]
    tables, freq_next, fresh = spectral(pixel_cube, freq_duals)
    spectral_sum = spectral_back(tables, fresh)
    spectral_sum, carry, work.sends, work.keeps = lax.optimization_barrier(
        (spectral_sum, carry, work.sends, work.keeps)
    )
    returned = lax.all_to_all(
        spectral_sum.reshape(peers, chans, share),
        "freq",
        split_axis=0,
        concat_axis=2,
        tiled=True,
    )
    for group in range(early, work.groups):
        carry = work.run(group, halos, carry)
    space_term, space_next = work.finish(carry)
    spectral_term = returned.reshape(chans, local_rows, columns)
    image_next = jnp.maximum(image_cube - TAU_STEP * (data_grad + space_term + spectral_term), 0.0)
    return (image_next, space_next, freq_next)


def solution(mesh):
    in_specs = (
        P("freq", "rows", None),
        P("freq", "rows", None),
        P(None, "freq", "rows", None),
        P(("rows", "freq"), None),
    )
    out_specs = (P("freq", "rows", None), P(None, "freq", "rows", None), P(("rows", "freq"), None))
    return jax.shard_map(local, mesh=mesh, in_specs=in_specs, out_specs=out_specs, check_vma=False)
```

```python
import math

import jax
import jax.numpy as jnp
from jax import lax
from jax.sharding import PartitionSpec as P
from jax.experimental import pallas as pl
from jax.experimental.pallas import tpu as pltpu

SCALES = 4


TAPS = (0.0625, 0.25, 0.375, 0.25, 0.0625)
SIGMA = 0.5
TAU_STEP = 0.5
SPACE_BOUND = 0.5
FREQ_BOUND = 1.0
CHUNK = 8
GROUPS = 4


def padded_2(cells, sides, width):
    for axis, dim in sides:
        count = lax.axis_size(axis)
        ends = count - 1
        head = lax.slice_in_dim(cells, 0, width, axis=dim)
        tail = lax.slice_in_dim(cells, cells.shape[dim] - width, cells.shape[dim], axis=dim)
        cells = jnp.concatenate(
            [
                lax.ppermute(tail, axis, [(i, (i + 1) % count) for i in range(ends)]),
                cells,
                lax.ppermute(head, axis, [((i + 1) % count, i) for i in range(ends)]),
            ],
            axis=dim,
        )
    return cells


def blur_rows(padded, dilation, out_rows):
    running = TAPS[0] * padded[:, 0:out_rows, :]
    for tap_idx in range(1, 5):
        offset = tap_idx * dilation
        running = running + TAPS[tap_idx] * padded[:, offset : offset + out_rows, :]
    return running


def blur_cols(planar, dilation):
    columns = planar.shape[2]
    reach_cols = 2 * dilation
    padded = jnp.pad(planar, ((0, 0), (0, 0), (reach_cols, reach_cols)))
    running = TAPS[0] * padded[:, :, 0:columns]
    for tap_idx in range(1, 5):
        offset = tap_idx * dilation
        running = running + TAPS[tap_idx] * padded[:, :, offset : offset + columns]
    return running


def inside_rows(margin, local_rows):
    first_row = lax.axis_index("rows") * local_rows - margin
    positions = first_row + jnp.arange(local_rows + 2 * margin, dtype=jnp.int32)
    limit = local_rows * lax.axis_size("rows")
    return ((positions >= 0) & (positions < limit)).astype(jnp.float32)[None, :, None]


def analyse(image_cube):
    local_rows = image_cube.shape[1]
    details = []
    depth = 2 ** (SCALES + 1) - 2
    current = padded_2(image_cube, (("rows", 1),), depth)
    inside = inside_rows(depth, local_rows)
    margin = depth
    for level_idx in range(SCALES):
        dilation = 2**level_idx
        reach_rows = 2 * dilation
        new_margin = margin - reach_rows
        out_rows = local_rows + 2 * new_margin
        start_row = depth - new_margin
        smoothed = blur_cols(blur_rows(current, dilation, out_rows), dilation)
        smoothed = smoothed * inside[:, start_row : start_row + out_rows, :]
        kept = current[:, reach_rows : reach_rows + out_rows, :] - smoothed
        details.append(kept[:, new_margin : new_margin + local_rows, :])
        current = smoothed
        margin = new_margin
    return details


def synthesise(space_next):
    local_rows = space_next.shape[2]
    running = jnp.zeros_like(space_next[0])
    for level_idx in reversed(range(SCALES)):
        dilation = 2**level_idx
        operand = running - space_next[level_idx]
        padded = padded_2(operand, (("rows", 1),), 2 * dilation)
        running = (
            blur_cols(blur_rows(padded, dilation, local_rows), dilation) + space_next[level_idx]
        )
    return running


def dct_table(length, parity=None):
    half = length if parity is None else length // 2
    split = 64 if half % 64 == 0 else 1
    groups = half // split
    period = 4 * length
    if parity is None:
        coef_idx = jnp.arange(length, dtype=jnp.int32)
    else:
        coef_idx = 2 * jnp.arange(half, dtype=jnp.int32) + parity
    scale = math.pi / (2 * length)
    outer_phase = (coef_idx[:, None] * (2 * split * jnp.arange(groups, dtype=jnp.int32))[None, :]) % period
    inner_phase = (coef_idx[:, None] * (2 * jnp.arange(split, dtype=jnp.int32) + 1)[None, :]) % period
    outer_angle = outer_phase.astype(jnp.float32) * scale
    inner_angle = inner_phase.astype(jnp.float32) * scale
    weights = jnp.where(
        coef_idx == 0, math.sqrt(1.0 / length), math.sqrt(2.0 / length)
    ).astype(jnp.float32)[:, None, None]
    table = (
        jnp.cos(outer_angle)[:, :, None] * jnp.cos(inner_angle)[:, None, :]
        - jnp.sin(outer_angle)[:, :, None] * jnp.sin(inner_angle)[:, None, :]
    ) * weights
    return table.reshape(coef_idx.shape[0], half)


def forward_dot(samples, table):
    return lax.dot_general(
        samples,
        table,
        (((0,), (1,)), ((), ())),
        precision=lax.Precision.HIGH,
        preferred_element_type=jnp.float32,
    )


def spectral(pixel_cube, freq_duals):
    chans_all, pixel_count = pixel_cube.shape
    if chans_all % 2:
        table = dct_table(chans_all)
        coeffs = forward_dot(pixel_cube, table)
        freq_next = jnp.clip(freq_duals + SIGMA * coeffs, -FREQ_BOUND, FREQ_BOUND)
        return (table,), freq_next, (freq_next,)
    half = chans_all // 2
    head = pixel_cube[:half]
    tail = pixel_cube[half:][::-1]
    tables = (dct_table(chans_all, 0), dct_table(chans_all, 1))
    pairs = freq_duals.reshape(pixel_count, half, 2)
    fresh = tuple(
        jnp.clip(pairs[:, :, parity] + SIGMA * forward_dot(samples, tables[parity]), -FREQ_BOUND, FREQ_BOUND)
        for parity, samples in ((0, head + tail), (1, head - tail))
    )
    freq_next = jnp.stack(fresh, axis=2).reshape(pixel_count, chans_all)
    return tables, freq_next, fresh


def spectral_back(tables, fresh):
    parts = [
        lax.dot_general(
            table,
            values,
            (((0,), (1,)), ((), ())),
            precision=lax.Precision.HIGH,
            preferred_element_type=jnp.float32,
        )
        for table, values in zip(tables, fresh)
    ]
    if len(parts) == 1:
        return parts[0]
    return jnp.concatenate([parts[0] + parts[1], (parts[0] - parts[1])[::-1]], axis=0)


def starlet_kernel(flags_ref, above_ref, own_ref, below_ref, duals_ref, *refs):
    sn_ref, send_ref, mid_ref, keep_ref, buf_a, buf_b = refs[-6:]
    block, local_rows, columns = own_ref.shape
    halo = 2 ** (SCALES + 1) - 2
    extent = 2 * halo + local_rows
    pad = 2 ** SCALES
    row0 = flags_ref[0] - halo
    total_rows = flags_ref[1]
    lane = lax.broadcasted_iota(jnp.int32, (1, block, columns), 2)
    weights = {}
    for level_idx in range(SCALES):
        dilation = 2**level_idx
        weights[dilation] = tuple(
            jnp.where(keep, tap, 0.0).astype(jnp.float32)
            for step, tap in ((dilation, TAPS[1]), (2 * dilation, TAPS[0]))
            for keep in (lane >= step, lane < columns - step)
        )

    def smooth_rows(src, dst, dilation, lo, hi):
        near_w, far_w = weights[dilation][0:2], weights[dilation][2:4]
        for start in range(lo, hi, CHUNK):
            size = min(CHUNK, hi - start)
            at = start + pad

            def compute(at=at, size=size, start=start, masked=True):
                def window(offset):
                    return src[pl.ds(at + offset, size)]

                y = TAPS[0] * (window(-2 * dilation) + window(2 * dilation)) + TAPS[1] * (
                    window(-dilation) + window(dilation)
                ) + TAPS[2] * window(0)
                z = (
                    pltpu.roll(y, dilation, 2) * near_w[0]
                    + pltpu.roll(y, columns - dilation, 2) * near_w[1]
                    + pltpu.roll(y, 2 * dilation, 2) * far_w[0]
                    + pltpu.roll(y, columns - 2 * dilation, 2) * far_w[1]
                    + TAPS[2] * y
                )
                if masked:
                    row = row0 + start + lax.broadcasted_iota(jnp.int32, (size, 1, 1), 0)
                    z = jnp.where((row >= 0) & (row < total_rows), z, 0.0)
                dst[pl.ds(at, size)] = z

            if start >= halo and start + size <= halo + local_rows:
                compute(masked=False)
            else:
                outside = (row0 + start + size <= 0) | (row0 + start >= total_rows)

                @pl.when(outside)
                def _(at=at, size=size):
                    dst[pl.ds(at, size)] = jnp.zeros((size, block, columns), jnp.float32)

                pl.when(jnp.logical_not(outside))(compute)

    def rows_major(value):
        return jnp.swapaxes(value, 0, 1)

    buf_a[...] = jnp.zeros_like(buf_a)
    above = rows_major(above_ref[...])[local_rows - halo :]
    below = rows_major(below_ref[...])[:halo]
    buf_a[pl.ds(pad, halo)] = jnp.where(flags_ref[2] > 0, above, 0.0)
    buf_a[pl.ds(pad + halo, local_rows)] = rows_major(own_ref[...])
    buf_a[pl.ds(pad + halo + local_rows, halo)] = jnp.where(flags_ref[3] > 0, below, 0.0)
    bufs = (buf_a, buf_b)
    own = pl.ds(pad + halo, local_rows)
    fresh = []
    lo, hi = 0, extent
    for level_idx in range(SCALES):
        dilation = 2**level_idx
        src, dst = bufs[level_idx % 2], bufs[(level_idx + 1) % 2]
        lo, hi = lo + 2 * dilation, hi - 2 * dilation
        smooth_rows(src, dst, dilation, lo, hi)
        plane = jnp.clip(
            duals_ref[level_idx] + SIGMA * rows_major(src[own] - dst[own]), -SPACE_BOUND, SPACE_BOUND
        )
        sn_ref[level_idx] = plane

    buf_a[...] = jnp.zeros_like(buf_a)
    buf_b[...] = jnp.zeros_like(buf_b)
    lo, hi = halo, halo + local_rows
    for count, level_idx in enumerate(reversed(range(SCALES))):
        dilation = 2**level_idx
        src, dst = bufs[count % 2], bufs[(count + 1) % 2]
        plane = rows_major(sn_ref[level_idx])
        src[own] = src[own] - plane
        lo, hi = lo - 2 * dilation, hi + 2 * dilation
        smooth_rows(src, dst, dilation, max(lo, 0), min(hi, extent))
        dst[own] = dst[own] + plane
    top = dst[pl.ds(pad + halo - local_rows, local_rows)]
    bot = dst[pl.ds(pad + halo + local_rows, local_rows)]
    swap = flags_ref[4] > 0
    send_ref[...] = rows_major(jnp.where(swap, bot, top))
    keep_ref[...] = rows_major(jnp.where(swap, top, bot))
    mid_ref[...] = rows_major(dst[own])


def starlet(flags, above, own, below, duals, halo, group, groups, carry=(), near_base=0, interpret=False):
    chans, local_rows, columns = own.shape
    block = math.gcd(chans, 8)
    steps = chans // block // groups
    base = group * steps
    extent = 2 * halo + local_rows + 2 * 2**SCALES
    near_spec = pl.BlockSpec((block, local_rows, columns), lambda i: (i + near_base, 0, 0))
    edge_spec = pl.BlockSpec((block, local_rows, columns), lambda i: (i, 0, 0))
    own_spec = pl.BlockSpec((block, local_rows, columns), lambda i: (i + base, 0, 0))
    dual_spec = pl.BlockSpec((SCALES, block, local_rows, columns), lambda i: (0, i + base, 0, 0))
    assert local_rows - halo <= 2**SCALES <= halo
    edge_shape = jax.ShapeDtypeStruct((chans // groups, local_rows, columns), jnp.float32)
    carry_specs = [pl.BlockSpec(memory_space=pl.ANY)] * len(carry)
    return pl.pallas_call(
        starlet_kernel,
        grid=(steps,),
        in_specs=[pl.BlockSpec(memory_space=pltpu.SMEM), near_spec, own_spec, near_spec, dual_spec] + carry_specs,
        out_specs=[dual_spec, edge_spec, own_spec, edge_spec],
        out_shape=[
            jax.ShapeDtypeStruct(duals.shape, jnp.float32),
            edge_shape,
            jax.ShapeDtypeStruct(own.shape, jnp.float32),
            edge_shape,
        ],
        scratch_shapes=[pltpu.VMEM((extent, block, columns), jnp.float32)] * 2,
        input_output_aliases={5: 0, 6: 2} if carry else {},
        interpret=interpret,
    )(flags, above, own, below, duals, *carry)


def row_plan(chans, local_rows):
    halo = 2 ** (SCALES + 1) - 2
    assert local_rows >= halo
    block = math.gcd(chans, 8)
    groups = math.gcd(chans // block, GROUPS)
    return halo, groups, chans // groups


def exchange_halos(image_cube, early):
    chans, local_rows, columns = image_cube.shape
    halo, groups, width = row_plan(chans, local_rows)
    count = lax.axis_size("rows")
    down = [(i, i + 1) for i in range(count - 1)]
    up = [(i + 1, i) for i in range(count - 1)]
    cuts = [(0, early), (early, groups)] if 0 < early < groups else [(0, groups)]
    halos = []
    previous = None
    for first, last in cuts:
        part = image_cube[first * width : last * width]
        if previous is not None:
            part, previous = lax.optimization_barrier((part, previous))
        if count == 2:
            got = lax.ppermute(part, "rows", down + up)
            pair = (got, got)
        else:
            pair = (lax.ppermute(part, "rows", down), lax.ppermute(part, "rows", up))
        previous = pair
        block = math.gcd(chans, 8)
        steps = width // block
        halos.extend((pair, (group - first) * steps) for group in range(first, last))
    return halos


class Spatial:
    def __init__(self, image_cube, space_duals):
        self.image_cube = image_cube
        self.space_duals = space_duals
        chans, local_rows, columns = image_cube.shape
        self.halo, self.groups, self.width = row_plan(chans, local_rows)
        count = lax.axis_size("rows")
        self.index = lax.axis_index("rows")
        self.down = [(i, i + 1) for i in range(count - 1)]
        self.up = [(i + 1, i) for i in range(count - 1)]
        self.paired = count == 2
        index = self.index
        self.flags = jnp.stack(
            [index * local_rows, count * local_rows, index > 0, index < count - 1, self.paired & (index == 0)]
        ).astype(jnp.int32)
        self.sends, self.keeps = [], []

    def run(self, group, halos, carry):
        (above, below), near_base = halos[group]
        space_next, send, mid, keep = starlet(
            self.flags, above, self.image_cube, below, self.space_duals, self.halo, group, self.groups, carry,
            near_base,
        )
        if self.paired:
            self.sends.append(lax.ppermute(send, "rows", self.down + self.up))
        else:
            self.sends.append(lax.ppermute(send, "rows", self.up))
            self.keeps.append(lax.ppermute(keep, "rows", self.down))
        return (space_next, mid)

    def finish(self, carry):
        space_next, mid = carry
        space_term = mid + jnp.concatenate(self.sends, axis=0)
        if not self.paired:
            space_term = space_term + jnp.concatenate(self.keeps, axis=0)
        return space_term, space_next


def local(image_cube, data_grad, space_duals, freq_duals):
    chans, local_rows, columns = image_cube.shape
    peers = lax.axis_size("freq")
    share = local_rows * columns // peers
    pieces = image_cube.reshape(chans, peers, share)
    work = Spatial(image_cube, space_duals)
    early = work.groups // 2
    halos = exchange_halos(image_cube, early)
    pixel_cube = lax.all_to_all(pieces, "freq", split_axis=1, concat_axis=0, tiled=True).reshape(
        chans * peers, share
    )
    carry = ()
    for group in range(early):
        carry = work.run(group, halos, carry)
    later = [pair for pair, _ in halos[early:]]
    pixel_cube, carry, later = lax.optimization_barrier((pixel_cube, carry, later))
    halos = halos[:early] + [(pair, base) for pair, (_, base) in zip(later, halos[early:])]
    tables, freq_next, fresh = spectral(pixel_cube, freq_duals)
    spectral_sum = spectral_back(tables, fresh)
    spectral_sum, carry, work.sends, work.keeps = lax.optimization_barrier(
        (spectral_sum, carry, work.sends, work.keeps)
    )
    returned = lax.all_to_all(
        spectral_sum.reshape(peers, chans, share),
        "freq",
        split_axis=0,
        concat_axis=2,
        tiled=True,
    )
    for group in range(early, work.groups):
        carry = work.run(group, halos, carry)
    space_term, space_next = work.finish(carry)
    spectral_term = returned.reshape(chans, local_rows, columns)
    image_next = jnp.maximum(image_cube - TAU_STEP * (data_grad + space_term + spectral_term), 0.0)
    return (image_next, space_next, freq_next)


def solution(mesh):
    in_specs = (
        P("freq", "rows", None),
        P("freq", "rows", None),
        P(None, "freq", "rows", None),
        P(("rows", "freq"), None),
    )
    out_specs = (P("freq", "rows", None), P(None, "freq", "rows", None), P(("rows", "freq"), None))
    return jax.shard_map(local, mesh=mesh, in_specs=in_specs, out_specs=out_specs, check_vma=False)
```

```python
import math

import jax
import jax.numpy as jnp
from jax import lax
from jax.sharding import PartitionSpec as P
from jax.experimental import pallas as pl
from jax.experimental.pallas import tpu as pltpu

SCALES = 4


TAPS = (0.0625, 0.25, 0.375, 0.25, 0.0625)
SIGMA = 0.5
TAU_STEP = 0.5
SPACE_BOUND = 0.5
FREQ_BOUND = 1.0
CHUNK = 8
GROUPS = 4


def padded_2(cells, sides, width):
    for axis, dim in sides:
        count = lax.axis_size(axis)
        ends = count - 1
        head = lax.slice_in_dim(cells, 0, width, axis=dim)
        tail = lax.slice_in_dim(cells, cells.shape[dim] - width, cells.shape[dim], axis=dim)
        cells = jnp.concatenate(
            [
                lax.ppermute(tail, axis, [(i, (i + 1) % count) for i in range(ends)]),
                cells,
                lax.ppermute(head, axis, [((i + 1) % count, i) for i in range(ends)]),
            ],
            axis=dim,
        )
    return cells


def blur_rows(padded, dilation, out_rows):
    running = TAPS[0] * padded[:, 0:out_rows, :]
    for tap_idx in range(1, 5):
        offset = tap_idx * dilation
        running = running + TAPS[tap_idx] * padded[:, offset : offset + out_rows, :]
    return running


def blur_cols(planar, dilation):
    columns = planar.shape[2]
    reach_cols = 2 * dilation
    padded = jnp.pad(planar, ((0, 0), (0, 0), (reach_cols, reach_cols)))
    running = TAPS[0] * padded[:, :, 0:columns]
    for tap_idx in range(1, 5):
        offset = tap_idx * dilation
        running = running + TAPS[tap_idx] * padded[:, :, offset : offset + columns]
    return running


def inside_rows(margin, local_rows):
    first_row = lax.axis_index("rows") * local_rows - margin
    positions = first_row + jnp.arange(local_rows + 2 * margin, dtype=jnp.int32)
    limit = local_rows * lax.axis_size("rows")
    return ((positions >= 0) & (positions < limit)).astype(jnp.float32)[None, :, None]


def analyse(image_cube):
    local_rows = image_cube.shape[1]
    details = []
    depth = 2 ** (SCALES + 1) - 2
    current = padded_2(image_cube, (("rows", 1),), depth)
    inside = inside_rows(depth, local_rows)
    margin = depth
    for level_idx in range(SCALES):
        dilation = 2**level_idx
        reach_rows = 2 * dilation
        new_margin = margin - reach_rows
        out_rows = local_rows + 2 * new_margin
        start_row = depth - new_margin
        smoothed = blur_cols(blur_rows(current, dilation, out_rows), dilation)
        smoothed = smoothed * inside[:, start_row : start_row + out_rows, :]
        kept = current[:, reach_rows : reach_rows + out_rows, :] - smoothed
        details.append(kept[:, new_margin : new_margin + local_rows, :])
        current = smoothed
        margin = new_margin
    return details


def synthesise(space_next):
    local_rows = space_next.shape[2]
    running = jnp.zeros_like(space_next[0])
    for level_idx in reversed(range(SCALES)):
        dilation = 2**level_idx
        operand = running - space_next[level_idx]
        padded = padded_2(operand, (("rows", 1),), 2 * dilation)
        running = (
            blur_cols(blur_rows(padded, dilation, local_rows), dilation) + space_next[level_idx]
        )
    return running


def dct_table(length, parity=None):
    half = length if parity is None else length // 2
    split = 64 if half % 64 == 0 else 1
    groups = half // split
    period = 4 * length
    if parity is None:
        coef_idx = jnp.arange(length, dtype=jnp.int32)
    else:
        coef_idx = 2 * jnp.arange(half, dtype=jnp.int32) + parity
    scale = math.pi / (2 * length)
    outer_phase = (coef_idx[:, None] * (2 * split * jnp.arange(groups, dtype=jnp.int32))[None, :]) % period
    inner_phase = (coef_idx[:, None] * (2 * jnp.arange(split, dtype=jnp.int32) + 1)[None, :]) % period
    outer_angle = outer_phase.astype(jnp.float32) * scale
    inner_angle = inner_phase.astype(jnp.float32) * scale
    weights = jnp.where(
        coef_idx == 0, math.sqrt(1.0 / length), math.sqrt(2.0 / length)
    ).astype(jnp.float32)[:, None, None]
    table = (
        jnp.cos(outer_angle)[:, :, None] * jnp.cos(inner_angle)[:, None, :]
        - jnp.sin(outer_angle)[:, :, None] * jnp.sin(inner_angle)[:, None, :]
    ) * weights
    return table.reshape(coef_idx.shape[0], half)


def forward_dot(samples, table):
    return lax.dot_general(
        samples,
        table,
        (((0,), (1,)), ((), ())),
        precision=lax.Precision.HIGH,
        preferred_element_type=jnp.float32,
    )


def spectral(pixel_cube, freq_duals):
    chans_all, pixel_count = pixel_cube.shape
    if chans_all % 2:
        table = dct_table(chans_all)
        coeffs = forward_dot(pixel_cube, table)
        freq_next = jnp.clip(freq_duals + SIGMA * coeffs, -FREQ_BOUND, FREQ_BOUND)
        return (table,), freq_next, (freq_next,)
    half = chans_all // 2
    head = pixel_cube[:half]
    tail = pixel_cube[half:][::-1]
    tables = (dct_table(chans_all, 0), dct_table(chans_all, 1))
    pairs = freq_duals.reshape(pixel_count, half, 2)
    fresh = tuple(
        jnp.clip(pairs[:, :, parity] + SIGMA * forward_dot(samples, tables[parity]), -FREQ_BOUND, FREQ_BOUND)
        for parity, samples in ((0, head + tail), (1, head - tail))
    )
    freq_next = jnp.stack(fresh, axis=2).reshape(pixel_count, chans_all)
    return tables, freq_next, fresh


def spectral_back(tables, fresh):
    parts = [
        lax.dot_general(
            table,
            values,
            (((0,), (1,)), ((), ())),
            precision=lax.Precision.HIGH,
            preferred_element_type=jnp.float32,
        )
        for table, values in zip(tables, fresh)
    ]
    if len(parts) == 1:
        return parts[0]
    return jnp.concatenate([parts[0] + parts[1], (parts[0] - parts[1])[::-1]], axis=0)


def starlet_kernel(flags_ref, above_ref, own_ref, below_ref, duals_ref, *refs):
    sn_ref, send_ref, mid_ref, keep_ref, buf_a, buf_b = refs[-6:]
    block, local_rows, columns = own_ref.shape
    halo = 2 ** (SCALES + 1) - 2
    extent = 2 * halo + local_rows
    pad = 2 ** SCALES
    row0 = flags_ref[0] - halo
    total_rows = flags_ref[1]
    lane = lax.broadcasted_iota(jnp.int32, (1, block, columns), 2)
    weights = {}
    for level_idx in range(SCALES):
        dilation = 2**level_idx
        weights[dilation] = tuple(
            jnp.where(keep, tap, 0.0).astype(jnp.float32)
            for step, tap in ((dilation, TAPS[1]), (2 * dilation, TAPS[0]))
            for keep in (lane >= step, lane < columns - step)
        )

    def smooth_rows(src, dst, dilation, lo, hi):
        near_w, far_w = weights[dilation][0:2], weights[dilation][2:4]
        for start in range(lo, hi, CHUNK):
            size = min(CHUNK, hi - start)
            at = start + pad

            def window(offset):
                return src[pl.ds(at + offset, size)]

            y = TAPS[0] * (window(-2 * dilation) + window(2 * dilation)) + TAPS[1] * (
                window(-dilation) + window(dilation)
            ) + TAPS[2] * window(0)
            z = (
                pltpu.roll(y, dilation, 2) * near_w[0]
                + pltpu.roll(y, columns - dilation, 2) * near_w[1]
                + pltpu.roll(y, 2 * dilation, 2) * far_w[0]
                + pltpu.roll(y, columns - 2 * dilation, 2) * far_w[1]
                + TAPS[2] * y
            )
            if start >= halo and start + size <= halo + local_rows:
                dst[pl.ds(at, size)] = z
            else:
                row = row0 + start + lax.broadcasted_iota(jnp.int32, (size, 1, 1), 0)
                dst[pl.ds(at, size)] = jnp.where((row >= 0) & (row < total_rows), z, 0.0)

    def rows_major(value):
        return jnp.swapaxes(value, 0, 1)

    buf_a[...] = jnp.zeros_like(buf_a)
    above = rows_major(above_ref[...])[local_rows - halo :]
    below = rows_major(below_ref[...])[:halo]
    buf_a[pl.ds(pad, halo)] = jnp.where(flags_ref[2] > 0, above, 0.0)
    buf_a[pl.ds(pad + halo, local_rows)] = rows_major(own_ref[...])
    buf_a[pl.ds(pad + halo + local_rows, halo)] = jnp.where(flags_ref[3] > 0, below, 0.0)
    bufs = (buf_a, buf_b)
    own = pl.ds(pad + halo, local_rows)
    fresh = []
    lo, hi = 0, extent
    for level_idx in range(SCALES):
        dilation = 2**level_idx
        src, dst = bufs[level_idx % 2], bufs[(level_idx + 1) % 2]
        lo, hi = lo + 2 * dilation, hi - 2 * dilation
        smooth_rows(src, dst, dilation, lo, hi)
        plane = jnp.clip(
            duals_ref[level_idx] + SIGMA * rows_major(src[own] - dst[own]), -SPACE_BOUND, SPACE_BOUND
        )
        sn_ref[level_idx] = plane

    buf_a[...] = jnp.zeros_like(buf_a)
    buf_b[...] = jnp.zeros_like(buf_b)
    lo, hi = halo, halo + local_rows
    for count, level_idx in enumerate(reversed(range(SCALES))):
        dilation = 2**level_idx
        src, dst = bufs[count % 2], bufs[(count + 1) % 2]
        plane = rows_major(sn_ref[level_idx])
        src[own] = src[own] - plane
        lo, hi = lo - 2 * dilation, hi + 2 * dilation
        smooth_rows(src, dst, dilation, max(lo, 0), min(hi, extent))
        dst[own] = dst[own] + plane
    top = dst[pl.ds(pad + halo - local_rows, local_rows)]
    bot = dst[pl.ds(pad + halo + local_rows, local_rows)]
    swap = flags_ref[4] > 0
    send_ref[...] = rows_major(jnp.where(swap, bot, top))
    keep_ref[...] = rows_major(jnp.where(swap, top, bot))
    mid_ref[...] = rows_major(dst[own])


def starlet(flags, above, own, below, duals, halo, group, groups, carry=(), near_base=0, interpret=False):
    chans, local_rows, columns = own.shape
    block = math.gcd(chans, 8)
    steps = chans // block // groups
    base = group * steps
    extent = 2 * halo + local_rows + 2 * 2**SCALES
    near_spec = pl.BlockSpec((block, local_rows, columns), lambda i: (i + near_base, 0, 0))
    edge_spec = pl.BlockSpec((block, local_rows, columns), lambda i: (i, 0, 0))
    own_spec = pl.BlockSpec((block, local_rows, columns), lambda i: (i + base, 0, 0))
    dual_spec = pl.BlockSpec((SCALES, block, local_rows, columns), lambda i: (0, i + base, 0, 0))
    assert local_rows - halo <= 2**SCALES <= halo
    edge_shape = jax.ShapeDtypeStruct((chans // groups, local_rows, columns), jnp.float32)
    carry_specs = [pl.BlockSpec(memory_space=pl.ANY)] * len(carry)
    return pl.pallas_call(
        starlet_kernel,
        grid=(steps,),
        in_specs=[pl.BlockSpec(memory_space=pltpu.SMEM), near_spec, own_spec, near_spec, dual_spec] + carry_specs,
        out_specs=[dual_spec, edge_spec, own_spec, edge_spec],
        out_shape=[
            jax.ShapeDtypeStruct(duals.shape, jnp.float32),
            edge_shape,
            jax.ShapeDtypeStruct(own.shape, jnp.float32),
            edge_shape,
        ],
        scratch_shapes=[pltpu.VMEM((extent, block, columns), jnp.float32)] * 2,
        input_output_aliases={5: 0, 6: 2} if carry else {},
        interpret=interpret,
    )(flags, above, own, below, duals, *carry)


def row_plan(chans, local_rows):
    halo = 2 ** (SCALES + 1) - 2
    assert local_rows >= halo
    block = math.gcd(chans, 8)
    groups = math.gcd(chans // block, GROUPS)
    return halo, groups, chans // groups


def exchange_halos(image_cube, early):
    chans, local_rows, columns = image_cube.shape
    halo, groups, width = row_plan(chans, local_rows)
    count = lax.axis_size("rows")
    down = [(i, i + 1) for i in range(count - 1)]
    up = [(i + 1, i) for i in range(count - 1)]
    cuts = [(0, early), (early, groups)] if 0 < early < groups else [(0, groups)]
    halos = []
    previous = None
    for first, last in cuts:
        part = image_cube[first * width : last * width]
        if previous is not None:
            part, previous = lax.optimization_barrier((part, previous))
        if count == 2:
            got = lax.ppermute(part, "rows", down + up)
            pair = (got, got)
        else:
            pair = (lax.ppermute(part, "rows", down), lax.ppermute(part, "rows", up))
        previous = pair
        block = math.gcd(chans, 8)
        steps = width // block
        halos.extend((pair, (group - first) * steps) for group in range(first, last))
    return halos


class Spatial:
    def __init__(self, image_cube, space_duals):
        self.image_cube = image_cube
        self.space_duals = space_duals
        chans, local_rows, columns = image_cube.shape
        self.halo, self.groups, self.width = row_plan(chans, local_rows)
        count = lax.axis_size("rows")
        self.index = lax.axis_index("rows")
        self.down = [(i, i + 1) for i in range(count - 1)]
        self.up = [(i + 1, i) for i in range(count - 1)]
        self.paired = count == 2
        index = self.index
        self.flags = jnp.stack(
            [index * local_rows, count * local_rows, index > 0, index < count - 1, self.paired & (index == 0)]
        ).astype(jnp.int32)
        self.sends, self.keeps = [], []

    def run(self, group, halos, carry):
        (above, below), near_base = halos[group]
        space_next, send, mid, keep = starlet(
            self.flags, above, self.image_cube, below, self.space_duals, self.halo, group, self.groups, carry,
            near_base,
        )
        if self.paired:
            self.sends.append(lax.ppermute(send, "rows", self.down + self.up))
        else:
            self.sends.append(lax.ppermute(send, "rows", self.up))
            self.keeps.append(lax.ppermute(keep, "rows", self.down))
        return (space_next, mid)

    def finish(self, carry):
        space_next, mid = carry
        space_term = mid + jnp.concatenate(self.sends, axis=0)
        if not self.paired:
            space_term = space_term + jnp.concatenate(self.keeps, axis=0)
        return space_term, space_next


def local(image_cube, data_grad, space_duals, freq_duals):
    chans, local_rows, columns = image_cube.shape
    peers = lax.axis_size("freq")
    share = local_rows * columns // peers
    pieces = image_cube.reshape(chans, peers, share)
    work = Spatial(image_cube, space_duals)
    early = max(1, work.groups // 4)
    halos = exchange_halos(image_cube, early)
    pixel_cube = lax.all_to_all(pieces, "freq", split_axis=1, concat_axis=0, tiled=True).reshape(
        chans * peers, share
    )
    carry = ()
    for group in range(early):
        carry = work.run(group, halos, carry)
    later = [pair for pair, _ in halos[early:]]
    pixel_cube, carry, later = lax.optimization_barrier((pixel_cube, carry, later))
    halos = halos[:early] + [(pair, base) for pair, (_, base) in zip(later, halos[early:])]
    tables, freq_next, fresh = spectral(pixel_cube, freq_duals)
    spectral_sum = spectral_back(tables, fresh)
    spectral_sum, carry, work.sends, work.keeps = lax.optimization_barrier(
        (spectral_sum, carry, work.sends, work.keeps)
    )
    returned = lax.all_to_all(
        spectral_sum.reshape(peers, chans, share),
        "freq",
        split_axis=0,
        concat_axis=2,
        tiled=True,
    )
    for group in range(early, work.groups):
        carry = work.run(group, halos, carry)
    space_term, space_next = work.finish(carry)
    spectral_term = returned.reshape(chans, local_rows, columns)
    image_next = jnp.maximum(image_cube - TAU_STEP * (data_grad + space_term + spectral_term), 0.0)
    return (image_next, space_next, freq_next)


def solution(mesh):
    in_specs = (
        P("freq", "rows", None),
        P("freq", "rows", None),
        P(None, "freq", "rows", None),
        P(("rows", "freq"), None),
    )
    out_specs = (P("freq", "rows", None), P(None, "freq", "rows", None), P(("rows", "freq"), None))
    return jax.shard_map(local, mesh=mesh, in_specs=in_specs, out_specs=out_specs, check_vma=False)
```

```python
import math

import jax
import jax.numpy as jnp
from jax import lax
from jax.sharding import PartitionSpec as P
from jax.experimental import pallas as pl
from jax.experimental.pallas import tpu as pltpu

SCALES = 4


TAPS = (0.0625, 0.25, 0.375, 0.25, 0.0625)
SIGMA = 0.5
TAU_STEP = 0.5
SPACE_BOUND = 0.5
FREQ_BOUND = 1.0
CHUNK = 8
GROUPS = 2


def padded_2(cells, sides, width):
    for axis, dim in sides:
        count = lax.axis_size(axis)
        ends = count - 1
        head = lax.slice_in_dim(cells, 0, width, axis=dim)
        tail = lax.slice_in_dim(cells, cells.shape[dim] - width, cells.shape[dim], axis=dim)
        cells = jnp.concatenate(
            [
                lax.ppermute(tail, axis, [(i, (i + 1) % count) for i in range(ends)]),
                cells,
                lax.ppermute(head, axis, [((i + 1) % count, i) for i in range(ends)]),
            ],
            axis=dim,
        )
    return cells


def blur_rows(padded, dilation, out_rows):
    running = TAPS[0] * padded[:, 0:out_rows, :]
    for tap_idx in range(1, 5):
        offset = tap_idx * dilation
        running = running + TAPS[tap_idx] * padded[:, offset : offset + out_rows, :]
    return running


def blur_cols(planar, dilation):
    columns = planar.shape[2]
    reach_cols = 2 * dilation
    padded = jnp.pad(planar, ((0, 0), (0, 0), (reach_cols, reach_cols)))
    running = TAPS[0] * padded[:, :, 0:columns]
    for tap_idx in range(1, 5):
        offset = tap_idx * dilation
        running = running + TAPS[tap_idx] * padded[:, :, offset : offset + columns]
    return running


def inside_rows(margin, local_rows):
    first_row = lax.axis_index("rows") * local_rows - margin
    positions = first_row + jnp.arange(local_rows + 2 * margin, dtype=jnp.int32)
    limit = local_rows * lax.axis_size("rows")
    return ((positions >= 0) & (positions < limit)).astype(jnp.float32)[None, :, None]


def analyse(image_cube):
    local_rows = image_cube.shape[1]
    details = []
    depth = 2 ** (SCALES + 1) - 2
    current = padded_2(image_cube, (("rows", 1),), depth)
    inside = inside_rows(depth, local_rows)
    margin = depth
    for level_idx in range(SCALES):
        dilation = 2**level_idx
        reach_rows = 2 * dilation
        new_margin = margin - reach_rows
        out_rows = local_rows + 2 * new_margin
        start_row = depth - new_margin
        smoothed = blur_cols(blur_rows(current, dilation, out_rows), dilation)
        smoothed = smoothed * inside[:, start_row : start_row + out_rows, :]
        kept = current[:, reach_rows : reach_rows + out_rows, :] - smoothed
        details.append(kept[:, new_margin : new_margin + local_rows, :])
        current = smoothed
        margin = new_margin
    return details


def synthesise(space_next):
    local_rows = space_next.shape[2]
    running = jnp.zeros_like(space_next[0])
    for level_idx in reversed(range(SCALES)):
        dilation = 2**level_idx
        operand = running - space_next[level_idx]
        padded = padded_2(operand, (("rows", 1),), 2 * dilation)
        running = (
            blur_cols(blur_rows(padded, dilation, local_rows), dilation) + space_next[level_idx]
        )
    return running


def dct_table(length, parity=None):
    half = length if parity is None else length // 2
    split = 64 if half % 64 == 0 else 1
    groups = half // split
    period = 4 * length
    if parity is None:
        coef_idx = jnp.arange(length, dtype=jnp.int32)
    else:
        coef_idx = 2 * jnp.arange(half, dtype=jnp.int32) + parity
    scale = math.pi / (2 * length)
    outer_phase = (coef_idx[:, None] * (2 * split * jnp.arange(groups, dtype=jnp.int32))[None, :]) % period
    inner_phase = (coef_idx[:, None] * (2 * jnp.arange(split, dtype=jnp.int32) + 1)[None, :]) % period
    outer_angle = outer_phase.astype(jnp.float32) * scale
    inner_angle = inner_phase.astype(jnp.float32) * scale
    weights = jnp.where(
        coef_idx == 0, math.sqrt(1.0 / length), math.sqrt(2.0 / length)
    ).astype(jnp.float32)[:, None, None]
    table = (
        jnp.cos(outer_angle)[:, :, None] * jnp.cos(inner_angle)[:, None, :]
        - jnp.sin(outer_angle)[:, :, None] * jnp.sin(inner_angle)[:, None, :]
    ) * weights
    return table.reshape(coef_idx.shape[0], half)


def forward_dot(samples, table):
    return lax.dot_general(
        samples,
        table,
        (((0,), (1,)), ((), ())),
        precision=lax.Precision.HIGH,
        preferred_element_type=jnp.float32,
    )


def spectral(pixel_cube, freq_duals):
    chans_all, pixel_count = pixel_cube.shape
    if chans_all % 2:
        table = dct_table(chans_all)
        coeffs = forward_dot(pixel_cube, table)
        freq_next = jnp.clip(freq_duals + SIGMA * coeffs, -FREQ_BOUND, FREQ_BOUND)
        return (table,), freq_next, (freq_next,)
    half = chans_all // 2
    head = pixel_cube[:half]
    tail = pixel_cube[half:][::-1]
    tables = (dct_table(chans_all, 0), dct_table(chans_all, 1))
    pairs = freq_duals.reshape(pixel_count, half, 2)
    fresh = tuple(
        jnp.clip(pairs[:, :, parity] + SIGMA * forward_dot(samples, tables[parity]), -FREQ_BOUND, FREQ_BOUND)
        for parity, samples in ((0, head + tail), (1, head - tail))
    )
    freq_next = jnp.stack(fresh, axis=2).reshape(pixel_count, chans_all)
    return tables, freq_next, fresh


def spectral_back(tables, fresh):
    parts = [
        lax.dot_general(
            table,
            values,
            (((0,), (1,)), ((), ())),
            precision=lax.Precision.HIGH,
            preferred_element_type=jnp.float32,
        )
        for table, values in zip(tables, fresh)
    ]
    if len(parts) == 1:
        return parts[0]
    return jnp.concatenate([parts[0] + parts[1], (parts[0] - parts[1])[::-1]], axis=0)


def starlet_kernel(flags_ref, above_ref, own_ref, below_ref, duals_ref, *refs):
    sn_ref, send_ref, mid_ref, keep_ref, buf_a, buf_b = refs[-6:]
    block, local_rows, columns = own_ref.shape
    halo = 2 ** (SCALES + 1) - 2
    extent = 2 * halo + local_rows
    pad = 2 ** SCALES
    row0 = flags_ref[0] - halo
    total_rows = flags_ref[1]
    lane = lax.broadcasted_iota(jnp.int32, (1, block, columns), 2)
    weights = {}
    for level_idx in range(SCALES):
        dilation = 2**level_idx
        weights[dilation] = tuple(
            jnp.where(keep, tap, 0.0).astype(jnp.float32)
            for step, tap in ((dilation, TAPS[1]), (2 * dilation, TAPS[0]))
            for keep in (lane >= step, lane < columns - step)
        )

    def smooth_rows(src, dst, dilation, lo, hi):
        near_w, far_w = weights[dilation][0:2], weights[dilation][2:4]
        for start in range(lo, hi, CHUNK):
            size = min(CHUNK, hi - start)
            at = start + pad

            def window(offset):
                return src[pl.ds(at + offset, size)]

            y = TAPS[0] * (window(-2 * dilation) + window(2 * dilation)) + TAPS[1] * (
                window(-dilation) + window(dilation)
            ) + TAPS[2] * window(0)
            z = (
                pltpu.roll(y, dilation, 2) * near_w[0]
                + pltpu.roll(y, columns - dilation, 2) * near_w[1]
                + pltpu.roll(y, 2 * dilation, 2) * far_w[0]
                + pltpu.roll(y, columns - 2 * dilation, 2) * far_w[1]
                + TAPS[2] * y
            )
            if start >= halo and start + size <= halo + local_rows:
                dst[pl.ds(at, size)] = z
            else:
                row = row0 + start + lax.broadcasted_iota(jnp.int32, (size, 1, 1), 0)
                dst[pl.ds(at, size)] = jnp.where((row >= 0) & (row < total_rows), z, 0.0)

    def rows_major(value):
        return jnp.swapaxes(value, 0, 1)

    buf_a[...] = jnp.zeros_like(buf_a)
    above = rows_major(above_ref[...])[local_rows - halo :]
    below = rows_major(below_ref[...])[:halo]
    buf_a[pl.ds(pad, halo)] = jnp.where(flags_ref[2] > 0, above, 0.0)
    buf_a[pl.ds(pad + halo, local_rows)] = rows_major(own_ref[...])
    buf_a[pl.ds(pad + halo + local_rows, halo)] = jnp.where(flags_ref[3] > 0, below, 0.0)
    bufs = (buf_a, buf_b)
    own = pl.ds(pad + halo, local_rows)
    fresh = []
    lo, hi = 0, extent
    for level_idx in range(SCALES):
        dilation = 2**level_idx
        src, dst = bufs[level_idx % 2], bufs[(level_idx + 1) % 2]
        lo, hi = lo + 2 * dilation, hi - 2 * dilation
        smooth_rows(src, dst, dilation, lo, hi)
        plane = jnp.clip(
            duals_ref[level_idx] + SIGMA * rows_major(src[own] - dst[own]), -SPACE_BOUND, SPACE_BOUND
        )
        sn_ref[level_idx] = plane

    buf_a[...] = jnp.zeros_like(buf_a)
    buf_b[...] = jnp.zeros_like(buf_b)
    lo, hi = halo, halo + local_rows
    for count, level_idx in enumerate(reversed(range(SCALES))):
        dilation = 2**level_idx
        src, dst = bufs[count % 2], bufs[(count + 1) % 2]
        plane = rows_major(sn_ref[level_idx])
        src[own] = src[own] - plane
        lo, hi = lo - 2 * dilation, hi + 2 * dilation
        smooth_rows(src, dst, dilation, max(lo, 0), min(hi, extent))
        dst[own] = dst[own] + plane
    top = dst[pl.ds(pad + halo - local_rows, local_rows)]
    bot = dst[pl.ds(pad + halo + local_rows, local_rows)]
    swap = flags_ref[4] > 0
    send_ref[...] = rows_major(jnp.where(swap, bot, top))
    keep_ref[...] = rows_major(jnp.where(swap, top, bot))
    mid_ref[...] = rows_major(dst[own])


def starlet(flags, above, own, below, duals, halo, group, groups, carry=(), near_base=0, interpret=False):
    chans, local_rows, columns = own.shape
    block = math.gcd(chans, 8)
    steps = chans // block // groups
    base = group * steps
    extent = 2 * halo + local_rows + 2 * 2**SCALES
    near_spec = pl.BlockSpec((block, local_rows, columns), lambda i: (i + near_base, 0, 0))
    edge_spec = pl.BlockSpec((block, local_rows, columns), lambda i: (i, 0, 0))
    own_spec = pl.BlockSpec((block, local_rows, columns), lambda i: (i + base, 0, 0))
    dual_spec = pl.BlockSpec((SCALES, block, local_rows, columns), lambda i: (0, i + base, 0, 0))
    assert local_rows - halo <= 2**SCALES <= halo
    edge_shape = jax.ShapeDtypeStruct((chans // groups, local_rows, columns), jnp.float32)
    carry_specs = [pl.BlockSpec(memory_space=pl.ANY)] * len(carry)
    return pl.pallas_call(
        starlet_kernel,
        grid=(steps,),
        in_specs=[pl.BlockSpec(memory_space=pltpu.SMEM), near_spec, own_spec, near_spec, dual_spec] + carry_specs,
        out_specs=[dual_spec, edge_spec, own_spec, edge_spec],
        out_shape=[
            jax.ShapeDtypeStruct(duals.shape, jnp.float32),
            edge_shape,
            jax.ShapeDtypeStruct(own.shape, jnp.float32),
            edge_shape,
        ],
        scratch_shapes=[pltpu.VMEM((extent, block, columns), jnp.float32)] * 2,
        input_output_aliases={5: 0, 6: 2} if carry else {},
        interpret=interpret,
    )(flags, above, own, below, duals, *carry)


def row_plan(chans, local_rows):
    halo = 2 ** (SCALES + 1) - 2
    assert local_rows >= halo
    block = math.gcd(chans, 8)
    groups = math.gcd(chans // block, GROUPS)
    return halo, groups, chans // groups


def exchange_halos(image_cube, early):
    chans, local_rows, columns = image_cube.shape
    halo, groups, width = row_plan(chans, local_rows)
    count = lax.axis_size("rows")
    down = [(i, i + 1) for i in range(count - 1)]
    up = [(i + 1, i) for i in range(count - 1)]
    cuts = [(0, early), (early, groups)] if 0 < early < groups else [(0, groups)]
    halos = []
    previous = None
    for first, last in cuts:
        part = image_cube[first * width : last * width]
        if previous is not None:
            part, previous = lax.optimization_barrier((part, previous))
        if count == 2:
            got = lax.ppermute(part, "rows", down + up)
            pair = (got, got)
        else:
            pair = (lax.ppermute(part, "rows", down), lax.ppermute(part, "rows", up))
        previous = pair
        block = math.gcd(chans, 8)
        steps = width // block
        halos.extend((pair, (group - first) * steps) for group in range(first, last))
    return halos


class Spatial:
    def __init__(self, image_cube, space_duals):
        self.image_cube = image_cube
        self.space_duals = space_duals
        chans, local_rows, columns = image_cube.shape
        self.halo, self.groups, self.width = row_plan(chans, local_rows)
        count = lax.axis_size("rows")
        self.index = lax.axis_index("rows")
        self.down = [(i, i + 1) for i in range(count - 1)]
        self.up = [(i + 1, i) for i in range(count - 1)]
        self.paired = count == 2
        index = self.index
        self.flags = jnp.stack(
            [index * local_rows, count * local_rows, index > 0, index < count - 1, self.paired & (index == 0)]
        ).astype(jnp.int32)
        self.sends, self.keeps = [], []

    def run(self, group, halos, carry):
        (above, below), near_base = halos[group]
        space_next, send, mid, keep = starlet(
            self.flags, above, self.image_cube, below, self.space_duals, self.halo, group, self.groups, carry,
            near_base,
        )
        if self.paired:
            self.sends.append(lax.ppermute(send, "rows", self.down + self.up))
        else:
            self.sends.append(lax.ppermute(send, "rows", self.up))
            self.keeps.append(lax.ppermute(keep, "rows", self.down))
        return (space_next, mid)

    def finish(self, carry):
        space_next, mid = carry
        space_term = mid + jnp.concatenate(self.sends, axis=0)
        if not self.paired:
            space_term = space_term + jnp.concatenate(self.keeps, axis=0)
        return space_term, space_next


def local(image_cube, data_grad, space_duals, freq_duals):
    chans, local_rows, columns = image_cube.shape
    peers = lax.axis_size("freq")
    share = local_rows * columns // peers
    pieces = image_cube.reshape(chans, peers, share)
    work = Spatial(image_cube, space_duals)
    early = work.groups // 2
    halos = exchange_halos(image_cube, early)
    pixel_cube = lax.all_to_all(pieces, "freq", split_axis=1, concat_axis=0, tiled=True).reshape(
        chans * peers, share
    )
    carry = ()
    for group in range(early):
        carry = work.run(group, halos, carry)
    later = [pair for pair, _ in halos[early:]]
    pixel_cube, carry, later = lax.optimization_barrier((pixel_cube, carry, later))
    halos = halos[:early] + [(pair, base) for pair, (_, base) in zip(later, halos[early:])]
    tables, freq_next, fresh = spectral(pixel_cube, freq_duals)
    spectral_sum = spectral_back(tables, fresh)
    spectral_sum, carry, work.sends, work.keeps = lax.optimization_barrier(
        (spectral_sum, carry, work.sends, work.keeps)
    )
    returned = lax.all_to_all(
        spectral_sum.reshape(peers, chans, share),
        "freq",
        split_axis=0,
        concat_axis=2,
        tiled=True,
    )
    for group in range(early, work.groups):
        carry = work.run(group, halos, carry)
    space_term, space_next = work.finish(carry)
    spectral_term = returned.reshape(chans, local_rows, columns)
    image_next = jnp.maximum(image_cube - TAU_STEP * (data_grad + space_term + spectral_term), 0.0)
    return (image_next, space_next, freq_next)


def solution(mesh):
    in_specs = (
        P("freq", "rows", None),
        P("freq", "rows", None),
        P(None, "freq", "rows", None),
        P(("rows", "freq"), None),
    )
    out_specs = (P("freq", "rows", None), P(None, "freq", "rows", None), P(("rows", "freq"), None))
    return jax.shard_map(local, mesh=mesh, in_specs=in_specs, out_specs=out_specs, check_vma=False)
```

```python
import math

import jax
import jax.numpy as jnp
from jax import lax
from jax.sharding import PartitionSpec as P
from jax.experimental import pallas as pl
from jax.experimental.pallas import tpu as pltpu

SCALES = 4


TAPS = (0.0625, 0.25, 0.375, 0.25, 0.0625)
SIGMA = 0.5
TAU_STEP = 0.5
SPACE_BOUND = 0.5
FREQ_BOUND = 1.0
CHUNK = 4
GROUPS = 2


def padded_2(cells, sides, width):
    for axis, dim in sides:
        count = lax.axis_size(axis)
        ends = count - 1
        head = lax.slice_in_dim(cells, 0, width, axis=dim)
        tail = lax.slice_in_dim(cells, cells.shape[dim] - width, cells.shape[dim], axis=dim)
        cells = jnp.concatenate(
            [
                lax.ppermute(tail, axis, [(i, (i + 1) % count) for i in range(ends)]),
                cells,
                lax.ppermute(head, axis, [((i + 1) % count, i) for i in range(ends)]),
            ],
            axis=dim,
        )
    return cells


def blur_rows(padded, dilation, out_rows):
    running = TAPS[0] * padded[:, 0:out_rows, :]
    for tap_idx in range(1, 5):
        offset = tap_idx * dilation
        running = running + TAPS[tap_idx] * padded[:, offset : offset + out_rows, :]
    return running


def blur_cols(planar, dilation):
    columns = planar.shape[2]
    reach_cols = 2 * dilation
    padded = jnp.pad(planar, ((0, 0), (0, 0), (reach_cols, reach_cols)))
    running = TAPS[0] * padded[:, :, 0:columns]
    for tap_idx in range(1, 5):
        offset = tap_idx * dilation
        running = running + TAPS[tap_idx] * padded[:, :, offset : offset + columns]
    return running


def inside_rows(margin, local_rows):
    first_row = lax.axis_index("rows") * local_rows - margin
    positions = first_row + jnp.arange(local_rows + 2 * margin, dtype=jnp.int32)
    limit = local_rows * lax.axis_size("rows")
    return ((positions >= 0) & (positions < limit)).astype(jnp.float32)[None, :, None]


def analyse(image_cube):
    local_rows = image_cube.shape[1]
    details = []
    depth = 2 ** (SCALES + 1) - 2
    current = padded_2(image_cube, (("rows", 1),), depth)
    inside = inside_rows(depth, local_rows)
    margin = depth
    for level_idx in range(SCALES):
        dilation = 2**level_idx
        reach_rows = 2 * dilation
        new_margin = margin - reach_rows
        out_rows = local_rows + 2 * new_margin
        start_row = depth - new_margin
        smoothed = blur_cols(blur_rows(current, dilation, out_rows), dilation)
        smoothed = smoothed * inside[:, start_row : start_row + out_rows, :]
        kept = current[:, reach_rows : reach_rows + out_rows, :] - smoothed
        details.append(kept[:, new_margin : new_margin + local_rows, :])
        current = smoothed
        margin = new_margin
    return details


def synthesise(space_next):
    local_rows = space_next.shape[2]
    running = jnp.zeros_like(space_next[0])
    for level_idx in reversed(range(SCALES)):
        dilation = 2**level_idx
        operand = running - space_next[level_idx]
        padded = padded_2(operand, (("rows", 1),), 2 * dilation)
        running = (
            blur_cols(blur_rows(padded, dilation, local_rows), dilation) + space_next[level_idx]
        )
    return running


def dct_table(length, parity=None):
    half = length if parity is None else length // 2
    split = 64 if half % 64 == 0 else 1
    groups = half // split
    period = 4 * length
    if parity is None:
        coef_idx = jnp.arange(length, dtype=jnp.int32)
    else:
        coef_idx = 2 * jnp.arange(half, dtype=jnp.int32) + parity
    scale = math.pi / (2 * length)
    outer_phase = (coef_idx[:, None] * (2 * split * jnp.arange(groups, dtype=jnp.int32))[None, :]) % period
    inner_phase = (coef_idx[:, None] * (2 * jnp.arange(split, dtype=jnp.int32) + 1)[None, :]) % period
    outer_angle = outer_phase.astype(jnp.float32) * scale
    inner_angle = inner_phase.astype(jnp.float32) * scale
    weights = jnp.where(
        coef_idx == 0, math.sqrt(1.0 / length), math.sqrt(2.0 / length)
    ).astype(jnp.float32)[:, None, None]
    table = (
        jnp.cos(outer_angle)[:, :, None] * jnp.cos(inner_angle)[:, None, :]
        - jnp.sin(outer_angle)[:, :, None] * jnp.sin(inner_angle)[:, None, :]
    ) * weights
    return table.reshape(coef_idx.shape[0], half)


def forward_dot(samples, table):
    return lax.dot_general(
        samples,
        table,
        (((0,), (1,)), ((), ())),
        precision=lax.Precision.HIGH,
        preferred_element_type=jnp.float32,
    )


def spectral(pixel_cube, freq_duals):
    chans_all, pixel_count = pixel_cube.shape
    if chans_all % 2:
        table = dct_table(chans_all)
        coeffs = forward_dot(pixel_cube, table)
        freq_next = jnp.clip(freq_duals + SIGMA * coeffs, -FREQ_BOUND, FREQ_BOUND)
        return (table,), freq_next, (freq_next,)
    half = chans_all // 2
    head = pixel_cube[:half]
    tail = pixel_cube[half:][::-1]
    tables = (dct_table(chans_all, 0), dct_table(chans_all, 1))
    pairs = freq_duals.reshape(pixel_count, half, 2)
    fresh = tuple(
        jnp.clip(pairs[:, :, parity] + SIGMA * forward_dot(samples, tables[parity]), -FREQ_BOUND, FREQ_BOUND)
        for parity, samples in ((0, head + tail), (1, head - tail))
    )
    freq_next = jnp.stack(fresh, axis=2).reshape(pixel_count, chans_all)
    return tables, freq_next, fresh


def spectral_back(tables, fresh):
    parts = [
        lax.dot_general(
            table,
            values,
            (((0,), (1,)), ((), ())),
            precision=lax.Precision.HIGH,
            preferred_element_type=jnp.float32,
        )
        for table, values in zip(tables, fresh)
    ]
    if len(parts) == 1:
        return parts[0]
    return jnp.concatenate([parts[0] + parts[1], (parts[0] - parts[1])[::-1]], axis=0)


def starlet_kernel(flags_ref, above_ref, own_ref, below_ref, duals_ref, *refs):
    sn_ref, send_ref, mid_ref, keep_ref, buf_a, buf_b = refs[-6:]
    block, local_rows, columns = own_ref.shape
    halo = 2 ** (SCALES + 1) - 2
    extent = 2 * halo + local_rows
    pad = 2 ** SCALES
    row0 = flags_ref[0] - halo
    total_rows = flags_ref[1]
    lane = lax.broadcasted_iota(jnp.int32, (1, block, columns), 2)
    weights = {}
    for level_idx in range(SCALES):
        dilation = 2**level_idx
        weights[dilation] = tuple(
            jnp.where(keep, tap, 0.0).astype(jnp.float32)
            for step, tap in ((dilation, TAPS[1]), (2 * dilation, TAPS[0]))
            for keep in (lane >= step, lane < columns - step)
        )

    def smooth_rows(src, dst, dilation, lo, hi):
        near_w, far_w = weights[dilation][0:2], weights[dilation][2:4]
        for start in range(lo, hi, CHUNK):
            size = min(CHUNK, hi - start)
            at = start + pad

            def window(offset):
                return src[pl.ds(at + offset, size)]

            y = TAPS[0] * (window(-2 * dilation) + window(2 * dilation)) + TAPS[1] * (
                window(-dilation) + window(dilation)
            ) + TAPS[2] * window(0)
            z = (
                pltpu.roll(y, dilation, 2) * near_w[0]
                + pltpu.roll(y, columns - dilation, 2) * near_w[1]
                + pltpu.roll(y, 2 * dilation, 2) * far_w[0]
                + pltpu.roll(y, columns - 2 * dilation, 2) * far_w[1]
                + TAPS[2] * y
            )
            if start >= halo and start + size <= halo + local_rows:
                dst[pl.ds(at, size)] = z
            else:
                row = row0 + start + lax.broadcasted_iota(jnp.int32, (size, 1, 1), 0)
                dst[pl.ds(at, size)] = jnp.where((row >= 0) & (row < total_rows), z, 0.0)

    def rows_major(value):
        return jnp.swapaxes(value, 0, 1)

    buf_a[...] = jnp.zeros_like(buf_a)
    above = rows_major(above_ref[...])[local_rows - halo :]
    below = rows_major(below_ref[...])[:halo]
    buf_a[pl.ds(pad, halo)] = jnp.where(flags_ref[2] > 0, above, 0.0)
    buf_a[pl.ds(pad + halo, local_rows)] = rows_major(own_ref[...])
    buf_a[pl.ds(pad + halo + local_rows, halo)] = jnp.where(flags_ref[3] > 0, below, 0.0)
    bufs = (buf_a, buf_b)
    own = pl.ds(pad + halo, local_rows)
    fresh = []
    lo, hi = 0, extent
    for level_idx in range(SCALES):
        dilation = 2**level_idx
        src, dst = bufs[level_idx % 2], bufs[(level_idx + 1) % 2]
        lo, hi = lo + 2 * dilation, hi - 2 * dilation
        smooth_rows(src, dst, dilation, lo, hi)
        plane = jnp.clip(
            duals_ref[level_idx] + SIGMA * rows_major(src[own] - dst[own]), -SPACE_BOUND, SPACE_BOUND
        )
        sn_ref[level_idx] = plane

    buf_a[...] = jnp.zeros_like(buf_a)
    buf_b[...] = jnp.zeros_like(buf_b)
    lo, hi = halo, halo + local_rows
    for count, level_idx in enumerate(reversed(range(SCALES))):
        dilation = 2**level_idx
        src, dst = bufs[count % 2], bufs[(count + 1) % 2]
        plane = rows_major(sn_ref[level_idx])
        src[own] = src[own] - plane
        lo, hi = lo - 2 * dilation, hi + 2 * dilation
        smooth_rows(src, dst, dilation, max(lo, 0), min(hi, extent))
        dst[own] = dst[own] + plane
    top = dst[pl.ds(pad + halo - local_rows, local_rows)]
    bot = dst[pl.ds(pad + halo + local_rows, local_rows)]
    swap = flags_ref[4] > 0
    send_ref[...] = rows_major(jnp.where(swap, bot, top))
    keep_ref[...] = rows_major(jnp.where(swap, top, bot))
    mid_ref[...] = rows_major(dst[own])


def starlet(flags, above, own, below, duals, halo, group, groups, carry=(), near_base=0, interpret=False):
    chans, local_rows, columns = own.shape
    block = math.gcd(chans, 8)
    steps = chans // block // groups
    base = group * steps
    extent = 2 * halo + local_rows + 2 * 2**SCALES
    near_spec = pl.BlockSpec((block, local_rows, columns), lambda i: (i + near_base, 0, 0))
    edge_spec = pl.BlockSpec((block, local_rows, columns), lambda i: (i, 0, 0))
    own_spec = pl.BlockSpec((block, local_rows, columns), lambda i: (i + base, 0, 0))
    dual_spec = pl.BlockSpec((SCALES, block, local_rows, columns), lambda i: (0, i + base, 0, 0))
    assert local_rows - halo <= 2**SCALES <= halo
    edge_shape = jax.ShapeDtypeStruct((chans // groups, local_rows, columns), jnp.float32)
    carry_specs = [pl.BlockSpec(memory_space=pl.ANY)] * len(carry)
    return pl.pallas_call(
        starlet_kernel,
        grid=(steps,),
        in_specs=[pl.BlockSpec(memory_space=pltpu.SMEM), near_spec, own_spec, near_spec, dual_spec] + carry_specs,
        out_specs=[dual_spec, edge_spec, own_spec, edge_spec],
        out_shape=[
            jax.ShapeDtypeStruct(duals.shape, jnp.float32),
            edge_shape,
            jax.ShapeDtypeStruct(own.shape, jnp.float32),
            edge_shape,
        ],
        scratch_shapes=[pltpu.VMEM((extent, block, columns), jnp.float32)] * 2,
        input_output_aliases={5: 0, 6: 2} if carry else {},
        interpret=interpret,
    )(flags, above, own, below, duals, *carry)


def row_plan(chans, local_rows):
    halo = 2 ** (SCALES + 1) - 2
    assert local_rows >= halo
    block = math.gcd(chans, 8)
    groups = math.gcd(chans // block, GROUPS)
    return halo, groups, chans // groups


def exchange_halos(image_cube, early):
    chans, local_rows, columns = image_cube.shape
    halo, groups, width = row_plan(chans, local_rows)
    count = lax.axis_size("rows")
    down = [(i, i + 1) for i in range(count - 1)]
    up = [(i + 1, i) for i in range(count - 1)]
    cuts = [(0, early), (early, groups)] if 0 < early < groups else [(0, groups)]
    halos = []
    previous = None
    for first, last in cuts:
        part = image_cube[first * width : last * width]
        if previous is not None:
            part, previous = lax.optimization_barrier((part, previous))
        if count == 2:
            got = lax.ppermute(part, "rows", down + up)
            pair = (got, got)
        else:
            pair = (lax.ppermute(part, "rows", down), lax.ppermute(part, "rows", up))
        previous = pair
        block = math.gcd(chans, 8)
        steps = width // block
        halos.extend((pair, (group - first) * steps) for group in range(first, last))
    return halos


class Spatial:
    def __init__(self, image_cube, space_duals):
        self.image_cube = image_cube
        self.space_duals = space_duals
        chans, local_rows, columns = image_cube.shape
        self.halo, self.groups, self.width = row_plan(chans, local_rows)
        count = lax.axis_size("rows")
        self.index = lax.axis_index("rows")
        self.down = [(i, i + 1) for i in range(count - 1)]
        self.up = [(i + 1, i) for i in range(count - 1)]
        self.paired = count == 2
        index = self.index
        self.flags = jnp.stack(
            [index * local_rows, count * local_rows, index > 0, index < count - 1, self.paired & (index == 0)]
        ).astype(jnp.int32)
        self.sends, self.keeps = [], []

    def run(self, group, halos, carry):
        (above, below), near_base = halos[group]
        space_next, send, mid, keep = starlet(
            self.flags, above, self.image_cube, below, self.space_duals, self.halo, group, self.groups, carry,
            near_base,
        )
        if self.paired:
            self.sends.append(lax.ppermute(send, "rows", self.down + self.up))
        else:
            self.sends.append(lax.ppermute(send, "rows", self.up))
            self.keeps.append(lax.ppermute(keep, "rows", self.down))
        return (space_next, mid)

    def finish(self, carry):
        space_next, mid = carry
        space_term = mid + jnp.concatenate(self.sends, axis=0)
        if not self.paired:
            space_term = space_term + jnp.concatenate(self.keeps, axis=0)
        return space_term, space_next


def local(image_cube, data_grad, space_duals, freq_duals):
    chans, local_rows, columns = image_cube.shape
    peers = lax.axis_size("freq")
    share = local_rows * columns // peers
    pieces = image_cube.reshape(chans, peers, share)
    work = Spatial(image_cube, space_duals)
    early = work.groups // 2
    halos = exchange_halos(image_cube, early)
    pixel_cube = lax.all_to_all(pieces, "freq", split_axis=1, concat_axis=0, tiled=True).reshape(
        chans * peers, share
    )
    carry = ()
    for group in range(early):
        carry = work.run(group, halos, carry)
    later = [pair for pair, _ in halos[early:]]
    pixel_cube, carry, later = lax.optimization_barrier((pixel_cube, carry, later))
    halos = halos[:early] + [(pair, base) for pair, (_, base) in zip(later, halos[early:])]
    tables, freq_next, fresh = spectral(pixel_cube, freq_duals)
    spectral_sum = spectral_back(tables, fresh)
    spectral_sum, carry, work.sends, work.keeps = lax.optimization_barrier(
        (spectral_sum, carry, work.sends, work.keeps)
    )
    returned = lax.all_to_all(
        spectral_sum.reshape(peers, chans, share),
        "freq",
        split_axis=0,
        concat_axis=2,
        tiled=True,
    )
    for group in range(early, work.groups):
        carry = work.run(group, halos, carry)
    space_term, space_next = work.finish(carry)
    spectral_term = returned.reshape(chans, local_rows, columns)
    image_next = jnp.maximum(image_cube - TAU_STEP * (data_grad + space_term + spectral_term), 0.0)
    return (image_next, space_next, freq_next)


def solution(mesh):
    in_specs = (
        P("freq", "rows", None),
        P("freq", "rows", None),
        P(None, "freq", "rows", None),
        P(("rows", "freq"), None),
    )
    out_specs = (P("freq", "rows", None), P(None, "freq", "rows", None), P(("rows", "freq"), None))
    return jax.shard_map(local, mesh=mesh, in_specs=in_specs, out_specs=out_specs, check_vma=False)
```
